512 devices in a mesh: lon: 32 (over x_hi, z), lat: 16 (over x_lo, y, core).
Axes of the slice: x: 4 (x_hi: 2, x_lo: 2; x = x_hi * 2 + x_lo), y: 4, z: 16, core: 2. Of those that a mesh axis runs over, the one named last changes fastest.
Arguments:
- surface: float32 [1792, 4096], P('lat', 'lon'), may hold values from -0.25 to 0.25
- momentum_x: float32 [1792, 4096], P('lat', 'lon'), may hold values from -1.2 to 1.2
- momentum_y: float32 [1792, 4096], P('lat', 'lon'), may hold values from -1.2 to 1.2
- water_depth: float32 [1792, 4096], P('lat', 'lon'), may hold values from 0.7 to 1.4
- wet_mask: int32 [1792, 4096], P('lat', 'lon'), may hold values 0 or 1
- slide_cells: int32 [16, 2048], P('lat', 'lon'), may hold values from 0 to 14335
- slide_rate: float32 [16, 2048], P('lat', 'lon'), may hold values from 1 to 4
Outputs:
- surface_next: float32 [1792, 4096], P('lat', 'lon')
- momentum_x_next: float32 [1792, 4096], P('lat', 'lon')
- momentum_y_next: float32 [1792, 4096], P('lat', 'lon')
- velocity_u: float32 [1792, 4096], P('lat', 'lon')
- velocity_v: float32 [1792, 4096], P('lat', 'lon')
The draws below stay inside these ranges and needn't reach their ends.
Inputs may be any that keep to these rules, and one draw needn't show every extreme that they name: `slide_cells`: entry (r, c) lists a cell of the block of rows r * 112 onward and columns (c // 64) * 128 onward, as row * 128 + column inside that block; cells may repeat.
All inputs are finite; a program needn't handle non-finite values. No bound on the sum of `wet_mask` on one device may be relied on, other than what follows from the above.
Results may differ from the reference program's by a relative error of at most 0.0001.
Values sent between devices are 32-bit elements; how exact they have to be, the bound alone decides.
No kernel may reach another device: no remote copies, remote signals or barrier semaphores. Data moves between devices by JAX's collectives and lax.ppermute only.
A program may use at most 64 MiB of HBM per device.

```python
import math
import jax
import jax.numpy as jnp
from jax import lax

CX = 128
CY = 112
FOOT = 64
NX = 4096
NY = 1792
SLIDE_ROWS = 16
SLIDE_COLS = 2048


def touch_ends(drawn, rng, smallest, top_value):
    extent = drawn.shape
    index_at = [jax.random.randint(jax.random.fold_in(rng, axis), (), 0, extent[axis]) for axis in range(len(extent))]
    drawn = drawn.at[tuple(index_at)].set(smallest)
    longest = extent.index(max(extent))
    index_at[longest] = (index_at[longest] + 1) % extent[longest]
    return drawn.at[tuple(index_at)].set(top_value)


def level_of(own_key, extent, shards, low, largest):
    level, own = 1.0, jax.random.fold_in(own_key, 6)
    for dim, parts in shards:
        draws = jnp.exp(jax.random.uniform(jax.random.fold_in(own, dim), (parts,), jnp.float32, low / len(shards), largest / len(shards)))
        level = level * jnp.repeat(draws, extent[dim] // parts).reshape([-1 if axis == dim else 1 for axis in range(len(extent))])
    return level


def scatter_about(stream_key, dims, scale, most, shards=(), held_as=jnp.bfloat16):
    array = scale * jax.random.normal(stream_key, dims, jnp.float32)
    if shards:
        array = array * level_of(stream_key, dims, shards, -0.22, 0.18)
    return jnp.clip(array, -most, most).astype(held_as)


def setup_inputs(seed: int = 0) -> dict:
    splits = jax.random.split(jax.random.key(seed), 8)
    return {
        "surface": scatter_about(splits[0], (NY, NX), 0.08, 0.25, ((0, 16), (1, 32)), jnp.float32),
        "momentum_x": scatter_about(splits[1], (NY, NX), 0.3, 1.2, ((0, 16), (1, 32)), jnp.float32),
        "momentum_y": scatter_about(splits[2], (NY, NX), 0.3, 1.2, ((0, 16), (1, 32)), jnp.float32),
        "water_depth": jnp.clip(jnp.exp(math.log(1.4) - 0.6931472 * jax.random.uniform(splits[3], (NY, NX), jnp.float32) ** level_of(splits[3], (NY, NX), ((0, 16), (1, 32)), -0.2, 0.2)), 0.7, 1.4),
        "wet_mask": touch_ends((jax.random.randint(splits[4], (NY, NX), 0, 16) < 15).astype(jnp.int32), jax.random.fold_in(splits[4], 1), 0, 1),
        "slide_cells": touch_ends(jax.random.randint(splits[5], (SLIDE_ROWS, SLIDE_COLS), 0, CY * CX), jax.random.fold_in(splits[5], 1), 0, (CY * CX) - 1).astype(jnp.int32),
        "slide_rate": jnp.clip(jnp.exp(math.log(4.0) - 1.3862944 * jax.random.uniform(splits[6], (SLIDE_ROWS, SLIDE_COLS), jnp.float32) ** level_of(splits[6], (SLIDE_ROWS, SLIDE_COLS), ((0, 16), (1, 32)), -0.2, 0.2)), 1.0, 4.0),
    }


GRAVITY = 1.0
LON_SPACING = 0.5
LAT_SPACING = 0.6
TIME_STEP = 0.1

def slab_of(values, start, stop, along_axis):
    return lax.slice_in_dim(values, start, stop, axis=along_axis)

def limited(former, latter):
    return jnp.maximum(jnp.minimum(former, latter), 0.0) + jnp.minimum(jnp.maximum(former, latter), 0.0)

def face_states(values, along_axis):
    length = values.shape[along_axis]
    jumps = slab_of(values, 1, length, along_axis) - slab_of(values, 0, length - 1, along_axis)
    slopes = limited(slab_of(jumps, 0, length - 2, along_axis), slab_of(jumps, 1, length - 1, along_axis))
    left_state = slab_of(values, 1, length - 2, along_axis) + 0.5 * slab_of(slopes, 0, length - 3, along_axis)
    right_state = slab_of(values, 2, length - 1, along_axis) - 0.5 * slab_of(slopes, 1, length - 2, along_axis)
    return (left_state, right_state)

def wave_flux(surface_left, surface_right, normal_left, normal_right, tangent_left, tangent_right, face_depth, opened):
    height_left = surface_left + face_depth
    height_right = surface_right + face_depth
    celerity_left = jnp.sqrt(GRAVITY * height_left)
    celerity_right = jnp.sqrt(GRAVITY * height_right)
    slowest = jnp.minimum(jnp.minimum(normal_left - celerity_left, normal_right - celerity_right), 0.0)
    fastest = jnp.maximum(jnp.maximum(normal_left + celerity_left, normal_right + celerity_right), 0.0)
    spread = fastest - slowest
    product = slowest * fastest
    mass_left = height_left * normal_left
    mass_right = height_right * normal_right
    push_left = mass_left * normal_left + GRAVITY * (0.5 * surface_left * surface_left + face_depth * surface_left)
    push_right = mass_right * normal_right + GRAVITY * (0.5 * surface_right * surface_right + face_depth * surface_right)
    carry_left = mass_left * tangent_left
    carry_right = mass_right * tangent_right
    mass_flux = opened * (fastest * mass_left - slowest * mass_right + product * (surface_right - surface_left)) / spread
    push_flux = opened * (fastest * push_left - slowest * push_right + product * (mass_right - mass_left)) / spread
    carry_flux = opened * (fastest * carry_left - slowest * carry_right + product * (height_right * tangent_right - height_left * tangent_left)) / spread
    return (mass_flux, push_flux, carry_flux)

def tendencies(across, along):
    width = across[0].shape[1] - 4
    row_count = along[0].shape[0] - 4
    surface_pair = face_states(across[0], 1)
    east_pair = face_states(across[1], 1)
    north_pair = face_states(across[2], 1)
    depth_lon = 0.5 * (across[3][:, 1:width + 2] + across[3][:, 2:width + 3])
    open_lon = across[4][:, 1:width + 2] * across[4][:, 2:width + 3]
    mass_lon, push_lon, carry_lon = wave_flux(surface_pair[0], surface_pair[1], east_pair[0], east_pair[1], north_pair[0], north_pair[1], depth_lon, open_lon)
    surface_pair = face_states(along[0], 0)
    east_pair = face_states(along[1], 0)
    north_pair = face_states(along[2], 0)
    depth_lat = 0.5 * (along[3][1:row_count + 2] + along[3][2:row_count + 3])
    open_lat = along[4][1:row_count + 2] * along[4][2:row_count + 3]
    mass_lat, push_lat, carry_lat = wave_flux(surface_pair[0], surface_pair[1], north_pair[0], north_pair[1], east_pair[0], east_pair[1], depth_lat, open_lat)
    surface_mid = across[0][:, 2:width + 2]
    wet_mid = across[4][:, 2:width + 2]
    rate_surface = -(mass_lon[:, 1:] - mass_lon[:, :-1]) / LON_SPACING - (mass_lat[1:] - mass_lat[:-1]) / LAT_SPACING
    source_east = GRAVITY * surface_mid * (depth_lon[:, 1:] - depth_lon[:, :-1]) / LON_SPACING
    source_north = GRAVITY * surface_mid * (depth_lat[1:] - depth_lat[:-1]) / LAT_SPACING
    rate_east = wet_mid * (source_east - (push_lon[:, 1:] - push_lon[:, :-1]) / LON_SPACING - (carry_lat[1:] - carry_lat[:-1]) / LAT_SPACING)
    rate_north = wet_mid * (source_north - (carry_lon[:, 1:] - carry_lon[:, :-1]) / LON_SPACING - (push_lat[1:] - push_lat[:-1]) / LAT_SPACING)
    return (rate_surface, rate_east, rate_north)

def thomas(lower_band, main_band, upper_band, rights):
    zero_row = jnp.zeros_like(main_band[0])

    def forward(carry, entries):
        ratio_prev, solved_prev = carry
        lower_now, main_now, upper_now, right_now = entries
        pivot = main_now - lower_now * ratio_prev
        ratio_now = upper_now / pivot
        solved_now = tuple(((member - lower_now * earlier) / pivot for member, earlier in zip(right_now, solved_prev)))
        return ((ratio_now, solved_now), (ratio_now, solved_now))
    start_state = (zero_row, tuple((zero_row for member in rights)))
    ignored, (ratios, reduced) = lax.scan(forward, start_state, (lower_band, main_band, upper_band, tuple(rights)))

    def backward(carry, entries):
        ratio_now, reduced_now = entries
        result = tuple((member - ratio_now * later for member, later in zip(reduced_now, carry)))
        return (result, result)
    ignored, solution = lax.scan(backward, tuple((zero_row for member in rights)), (ratios, reduced), reverse=True)
    return list(solution)

def cyclic_solve(lower_band, main_band, upper_band, rights):
    corner_top = lower_band[0]
    corner_bottom = upper_band[-1]
    shift_value = -main_band[0]
    main_open = main_band.at[0].add(-shift_value).at[-1].add(-corner_bottom * corner_top / shift_value)
    lower_open = lower_band.at[0].set(0.0)
    upper_open = upper_band.at[-1].set(0.0)
    helper_right = jnp.zeros_like(main_band).at[0].set(shift_value).at[-1].set(corner_bottom)
    solved = thomas(lower_open, main_open, upper_open, list(rights) + [helper_right])
    helper = solved[-1]
    denominator = 1.0 + helper[0] + corner_top * helper[-1] / shift_value
    return [member - (member[0] + corner_top * member[-1] / shift_value) / denominator * helper for member in solved[:-1]]

def extend(field, sign):
    wide = jnp.concatenate([field[:, -2:], field, field[:, :2]], axis=1)
    return jnp.concatenate([sign * wide[1::-1], wide, sign * wide[-1:-3:-1]], axis=0)

def section_tendency(surface, momentum_x, momentum_y, water_depth, wet_float, lift):
    height = water_depth + surface
    coef_lon = water_depth * water_depth / (3.0 * LON_SPACING * LON_SPACING)
    coef_lat = water_depth * water_depth / (3.0 * LAT_SPACING * LAT_SPACING)
    coef_turned = coef_lon.T
    east_raw = cyclic_solve(-coef_turned, 1.0 + 2.0 * coef_turned, -coef_turned, [(momentum_x / height).T])[0].T
    velocity_u = wet_float * east_raw
    north_raw = thomas(-coef_lat, 1.0 + 2.0 * coef_lat, -coef_lat, [momentum_y / height])[0]
    velocity_v = wet_float * north_raw
    padded = jnp.stack([extend(surface, 1.0), extend(velocity_u, 1.0), extend(velocity_v, -1.0), extend(water_depth, 1.0), extend(wet_float, 1.0)])
    block_rows = CY // 8

    def one_block(start):
        across = lax.dynamic_slice_in_dim(padded, start + 2, block_rows, axis=1)
        along = lax.dynamic_slice_in_dim(padded, start, block_rows + 4, axis=1)[:, :, 2:-2]
        return tendencies(across, along)
    starts = (jnp.arange(NY // block_rows) * block_rows).astype(jnp.int32)
    rates = lax.map(one_block, starts)
    rate_surface, rate_east, rate_north = (member.reshape(NY, NX) for member in rates)
    return ((rate_surface + lift, rate_east, rate_north), velocity_u, velocity_v)

def reference(surface, momentum_x, momentum_y, water_depth, wet_mask, slide_cells, slide_rate):
    wet_float = wet_mask.astype(jnp.float32)
    tile_row = lax.broadcasted_iota(jnp.int32, slide_cells.shape, 0)
    tile_col = lax.broadcasted_iota(jnp.int32, slide_cells.shape, 1) // FOOT
    cell_row = tile_row * CY + slide_cells // CX
    cell_col = tile_col * CX + slide_cells % CX
    lift = jnp.zeros((NY, NX), jnp.float32).at[cell_row, cell_col].add(slide_rate)
    initial = (surface, momentum_x, momentum_y)
    current = initial
    velocity_u = surface
    velocity_v = surface
    for first, second in ((0.0, 1.0), (0.75, 0.25), (1.0 / 3.0, 2.0 / 3.0)):
        rates, velocity_u, velocity_v = section_tendency(current[0], current[1], current[2], water_depth, wet_float, lift)
        current = tuple((first * start_value + second * (now + TIME_STEP * rate) for start_value, now, rate in zip(initial, current, rates)))
    return (current[0], current[1], current[2], velocity_u, velocity_v)
```

```python
import jax
import jax.numpy as jnp
from jax import lax
from jax.sharding import PartitionSpec as P

GRAVITY = 1.0
LON_SPACING = 0.5
LAT_SPACING = 0.6
TIME_STEP = 0.1
WINDOW_LON = 40
WINDOW_LAT = 32


def shifted(block, axis, distance):
    devices = range(lax.axis_size(axis))
    route = [((i - distance) % len(devices), i) for i in devices]
    return lax.ppermute(block, axis, route)


def passed_along(x, axis, by):
    peers = lax.axis_size(axis)
    pairs = [(i, i + by) for i in range(peers) if 0 <= i + by < peers]
    return lax.ppermute(x, axis, pairs)


def extended(cells, sides, width, closed):
    for axis, dim in sides:
        count = lax.axis_size(axis)
        ends = count if closed else count - 1
        head = lax.slice_in_dim(cells, 0, width, axis=dim)
        tail = lax.slice_in_dim(cells, cells.shape[dim] - width, cells.shape[dim], axis=dim)
        cells = jnp.concatenate(
            [
                lax.ppermute(tail, axis, [(i, (i + 1) % count) for i in range(ends)]),
                cells,
                lax.ppermute(head, axis, [((i + 1) % count, i) for i in range(ends)]),
            ],
            axis=dim,
        )
    return cells


def slab_of(values, start, stop, along_axis):
    return lax.slice_in_dim(values, start, stop, axis=along_axis)


def limited(former, latter):
    return jnp.maximum(jnp.minimum(former, latter), 0.0) + jnp.minimum(
        jnp.maximum(former, latter), 0.0
    )


def face_states(values, along_axis):
    length = values.shape[along_axis]
    jumps = slab_of(values, 1, length, along_axis) - slab_of(values, 0, length - 1, along_axis)
    slopes = limited(
        slab_of(jumps, 0, length - 2, along_axis), slab_of(jumps, 1, length - 1, along_axis)
    )
    left_state = slab_of(values, 1, length - 2, along_axis) + 0.5 * slab_of(
        slopes, 0, length - 3, along_axis
    )
    right_state = slab_of(values, 2, length - 1, along_axis) - 0.5 * slab_of(
        slopes, 1, length - 2, along_axis
    )
    return (left_state, right_state)


def wave_flux(
    surface_left,
    surface_right,
    normal_left,
    normal_right,
    tangent_left,
    tangent_right,
    face_depth,
    opened,
):
    height_left = surface_left + face_depth
    height_right = surface_right + face_depth
    celerity_left = jnp.sqrt(GRAVITY * height_left)
    celerity_right = jnp.sqrt(GRAVITY * height_right)
    slowest = jnp.minimum(
        jnp.minimum(normal_left - celerity_left, normal_right - celerity_right), 0.0
    )
    fastest = jnp.maximum(
        jnp.maximum(normal_left + celerity_left, normal_right + celerity_right), 0.0
    )
    spread = fastest - slowest
    product = slowest * fastest
    mass_left = height_left * normal_left
    mass_right = height_right * normal_right
    push_left = mass_left * normal_left + GRAVITY * (
        0.5 * surface_left * surface_left + face_depth * surface_left
    )
    push_right = mass_right * normal_right + GRAVITY * (
        0.5 * surface_right * surface_right + face_depth * surface_right
    )
    carry_left = mass_left * tangent_left
    carry_right = mass_right * tangent_right
    mass_flux = (
        opened
        * (fastest * mass_left - slowest * mass_right + product * (surface_right - surface_left))
        / spread
    )
    push_flux = (
        opened
        * (fastest * push_left - slowest * push_right + product * (mass_right - mass_left))
        / spread
    )
    carry_flux = (
        opened
        * (
            fastest * carry_left
            - slowest * carry_right
            + product * (height_right * tangent_right - height_left * tangent_left)
        )
        / spread
    )
    return (mass_flux, push_flux, carry_flux)


def tendencies(across, along):
    width = across[0].shape[1] - 4
    row_count = along[0].shape[0] - 4
    surface_pair = face_states(across[0], 1)
    east_pair = face_states(across[1], 1)
    north_pair = face_states(across[2], 1)
    depth_lon = 0.5 * (across[3][:, 1 : width + 2] + across[3][:, 2 : width + 3])
    open_lon = across[4][:, 1 : width + 2] * across[4][:, 2 : width + 3]
    mass_lon, push_lon, carry_lon = wave_flux(
        surface_pair[0],
        surface_pair[1],
        east_pair[0],
        east_pair[1],
        north_pair[0],
        north_pair[1],
        depth_lon,
        open_lon,
    )
    surface_pair = face_states(along[0], 0)
    east_pair = face_states(along[1], 0)
    north_pair = face_states(along[2], 0)
    depth_lat = 0.5 * (along[3][1 : row_count + 2] + along[3][2 : row_count + 3])
    open_lat = along[4][1 : row_count + 2] * along[4][2 : row_count + 3]
    mass_lat, push_lat, carry_lat = wave_flux(
        surface_pair[0],
        surface_pair[1],
        north_pair[0],
        north_pair[1],
        east_pair[0],
        east_pair[1],
        depth_lat,
        open_lat,
    )
    surface_mid = across[0][:, 2 : width + 2]
    wet_mid = across[4][:, 2 : width + 2]
    rate_surface = (
        -(mass_lon[:, 1:] - mass_lon[:, :-1]) / LON_SPACING
        - (mass_lat[1:] - mass_lat[:-1]) / LAT_SPACING
    )
    source_east = GRAVITY * surface_mid * (depth_lon[:, 1:] - depth_lon[:, :-1]) / LON_SPACING
    source_north = GRAVITY * surface_mid * (depth_lat[1:] - depth_lat[:-1]) / LAT_SPACING
    rate_east = wet_mid * (
        source_east
        - (push_lon[:, 1:] - push_lon[:, :-1]) / LON_SPACING
        - (carry_lat[1:] - carry_lat[:-1]) / LAT_SPACING
    )
    rate_north = wet_mid * (
        source_north
        - (carry_lon[:, 1:] - carry_lon[:, :-1]) / LON_SPACING
        - (push_lat[1:] - push_lat[:-1]) / LAT_SPACING
    )
    return (rate_surface, rate_east, rate_north)


def from_below(values, stride, along_axis, filler):
    length = values.shape[along_axis]
    padding = jnp.full_like(slab_of(values, 0, stride, along_axis), filler)
    return jnp.concatenate([padding, slab_of(values, 0, length - stride, along_axis)], along_axis)


def from_above(values, stride, along_axis, filler):
    length = values.shape[along_axis]
    padding = jnp.full_like(slab_of(values, 0, stride, along_axis), filler)
    return jnp.concatenate([slab_of(values, stride, length, along_axis), padding], along_axis)


def reduction_plan(lower_band, main_band, upper_band, along_axis):
    length = main_band.shape[along_axis]
    stride = 1
    weights = []
    while stride < length:
        below = [from_below(band, stride, along_axis, fill) for band, fill in
                 ((lower_band, 0.0), (main_band, 1.0), (upper_band, 0.0))]
        above = [from_above(band, stride, along_axis, fill) for band, fill in
                 ((lower_band, 0.0), (main_band, 1.0), (upper_band, 0.0))]
        weight_below = lower_band / below[1]
        weight_above = upper_band / above[1]
        new_lower = -weight_below * below[0]
        new_main = main_band - weight_below * below[2] - weight_above * above[0]
        new_upper = -weight_above * above[2]
        weights.append((weight_below, weight_above))
        lower_band, main_band, upper_band = new_lower, new_main, new_upper
        stride = stride * 2
    return weights, main_band


def apply_plan(plan, rights, along_axis):
    weights, main_band = plan
    stride = 1
    for weight_below, weight_above in weights:
        rights = (
            rights
            - weight_below * from_below(rights, stride, along_axis, 0.0)
            - weight_above * from_above(rights, stride, along_axis, 0.0)
        )
        stride = stride * 2
    return rights / main_band


def halo_box(fields, wide_x, wide_y, place, count):
    lon_count = lax.axis_size("lon")
    west = lax.ppermute(
        fields[:, :, -wide_x:], "lon", [(i, (i + 1) % lon_count) for i in range(lon_count)]
    )
    east = lax.ppermute(
        fields[:, :, :wide_x], "lon", [((i + 1) % lon_count, i) for i in range(lon_count)]
    )
    wide = jnp.concatenate([west, fields, east], axis=2)
    above = passed_along(wide[:, -wide_y:], "lat", 1)
    below = passed_along(wide[:, :wide_y], "lat", -1)
    above = jnp.where(place == 0, wide[:, wide_y - 1 :: -1], above)
    below = jnp.where(place == count - 1, wide[:, : -wide_y - 1 : -1], below)
    return jnp.concatenate([above, wide, below], axis=1)


def local(surface, momentum_x, momentum_y, water_depth, wet_mask, slide_cells, slide_rate):
    wet_float = wet_mask.astype(jnp.float32)
    place = lax.axis_index("lat")
    count = lax.axis_size("lat")
    tile_rows, tile_cols = surface.shape
    wide_x = WINDOW_LON + 2
    wide_y = WINDOW_LAT + 2
    lift = (
        jnp.zeros((tile_rows * tile_cols,), jnp.float32)
        .at[slide_cells.reshape(-1)]
        .add(slide_rate.reshape(-1))
        .reshape(tile_rows, tile_cols)
    )
    box_rows = tile_rows + 2 * wide_y
    box_cols = tile_cols + 2 * wide_x
    core_rows = slice(wide_y - 2, wide_y + tile_rows + 2)
    core_cols = slice(wide_x - 2, wide_x + tile_cols + 2)
    global_row = place * tile_rows - wide_y + lax.broadcasted_iota(
        jnp.int32, (box_rows, tile_cols + 4), 0
    )
    inside = (global_row >= 0) & (global_row < count * tile_rows)

    initial = (surface, momentum_x, momentum_y)
    current = initial
    velocity_u = surface
    velocity_v = surface
    plans = None
    for first, second in ((0.0, 1.0), (0.75, 0.25), (1.0 / 3.0, 2.0 / 3.0)):
        if plans is None:
            box = halo_box(
                jnp.stack([current[0], current[1], current[2], water_depth, wet_float]),
                wide_x, wide_y, place, count,
            )
            depth_box, wet_box = box[3], box[4]
            coef_lon = depth_box[core_rows] * depth_box[core_rows] / (3.0 * LON_SPACING * LON_SPACING)
            coef_lat = depth_box[:, core_cols] * depth_box[:, core_cols] / (3.0 * LAT_SPACING * LAT_SPACING)
            plans = (
                reduction_plan(-coef_lon, 1.0 + 2.0 * coef_lon, -coef_lon, 1),
                reduction_plan(
                    jnp.where(inside, -coef_lat, 0.0),
                    jnp.where(inside, 1.0 + 2.0 * coef_lat, 1.0),
                    jnp.where(inside, -coef_lat, 0.0),
                    0,
                ),
            )
        else:
            box = halo_box(jnp.stack(list(current)), wide_x, wide_y, place, count)
        surface_box, east_box, north_box = box[0], box[1], box[2]
        height_box = depth_box + surface_box
        east_raw = apply_plan(plans[0], east_box[core_rows] / height_box[core_rows], 1)[:, core_cols]
        north_rights = jnp.where(inside, north_box[:, core_cols] / height_box[:, core_cols], 0.0)
        north_raw = apply_plan(plans[1], north_rights, 0)[core_rows]
        wet_core = wet_box[core_rows, core_cols]
        u_core = wet_core * east_raw
        v_core = wet_core * north_raw
        v_core = jnp.where(place == 0, jnp.concatenate([-v_core[3:1:-1], v_core[2:]], axis=0), v_core)
        v_core = jnp.where(
            place == count - 1, jnp.concatenate([v_core[:-2], -v_core[-3:-5:-1]], axis=0), v_core
        )
        fields = jnp.stack(
            [surface_box[core_rows, core_cols], u_core, v_core, depth_box[core_rows, core_cols], wet_core]
        )
        across = fields[:, 2:-2, :]
        along = fields[:, :, 2:-2]
        rate_surface, rate_east, rate_north = tendencies(across, along)
        rates = (rate_surface + lift, rate_east, rate_north)
        velocity_u = u_core[2:-2, 2:-2]
        velocity_v = v_core[2:-2, 2:-2]
        current = tuple(
            (
                first * start_value + second * (now + TIME_STEP * rate)
                for start_value, now, rate in zip(initial, current, rates)
            )
        )
    return (current[0], current[1], current[2], velocity_u, velocity_v)


def solution(mesh):
    in_specs = (P("lat", "lon"),) * 7
    out_specs = (P("lat", "lon"),) * 5
    return jax.shard_map(local, mesh=mesh, in_specs=in_specs, out_specs=out_specs, check_vma=False)
```

```python
import jax
import jax.numpy as jnp
from jax import lax
from jax.sharding import PartitionSpec as P
from jax.experimental import pallas as pl
from jax.experimental.pallas import tpu as pltpu

GRAVITY = 1.0
LON_SPACING = 0.5
LAT_SPACING = 0.6
TIME_STEP = 0.1
WINDOW_LON = 40
WINDOW_LAT = 32
PCR_STEPS = 6


def shifted(block, axis, distance):
    devices = range(lax.axis_size(axis))
    route = [((i - distance) % len(devices), i) for i in devices]
    return lax.ppermute(block, axis, route)


def passed_along(x, axis, by):
    peers = lax.axis_size(axis)
    pairs = [(i, i + by) for i in range(peers) if 0 <= i + by < peers]
    return lax.ppermute(x, axis, pairs)


def extended(cells, sides, width, closed):
    for axis, dim in sides:
        count = lax.axis_size(axis)
        ends = count if closed else count - 1
        head = lax.slice_in_dim(cells, 0, width, axis=dim)
        tail = lax.slice_in_dim(cells, cells.shape[dim] - width, cells.shape[dim], axis=dim)
        cells = jnp.concatenate(
            [
                lax.ppermute(tail, axis, [(i, (i + 1) % count) for i in range(ends)]),
                cells,
                lax.ppermute(head, axis, [((i + 1) % count, i) for i in range(ends)]),
            ],
            axis=dim,
        )
    return cells


def slab_of(values, start, stop, along_axis):
    return lax.slice_in_dim(values, start, stop, axis=along_axis)


def limited(former, latter):
    return jnp.maximum(jnp.minimum(former, latter), 0.0) + jnp.minimum(
        jnp.maximum(former, latter), 0.0
    )


def face_states(values, along_axis):
    length = values.shape[along_axis]
    jumps = slab_of(values, 1, length, along_axis) - slab_of(values, 0, length - 1, along_axis)
    slopes = limited(
        slab_of(jumps, 0, length - 2, along_axis), slab_of(jumps, 1, length - 1, along_axis)
    )
    left_state = slab_of(values, 1, length - 2, along_axis) + 0.5 * slab_of(
        slopes, 0, length - 3, along_axis
    )
    right_state = slab_of(values, 2, length - 1, along_axis) - 0.5 * slab_of(
        slopes, 1, length - 2, along_axis
    )
    return (left_state, right_state)


def wave_flux(
    surface_left,
    surface_right,
    normal_left,
    normal_right,
    tangent_left,
    tangent_right,
    face_depth,
    opened,
):
    height_left = surface_left + face_depth
    height_right = surface_right + face_depth
    celerity_left = jnp.sqrt(GRAVITY * height_left)
    celerity_right = jnp.sqrt(GRAVITY * height_right)
    slowest = jnp.minimum(
        jnp.minimum(normal_left - celerity_left, normal_right - celerity_right), 0.0
    )
    fastest = jnp.maximum(
        jnp.maximum(normal_left + celerity_left, normal_right + celerity_right), 0.0
    )
    spread = fastest - slowest
    product = slowest * fastest
    mass_left = height_left * normal_left
    mass_right = height_right * normal_right
    push_left = mass_left * normal_left + GRAVITY * (
        0.5 * surface_left * surface_left + face_depth * surface_left
    )
    push_right = mass_right * normal_right + GRAVITY * (
        0.5 * surface_right * surface_right + face_depth * surface_right
    )
    carry_left = mass_left * tangent_left
    carry_right = mass_right * tangent_right
    mass_flux = (
        opened
        * (fastest * mass_left - slowest * mass_right + product * (surface_right - surface_left))
        / spread
    )
    push_flux = (
        opened
        * (fastest * push_left - slowest * push_right + product * (mass_right - mass_left))
        / spread
    )
    carry_flux = (
        opened
        * (
            fastest * carry_left
            - slowest * carry_right
            + product * (height_right * tangent_right - height_left * tangent_left)
        )
        / spread
    )
    return (mass_flux, push_flux, carry_flux)


def tendencies(across, along):
    width = across[0].shape[1] - 4
    row_count = along[0].shape[0] - 4
    surface_pair = face_states(across[0], 1)
    east_pair = face_states(across[1], 1)
    north_pair = face_states(across[2], 1)
    depth_lon = 0.5 * (across[3][:, 1 : width + 2] + across[3][:, 2 : width + 3])
    open_lon = across[4][:, 1 : width + 2] * across[4][:, 2 : width + 3]
    mass_lon, push_lon, carry_lon = wave_flux(
        surface_pair[0],
        surface_pair[1],
        east_pair[0],
        east_pair[1],
        north_pair[0],
        north_pair[1],
        depth_lon,
        open_lon,
    )
    surface_pair = face_states(along[0], 0)
    east_pair = face_states(along[1], 0)
    north_pair = face_states(along[2], 0)
    depth_lat = 0.5 * (along[3][1 : row_count + 2] + along[3][2 : row_count + 3])
    open_lat = along[4][1 : row_count + 2] * along[4][2 : row_count + 3]
    mass_lat, push_lat, carry_lat = wave_flux(
        surface_pair[0],
        surface_pair[1],
        north_pair[0],
        north_pair[1],
        east_pair[0],
        east_pair[1],
        depth_lat,
        open_lat,
    )
    surface_mid = across[0][:, 2 : width + 2]
    wet_mid = across[4][:, 2 : width + 2]
    rate_surface = (
        -(mass_lon[:, 1:] - mass_lon[:, :-1]) / LON_SPACING
        - (mass_lat[1:] - mass_lat[:-1]) / LAT_SPACING
    )
    source_east = GRAVITY * surface_mid * (depth_lon[:, 1:] - depth_lon[:, :-1]) / LON_SPACING
    source_north = GRAVITY * surface_mid * (depth_lat[1:] - depth_lat[:-1]) / LAT_SPACING
    rate_east = wet_mid * (
        source_east
        - (push_lon[:, 1:] - push_lon[:, :-1]) / LON_SPACING
        - (carry_lat[1:] - carry_lat[:-1]) / LAT_SPACING
    )
    rate_north = wet_mid * (
        source_north
        - (carry_lon[:, 1:] - carry_lon[:, :-1]) / LON_SPACING
        - (push_lat[1:] - push_lat[:-1]) / LAT_SPACING
    )
    return (rate_surface, rate_east, rate_north)


def from_below(values, stride, along_axis, filler):
    length = values.shape[along_axis]
    padding = jnp.full_like(slab_of(values, 0, stride, along_axis), filler)
    return jnp.concatenate([padding, slab_of(values, 0, length - stride, along_axis)], along_axis)


def from_above(values, stride, along_axis, filler):
    length = values.shape[along_axis]
    padding = jnp.full_like(slab_of(values, 0, stride, along_axis), filler)
    return jnp.concatenate([slab_of(values, stride, length, along_axis), padding], along_axis)


def reduction_kernel(lower_ref, main_ref, upper_ref, rights_ref, out_ref, *, along_axis):
    lower_band, main_band, upper_band = lower_ref[...], main_ref[...], upper_ref[...]
    rights = rights_ref[...]
    length = rights.shape[along_axis]
    position = lax.broadcasted_iota(jnp.int32, rights.shape, along_axis)
    stride = 1
    for _ in range(PCR_STEPS):
        def from_lower(values, fill):
            return jnp.where(position >= stride, pltpu.roll(values, stride, along_axis), fill)

        def from_upper(values, fill):
            return jnp.where(
                position < length - stride, pltpu.roll(values, length - stride, along_axis), fill
            )

        below = [from_lower(band, fill) for band, fill in
                 ((lower_band, 0.0), (main_band, 1.0), (upper_band, 0.0), (rights, 0.0))]
        above = [from_upper(band, fill) for band, fill in
                 ((lower_band, 0.0), (main_band, 1.0), (upper_band, 0.0), (rights, 0.0))]
        weight_below = lower_band / below[1]
        weight_above = upper_band / above[1]
        new_lower = -weight_below * below[0]
        new_main = main_band - weight_below * below[2] - weight_above * above[0]
        new_upper = -weight_above * above[2]
        rights = rights - weight_below * below[3] - weight_above * above[3]
        lower_band, main_band, upper_band = new_lower, new_main, new_upper
        stride = stride * 2
    out_ref[...] = rights / main_band


def padded(values, shape, fill):
    return jnp.pad(
        values, [(0, want - have) for want, have in zip(shape, values.shape)], constant_values=fill
    )


def line_solve(bands, rights, along_axis):
    lower_band, main_band, upper_band = bands
    shape = main_band.shape
    count = rights.shape
    spec = pl.BlockSpec(memory_space=pltpu.VMEM)
    solved = pl.pallas_call(
        lambda *refs: reduction_kernel(*refs, along_axis=along_axis),
        out_shape=jax.ShapeDtypeStruct(shape, jnp.float32),
        in_specs=[spec] * 4,
        out_specs=spec,
        name="line_solve",
    )(lower_band, main_band, upper_band, padded(rights, shape, 0.0))
    return solved[: count[0], : count[1]]


def band_set(coef, keep):
    shape = tuple(-(-size // unit) * unit for size, unit in zip(coef.shape, (8, 128)))
    return (
        padded(jnp.where(keep, -coef, 0.0), shape, 0.0),
        padded(jnp.where(keep, 1.0 + 2.0 * coef, 1.0), shape, 1.0),
        padded(jnp.where(keep, -coef, 0.0), shape, 0.0),
    )


def halo_box(fields, wide_x, wide_y, place, count):
    lon_count = lax.axis_size("lon")
    west = lax.ppermute(
        fields[:, :, -wide_x:], "lon", [(i, (i + 1) % lon_count) for i in range(lon_count)]
    )
    east = lax.ppermute(
        fields[:, :, :wide_x], "lon", [((i + 1) % lon_count, i) for i in range(lon_count)]
    )
    wide = jnp.concatenate([west, fields, east], axis=2)
    above = passed_along(wide[:, -wide_y:], "lat", 1)
    below = passed_along(wide[:, :wide_y], "lat", -1)
    above = jnp.where(place == 0, wide[:, wide_y - 1 :: -1], above)
    below = jnp.where(place == count - 1, wide[:, : -wide_y - 1 : -1], below)
    return jnp.concatenate([above, wide, below], axis=1)


def local(surface, momentum_x, momentum_y, water_depth, wet_mask, slide_cells, slide_rate):
    wet_float = wet_mask.astype(jnp.float32)
    place = lax.axis_index("lat")
    count = lax.axis_size("lat")
    tile_rows, tile_cols = surface.shape
    wide_x = WINDOW_LON + 2
    wide_y = WINDOW_LAT + 2
    lift = (
        jnp.zeros((tile_rows * tile_cols,), jnp.float32)
        .at[slide_cells.reshape(-1)]
        .add(slide_rate.reshape(-1))
        .reshape(tile_rows, tile_cols)
    )
    box_rows = tile_rows + 2 * wide_y
    box_cols = tile_cols + 2 * wide_x
    core_rows = slice(wide_y - 2, wide_y + tile_rows + 2)
    core_cols = slice(wide_x - 2, wide_x + tile_cols + 2)
    global_row = place * tile_rows - wide_y + lax.broadcasted_iota(
        jnp.int32, (box_rows, tile_cols + 4), 0
    )
    inside = (global_row >= 0) & (global_row < count * tile_rows)

    initial = (surface, momentum_x, momentum_y)
    current = initial
    velocity_u = surface
    velocity_v = surface
    bands = None
    for first, second in ((0.0, 1.0), (0.75, 0.25), (1.0 / 3.0, 2.0 / 3.0)):
        if bands is None:
            box = halo_box(
                jnp.stack([current[0], current[1], current[2], water_depth, wet_float]),
                wide_x, wide_y, place, count,
            )
            depth_box, wet_box = box[3], box[4]
            coef_lon = depth_box[core_rows] * depth_box[core_rows] / (3.0 * LON_SPACING * LON_SPACING)
            coef_lat = depth_box[:, core_cols] * depth_box[:, core_cols] / (3.0 * LAT_SPACING * LAT_SPACING)
            bands = (band_set(coef_lon, True), band_set(coef_lat, inside))
        else:
            box = halo_box(jnp.stack(list(current)), wide_x, wide_y, place, count)
        surface_box, east_box, north_box = box[0], box[1], box[2]
        height_box = depth_box + surface_box
        east_raw = line_solve(bands[0], east_box[core_rows] / height_box[core_rows], 1)[:, core_cols]
        north_rights = jnp.where(inside, north_box[:, core_cols] / height_box[:, core_cols], 0.0)
        north_raw = line_solve(bands[1], north_rights, 0)[core_rows]
        wet_core = wet_box[core_rows, core_cols]
        u_core = wet_core * east_raw
        v_core = wet_core * north_raw
        v_core = jnp.where(place == 0, jnp.concatenate([-v_core[3:1:-1], v_core[2:]], axis=0), v_core)
        v_core = jnp.where(
            place == count - 1, jnp.concatenate([v_core[:-2], -v_core[-3:-5:-1]], axis=0), v_core
        )
        fields = jnp.stack(
            [surface_box[core_rows, core_cols], u_core, v_core, depth_box[core_rows, core_cols], wet_core]
        )
        across = fields[:, 2:-2, :]
        along = fields[:, :, 2:-2]
        rate_surface, rate_east, rate_north = tendencies(across, along)
        rates = (rate_surface + lift, rate_east, rate_north)
        velocity_u = u_core[2:-2, 2:-2]
        velocity_v = v_core[2:-2, 2:-2]
        current = tuple(
            (
                first * start_value + second * (now + TIME_STEP * rate)
                for start_value, now, rate in zip(initial, current, rates)
            )
        )
    return (current[0], current[1], current[2], velocity_u, velocity_v)


def solution(mesh):
    in_specs = (P("lat", "lon"),) * 7
    out_specs = (P("lat", "lon"),) * 5
    return jax.shard_map(local, mesh=mesh, in_specs=in_specs, out_specs=out_specs, check_vma=False)
```

```python
import jax
import jax.numpy as jnp
from jax import lax
from jax.sharding import PartitionSpec as P
from jax.experimental import pallas as pl
from jax.experimental.pallas import tpu as pltpu

GRAVITY = 1.0
LON_SPACING = 0.5
LAT_SPACING = 0.6
TIME_STEP = 0.1
WINDOW_LON = 40
WINDOW_LAT = 32
PCR_STEPS = 6


def shifted(block, axis, distance):
    devices = range(lax.axis_size(axis))
    route = [((i - distance) % len(devices), i) for i in devices]
    return lax.ppermute(block, axis, route)


def passed_along(x, axis, by):
    peers = lax.axis_size(axis)
    pairs = [(i, i + by) for i in range(peers) if 0 <= i + by < peers]
    return lax.ppermute(x, axis, pairs)


def extended(cells, sides, width, closed):
    for axis, dim in sides:
        count = lax.axis_size(axis)
        ends = count if closed else count - 1
        head = lax.slice_in_dim(cells, 0, width, axis=dim)
        tail = lax.slice_in_dim(cells, cells.shape[dim] - width, cells.shape[dim], axis=dim)
        cells = jnp.concatenate(
            [
                lax.ppermute(tail, axis, [(i, (i + 1) % count) for i in range(ends)]),
                cells,
                lax.ppermute(head, axis, [((i + 1) % count, i) for i in range(ends)]),
            ],
            axis=dim,
        )
    return cells


def slab_of(values, start, stop, along_axis):
    return lax.slice_in_dim(values, start, stop, axis=along_axis)


def limited(former, latter):
    return jnp.maximum(jnp.minimum(former, latter), 0.0) + jnp.minimum(
        jnp.maximum(former, latter), 0.0
    )


def face_states(values, along_axis):
    length = values.shape[along_axis]
    jumps = slab_of(values, 1, length, along_axis) - slab_of(values, 0, length - 1, along_axis)
    slopes = limited(
        slab_of(jumps, 0, length - 2, along_axis), slab_of(jumps, 1, length - 1, along_axis)
    )
    left_state = slab_of(values, 1, length - 2, along_axis) + 0.5 * slab_of(
        slopes, 0, length - 3, along_axis
    )
    right_state = slab_of(values, 2, length - 1, along_axis) - 0.5 * slab_of(
        slopes, 1, length - 2, along_axis
    )
    return (left_state, right_state)


def wave_flux(
    surface_left,
    surface_right,
    normal_left,
    normal_right,
    tangent_left,
    tangent_right,
    face_depth,
    opened,
):
    height_left = surface_left + face_depth
    height_right = surface_right + face_depth
    celerity_left = jnp.sqrt(GRAVITY * height_left)
    celerity_right = jnp.sqrt(GRAVITY * height_right)
    slowest = jnp.minimum(
        jnp.minimum(normal_left - celerity_left, normal_right - celerity_right), 0.0
    )
    fastest = jnp.maximum(
        jnp.maximum(normal_left + celerity_left, normal_right + celerity_right), 0.0
    )
    spread = fastest - slowest
    product = slowest * fastest
    mass_left = height_left * normal_left
    mass_right = height_right * normal_right
    push_left = mass_left * normal_left + GRAVITY * (
        0.5 * surface_left * surface_left + face_depth * surface_left
    )
    push_right = mass_right * normal_right + GRAVITY * (
        0.5 * surface_right * surface_right + face_depth * surface_right
    )
    carry_left = mass_left * tangent_left
    carry_right = mass_right * tangent_right
    mass_flux = (
        opened
        * (fastest * mass_left - slowest * mass_right + product * (surface_right - surface_left))
        / spread
    )
    push_flux = (
        opened
        * (fastest * push_left - slowest * push_right + product * (mass_right - mass_left))
        / spread
    )
    carry_flux = (
        opened
        * (
            fastest * carry_left
            - slowest * carry_right
            + product * (height_right * tangent_right - height_left * tangent_left)
        )
        / spread
    )
    return (mass_flux, push_flux, carry_flux)


def tendencies(across, along):
    width = across[0].shape[1] - 4
    row_count = along[0].shape[0] - 4
    surface_pair = face_states(across[0], 1)
    east_pair = face_states(across[1], 1)
    north_pair = face_states(across[2], 1)
    depth_lon = 0.5 * (across[3][:, 1 : width + 2] + across[3][:, 2 : width + 3])
    open_lon = across[4][:, 1 : width + 2] * across[4][:, 2 : width + 3]
    mass_lon, push_lon, carry_lon = wave_flux(
        surface_pair[0],
        surface_pair[1],
        east_pair[0],
        east_pair[1],
        north_pair[0],
        north_pair[1],
        depth_lon,
        open_lon,
    )
    surface_pair = face_states(along[0], 0)
    east_pair = face_states(along[1], 0)
    north_pair = face_states(along[2], 0)
    depth_lat = 0.5 * (along[3][1 : row_count + 2] + along[3][2 : row_count + 3])
    open_lat = along[4][1 : row_count + 2] * along[4][2 : row_count + 3]
    mass_lat, push_lat, carry_lat = wave_flux(
        surface_pair[0],
        surface_pair[1],
        north_pair[0],
        north_pair[1],
        east_pair[0],
        east_pair[1],
        depth_lat,
        open_lat,
    )
    surface_mid = across[0][:, 2 : width + 2]
    wet_mid = across[4][:, 2 : width + 2]
    rate_surface = (
        -(mass_lon[:, 1:] - mass_lon[:, :-1]) / LON_SPACING
        - (mass_lat[1:] - mass_lat[:-1]) / LAT_SPACING
    )
    source_east = GRAVITY * surface_mid * (depth_lon[:, 1:] - depth_lon[:, :-1]) / LON_SPACING
    source_north = GRAVITY * surface_mid * (depth_lat[1:] - depth_lat[:-1]) / LAT_SPACING
    rate_east = wet_mid * (
        source_east
        - (push_lon[:, 1:] - push_lon[:, :-1]) / LON_SPACING
        - (carry_lat[1:] - carry_lat[:-1]) / LAT_SPACING
    )
    rate_north = wet_mid * (
        source_north
        - (carry_lon[:, 1:] - carry_lon[:, :-1]) / LON_SPACING
        - (push_lat[1:] - push_lat[:-1]) / LAT_SPACING
    )
    return (rate_surface, rate_east, rate_north)


def from_below(values, stride, along_axis, filler):
    length = values.shape[along_axis]
    padding = jnp.full_like(slab_of(values, 0, stride, along_axis), filler)
    return jnp.concatenate([padding, slab_of(values, 0, length - stride, along_axis)], along_axis)


def from_above(values, stride, along_axis, filler):
    length = values.shape[along_axis]
    padding = jnp.full_like(slab_of(values, 0, stride, along_axis), filler)
    return jnp.concatenate([slab_of(values, stride, length, along_axis), padding], along_axis)


def reduction_kernel(lower_ref, main_ref, upper_ref, rights_ref, out_ref, *, along_axis):
    lower_band, main_band, upper_band = lower_ref[...], main_ref[...], upper_ref[...]
    rights = rights_ref[...]
    length = rights.shape[along_axis]
    position = lax.broadcasted_iota(jnp.int32, rights.shape, along_axis)
    stride = 1
    for _ in range(PCR_STEPS):
        def from_lower(values, fill):
            return jnp.where(position >= stride, pltpu.roll(values, stride, along_axis), fill)

        def from_upper(values, fill):
            return jnp.where(
                position < length - stride, pltpu.roll(values, length - stride, along_axis), fill
            )

        below = [from_lower(band, fill) for band, fill in
                 ((lower_band, 0.0), (main_band, 1.0), (upper_band, 0.0), (rights, 0.0))]
        above = [from_upper(band, fill) for band, fill in
                 ((lower_band, 0.0), (main_band, 1.0), (upper_band, 0.0), (rights, 0.0))]
        weight_below = lower_band / below[1]
        weight_above = upper_band / above[1]
        new_lower = -weight_below * below[0]
        new_main = main_band - weight_below * below[2] - weight_above * above[0]
        new_upper = -weight_above * above[2]
        rights = rights - weight_below * below[3] - weight_above * above[3]
        lower_band, main_band, upper_band = new_lower, new_main, new_upper
        stride = stride * 2
    out_ref[...] = rights / main_band


def padded(values, shape, fill):
    return jnp.pad(
        values, [(0, want - have) for want, have in zip(shape, values.shape)], constant_values=fill
    )


def line_solve(bands, rights, along_axis):
    lower_band, main_band, upper_band = bands
    shape = main_band.shape
    count = rights.shape
    spec = pl.BlockSpec(memory_space=pltpu.VMEM)
    solved = pl.pallas_call(
        lambda *refs: reduction_kernel(*refs, along_axis=along_axis),
        out_shape=jax.ShapeDtypeStruct(shape, jnp.float32),
        in_specs=[spec] * 4,
        out_specs=spec,
        name="line_solve",
    )(lower_band, main_band, upper_band, padded(rights, shape, 0.0))
    return solved[: count[0], : count[1]]


def band_set(coef, keep):
    shape = tuple(-(-size // unit) * unit for size, unit in zip(coef.shape, (8, 128)))
    return (
        padded(jnp.where(keep, -coef, 0.0), shape, 0.0),
        padded(jnp.where(keep, 1.0 + 2.0 * coef, 1.0), shape, 1.0),
        padded(jnp.where(keep, -coef, 0.0), shape, 0.0),
    )


def moved(block, lat_step, lon_step):
    lat_count = lax.axis_size("lat")
    lon_count = lax.axis_size("lon")
    pairs = [
        (lon * lat_count + lat, ((lon + lon_step) % lon_count) * lat_count + lat + lat_step)
        for lon in range(lon_count)
        for lat in range(lat_count)
        if 0 <= lat + lat_step < lat_count
    ]
    return lax.ppermute(block, ("lon", "lat"), pairs)


def halo_box(fields, wide_x, wide_y, place, count):
    west = moved(fields[:, :, -wide_x:], 0, 1)
    east = moved(fields[:, :, :wide_x], 0, -1)
    above = moved(fields[:, -wide_y:], 1, 0)
    below = moved(fields[:, :wide_y], -1, 0)
    above_west = moved(fields[:, -wide_y:, -wide_x:], 1, 1)
    above_east = moved(fields[:, -wide_y:, :wide_x], 1, -1)
    below_west = moved(fields[:, :wide_y, -wide_x:], -1, 1)
    below_east = moved(fields[:, :wide_y, :wide_x], -1, -1)
    wide = jnp.concatenate([west, fields, east], axis=2)
    top = jnp.concatenate([above_west, above, above_east], axis=2)
    bottom = jnp.concatenate([below_west, below, below_east], axis=2)
    top = jnp.where(place == 0, wide[:, wide_y - 1 :: -1], top)
    bottom = jnp.where(place == count - 1, wide[:, : -wide_y - 1 : -1], bottom)
    return jnp.concatenate([top, wide, bottom], axis=1)


def local(surface, momentum_x, momentum_y, water_depth, wet_mask, slide_cells, slide_rate):
    wet_float = wet_mask.astype(jnp.float32)
    place = lax.axis_index("lat")
    count = lax.axis_size("lat")
    tile_rows, tile_cols = surface.shape
    wide_x = WINDOW_LON + 2
    wide_y = WINDOW_LAT + 2
    lift = (
        jnp.zeros((tile_rows * tile_cols,), jnp.float32)
        .at[slide_cells.reshape(-1)]
        .add(slide_rate.reshape(-1))
        .reshape(tile_rows, tile_cols)
    )
    box_rows = tile_rows + 2 * wide_y
    box_cols = tile_cols + 2 * wide_x
    core_rows = slice(wide_y - 2, wide_y + tile_rows + 2)
    core_cols = slice(wide_x - 2, wide_x + tile_cols + 2)
    global_row = place * tile_rows - wide_y + lax.broadcasted_iota(
        jnp.int32, (box_rows, tile_cols + 4), 0
    )
    inside = (global_row >= 0) & (global_row < count * tile_rows)

    initial = (surface, momentum_x, momentum_y)
    current = initial
    velocity_u = surface
    velocity_v = surface
    bands = None
    for first, second in ((0.0, 1.0), (0.75, 0.25), (1.0 / 3.0, 2.0 / 3.0)):
        if bands is None:
            box = halo_box(
                jnp.stack([current[0], current[1], current[2], water_depth, wet_float]),
                wide_x, wide_y, place, count,
            )
            depth_box, wet_box = box[3], box[4]
            coef_lon = depth_box[core_rows] * depth_box[core_rows] / (3.0 * LON_SPACING * LON_SPACING)
            coef_lat = depth_box[:, core_cols] * depth_box[:, core_cols] / (3.0 * LAT_SPACING * LAT_SPACING)
            bands = (band_set(coef_lon, True), band_set(coef_lat, inside))
        else:
            box = halo_box(jnp.stack(list(current)), wide_x, wide_y, place, count)
        surface_box, east_box, north_box = box[0], box[1], box[2]
        height_box = depth_box + surface_box
        east_raw = line_solve(bands[0], east_box[core_rows] / height_box[core_rows], 1)[:, core_cols]
        north_rights = jnp.where(inside, north_box[:, core_cols] / height_box[:, core_cols], 0.0)
        north_raw = line_solve(bands[1], north_rights, 0)[core_rows]
        wet_core = wet_box[core_rows, core_cols]
        u_core = wet_core * east_raw
        v_core = wet_core * north_raw
        v_core = jnp.where(place == 0, jnp.concatenate([-v_core[3:1:-1], v_core[2:]], axis=0), v_core)
        v_core = jnp.where(
            place == count - 1, jnp.concatenate([v_core[:-2], -v_core[-3:-5:-1]], axis=0), v_core
        )
        fields = jnp.stack(
            [surface_box[core_rows, core_cols], u_core, v_core, depth_box[core_rows, core_cols], wet_core]
        )
        across = fields[:, 2:-2, :]
        along = fields[:, :, 2:-2]
        rate_surface, rate_east, rate_north = tendencies(across, along)
        rates = (rate_surface + lift, rate_east, rate_north)
        velocity_u = u_core[2:-2, 2:-2]
        velocity_v = v_core[2:-2, 2:-2]
        current = tuple(
            (
                first * start_value + second * (now + TIME_STEP * rate)
                for start_value, now, rate in zip(initial, current, rates)
            )
        )
    return (current[0], current[1], current[2], velocity_u, velocity_v)


def solution(mesh):
    in_specs = (P("lat", "lon"),) * 7
    out_specs = (P("lat", "lon"),) * 5
    return jax.shard_map(local, mesh=mesh, in_specs=in_specs, out_specs=out_specs, check_vma=False)
```

```python
import jax
import jax.numpy as jnp
from jax import lax
from jax.sharding import PartitionSpec as P
from jax.experimental import pallas as pl
from jax.experimental.pallas import tpu as pltpu

GRAVITY = 1.0
LON_SPACING = 0.5
LAT_SPACING = 0.6
TIME_STEP = 0.1
WINDOW_LON = 40
WINDOW_LAT = 32
PCR_STEPS = 6


def shifted(block, axis, distance):
    devices = range(lax.axis_size(axis))
    route = [((i - distance) % len(devices), i) for i in devices]
    return lax.ppermute(block, axis, route)


def passed_along(x, axis, by):
    peers = lax.axis_size(axis)
    pairs = [(i, i + by) for i in range(peers) if 0 <= i + by < peers]
    return lax.ppermute(x, axis, pairs)


def extended(cells, sides, width, closed):
    for axis, dim in sides:
        count = lax.axis_size(axis)
        ends = count if closed else count - 1
        head = lax.slice_in_dim(cells, 0, width, axis=dim)
        tail = lax.slice_in_dim(cells, cells.shape[dim] - width, cells.shape[dim], axis=dim)
        cells = jnp.concatenate(
            [
                lax.ppermute(tail, axis, [(i, (i + 1) % count) for i in range(ends)]),
                cells,
                lax.ppermute(head, axis, [((i + 1) % count, i) for i in range(ends)]),
            ],
            axis=dim,
        )
    return cells


def slab_of(values, start, stop, along_axis):
    return lax.slice_in_dim(values, start, stop, axis=along_axis)


def limited(former, latter):
    return jnp.maximum(jnp.minimum(former, latter), 0.0) + jnp.minimum(
        jnp.maximum(former, latter), 0.0
    )


def face_states(values, along_axis):
    length = values.shape[along_axis]
    jumps = slab_of(values, 1, length, along_axis) - slab_of(values, 0, length - 1, along_axis)
    slopes = limited(
        slab_of(jumps, 0, length - 2, along_axis), slab_of(jumps, 1, length - 1, along_axis)
    )
    left_state = slab_of(values, 1, length - 2, along_axis) + 0.5 * slab_of(
        slopes, 0, length - 3, along_axis
    )
    right_state = slab_of(values, 2, length - 1, along_axis) - 0.5 * slab_of(
        slopes, 1, length - 2, along_axis
    )
    return (left_state, right_state)


def wave_flux(
    surface_left,
    surface_right,
    normal_left,
    normal_right,
    tangent_left,
    tangent_right,
    face_depth,
    opened,
):
    height_left = surface_left + face_depth
    height_right = surface_right + face_depth
    celerity_left = jnp.sqrt(GRAVITY * height_left)
    celerity_right = jnp.sqrt(GRAVITY * height_right)
    slowest = jnp.minimum(
        jnp.minimum(normal_left - celerity_left, normal_right - celerity_right), 0.0
    )
    fastest = jnp.maximum(
        jnp.maximum(normal_left + celerity_left, normal_right + celerity_right), 0.0
    )
    spread = fastest - slowest
    product = slowest * fastest
    mass_left = height_left * normal_left
    mass_right = height_right * normal_right
    push_left = mass_left * normal_left + GRAVITY * (
        0.5 * surface_left * surface_left + face_depth * surface_left
    )
    push_right = mass_right * normal_right + GRAVITY * (
        0.5 * surface_right * surface_right + face_depth * surface_right
    )
    carry_left = mass_left * tangent_left
    carry_right = mass_right * tangent_right
    mass_flux = (
        opened
        * (fastest * mass_left - slowest * mass_right + product * (surface_right - surface_left))
        / spread
    )
    push_flux = (
        opened
        * (fastest * push_left - slowest * push_right + product * (mass_right - mass_left))
        / spread
    )
    carry_flux = (
        opened
        * (
            fastest * carry_left
            - slowest * carry_right
            + product * (height_right * tangent_right - height_left * tangent_left)
        )
        / spread
    )
    return (mass_flux, push_flux, carry_flux)


def tendencies(across, along):
    width = across[0].shape[1] - 4
    row_count = along[0].shape[0] - 4
    surface_pair = face_states(across[0], 1)
    east_pair = face_states(across[1], 1)
    north_pair = face_states(across[2], 1)
    depth_lon = 0.5 * (across[3][:, 1 : width + 2] + across[3][:, 2 : width + 3])
    open_lon = across[4][:, 1 : width + 2] * across[4][:, 2 : width + 3]
    mass_lon, push_lon, carry_lon = wave_flux(
        surface_pair[0],
        surface_pair[1],
        east_pair[0],
        east_pair[1],
        north_pair[0],
        north_pair[1],
        depth_lon,
        open_lon,
    )
    surface_pair = face_states(along[0], 0)
    east_pair = face_states(along[1], 0)
    north_pair = face_states(along[2], 0)
    depth_lat = 0.5 * (along[3][1 : row_count + 2] + along[3][2 : row_count + 3])
    open_lat = along[4][1 : row_count + 2] * along[4][2 : row_count + 3]
    mass_lat, push_lat, carry_lat = wave_flux(
        surface_pair[0],
        surface_pair[1],
        north_pair[0],
        north_pair[1],
        east_pair[0],
        east_pair[1],
        depth_lat,
        open_lat,
    )
    surface_mid = across[0][:, 2 : width + 2]
    wet_mid = across[4][:, 2 : width + 2]
    rate_surface = (
        -(mass_lon[:, 1:] - mass_lon[:, :-1]) / LON_SPACING
        - (mass_lat[1:] - mass_lat[:-1]) / LAT_SPACING
    )
    source_east = GRAVITY * surface_mid * (depth_lon[:, 1:] - depth_lon[:, :-1]) / LON_SPACING
    source_north = GRAVITY * surface_mid * (depth_lat[1:] - depth_lat[:-1]) / LAT_SPACING
    rate_east = wet_mid * (
        source_east
        - (push_lon[:, 1:] - push_lon[:, :-1]) / LON_SPACING
        - (carry_lat[1:] - carry_lat[:-1]) / LAT_SPACING
    )
    rate_north = wet_mid * (
        source_north
        - (carry_lon[:, 1:] - carry_lon[:, :-1]) / LON_SPACING
        - (push_lat[1:] - push_lat[:-1]) / LAT_SPACING
    )
    return (rate_surface, rate_east, rate_north)


def from_below(values, stride, along_axis, filler):
    length = values.shape[along_axis]
    padding = jnp.full_like(slab_of(values, 0, stride, along_axis), filler)
    return jnp.concatenate([padding, slab_of(values, 0, length - stride, along_axis)], along_axis)


def from_above(values, stride, along_axis, filler):
    length = values.shape[along_axis]
    padding = jnp.full_like(slab_of(values, 0, stride, along_axis), filler)
    return jnp.concatenate([slab_of(values, stride, length, along_axis), padding], along_axis)


def reduce_lines(lower_band, main_band, upper_band, rights, along_axis):
    length = rights.shape[along_axis]
    position = lax.broadcasted_iota(jnp.int32, rights.shape, along_axis)
    stride = 1
    for _ in range(PCR_STEPS):
        def from_lower(values, fill):
            return jnp.where(position >= stride, pltpu.roll(values, stride, along_axis), fill)

        def from_upper(values, fill):
            return jnp.where(
                position < length - stride, pltpu.roll(values, length - stride, along_axis), fill
            )

        below = [from_lower(band, fill) for band, fill in
                 ((lower_band, 0.0), (main_band, 1.0), (upper_band, 0.0), (rights, 0.0))]
        above = [from_upper(band, fill) for band, fill in
                 ((lower_band, 0.0), (main_band, 1.0), (upper_band, 0.0), (rights, 0.0))]
        weight_below = lower_band / below[1]
        weight_above = upper_band / above[1]
        new_lower = -weight_below * below[0]
        new_main = main_band - weight_below * below[2] - weight_above * above[0]
        new_upper = -weight_above * above[2]
        rights = rights - weight_below * below[3] - weight_above * above[3]
        lower_band, main_band, upper_band = new_lower, new_main, new_upper
        stride = stride * 2
    return rights / main_band


def solve_kernel(surface_ref, east_ref, north_ref, depth_ref, keep_ref, east_out, north_out, *,
                 first_row, used_cols):
    rows = east_out.shape[0]
    depth = depth_ref[pl.ds(first_row, rows), :]
    coef = depth * depth / (3.0 * LON_SPACING * LON_SPACING)
    keep = lax.broadcasted_iota(jnp.int32, depth.shape, 1) < used_cols
    rights = east_ref[pl.ds(first_row, rows), :] / (depth + surface_ref[pl.ds(first_row, rows), :])
    east_out[...] = reduce_lines(
        jnp.where(keep, -coef, 0.0),
        jnp.where(keep, 1.0 + 2.0 * coef, 1.0),
        jnp.where(keep, -coef, 0.0),
        jnp.where(keep, rights, 0.0),
        1,
    )
    depth = depth_ref[...]
    coef = depth * depth / (3.0 * LAT_SPACING * LAT_SPACING)
    keep = keep_ref[...] > 0.0
    rights = north_ref[...] / (depth + surface_ref[...])
    north_out[...] = reduce_lines(
        jnp.where(keep, -coef, 0.0),
        jnp.where(keep, 1.0 + 2.0 * coef, 1.0),
        jnp.where(keep, -coef, 0.0),
        jnp.where(keep, rights, 0.0),
        0,
    )


def line_solves(box, depth_box, keep, first_row, rows, used_cols):
    spec = pl.BlockSpec(memory_space=pltpu.VMEM)
    return pl.pallas_call(
        lambda *refs: solve_kernel(*refs, first_row=first_row, used_cols=used_cols),
        out_shape=(
            jax.ShapeDtypeStruct((rows, depth_box.shape[1]), jnp.float32),
            jax.ShapeDtypeStruct(depth_box.shape, jnp.float32),
        ),
        in_specs=[spec] * 5,
        out_specs=(spec, spec),
        name="line_solves",
    )(box[0], box[1], box[2], depth_box, keep)


def halo_box(fields, wide_x, wide_y, place, count):
    lon_count = lax.axis_size("lon")
    west = lax.ppermute(
        fields[:, :, -wide_x:], "lon", [(i, (i + 1) % lon_count) for i in range(lon_count)]
    )
    east = lax.ppermute(
        fields[:, :, :wide_x], "lon", [((i + 1) % lon_count, i) for i in range(lon_count)]
    )
    wide = jnp.concatenate([west, fields, east], axis=2)
    above = passed_along(wide[:, -wide_y:], "lat", 1)
    below = passed_along(wide[:, :wide_y], "lat", -1)
    above = jnp.where(place == 0, wide[:, wide_y - 1 :: -1], above)
    below = jnp.where(place == count - 1, wide[:, : -wide_y - 1 : -1], below)
    box = jnp.concatenate([above, wide, below], axis=1)
    aligned = [-(-size // unit) * unit for size, unit in zip(box.shape[1:], (8, 128))]
    return jnp.pad(box, ((0, 0), (0, aligned[0] - box.shape[1]), (0, aligned[1] - box.shape[2])))


def local(surface, momentum_x, momentum_y, water_depth, wet_mask, slide_cells, slide_rate):
    wet_float = wet_mask.astype(jnp.float32)
    place = lax.axis_index("lat")
    count = lax.axis_size("lat")
    tile_rows, tile_cols = surface.shape
    wide_x = WINDOW_LON + 2
    wide_y = WINDOW_LAT + 2
    lift = (
        jnp.zeros((tile_rows * tile_cols,), jnp.float32)
        .at[slide_cells.reshape(-1)]
        .add(slide_rate.reshape(-1))
        .reshape(tile_rows, tile_cols)
    )
    box_rows = tile_rows + 2 * wide_y
    box_cols = tile_cols + 2 * wide_x
    core_rows = slice(wide_y - 2, wide_y + tile_rows + 2)
    core_cols = slice(wide_x - 2, wide_x + tile_cols + 2)
    aligned_rows = -(-box_rows // 8) * 8
    aligned_cols = -(-box_cols // 128) * 128
    global_row = place * tile_rows - wide_y + lax.broadcasted_iota(
        jnp.int32, (aligned_rows, aligned_cols), 0
    )
    inside = (global_row >= 0) & (global_row < count * tile_rows) & (global_row < place * tile_rows - wide_y + box_rows)
    keep = inside.astype(jnp.float32)
    first_row = (wide_y - 2) // 8 * 8
    east_rows = -(-(wide_y + tile_rows + 2 - first_row) // 8) * 8

    initial = (surface, momentum_x, momentum_y)
    current = initial
    velocity_u = surface
    velocity_v = surface
    depth_box = None
    for first, second in ((0.0, 1.0), (0.75, 0.25), (1.0 / 3.0, 2.0 / 3.0)):
        if depth_box is None:
            box = halo_box(
                jnp.stack([current[0], current[1], current[2], water_depth, wet_float]),
                wide_x, wide_y, place, count,
            )
            depth_box, wet_box = box[3], box[4]
        else:
            box = halo_box(jnp.stack(list(current)), wide_x, wide_y, place, count)
        surface_box, east_box, north_box = box[0], box[1], box[2]
        east_solved, north_solved = line_solves(box, depth_box, keep, first_row, east_rows, box_cols)
        east_raw = east_solved[core_rows.start - first_row : core_rows.stop - first_row, core_cols]
        north_raw = north_solved[core_rows, core_cols]
        wet_core = wet_box[core_rows, core_cols]
        u_core = wet_core * east_raw
        v_core = wet_core * north_raw
        v_core = jnp.where(place == 0, jnp.concatenate([-v_core[3:1:-1], v_core[2:]], axis=0), v_core)
        v_core = jnp.where(
            place == count - 1, jnp.concatenate([v_core[:-2], -v_core[-3:-5:-1]], axis=0), v_core
        )
        fields = jnp.stack(
            [surface_box[core_rows, core_cols], u_core, v_core, depth_box[core_rows, core_cols], wet_core]
        )
        across = fields[:, 2:-2, :]
        along = fields[:, :, 2:-2]
        rate_surface, rate_east, rate_north = tendencies(across, along)
        rates = (rate_surface + lift, rate_east, rate_north)
        velocity_u = u_core[2:-2, 2:-2]
        velocity_v = v_core[2:-2, 2:-2]
        current = tuple(
            (
                first * start_value + second * (now + TIME_STEP * rate)
                for start_value, now, rate in zip(initial, current, rates)
            )
        )
    return (current[0], current[1], current[2], velocity_u, velocity_v)


def solution(mesh):
    in_specs = (P("lat", "lon"),) * 7
    out_specs = (P("lat", "lon"),) * 5
    return jax.shard_map(local, mesh=mesh, in_specs=in_specs, out_specs=out_specs, check_vma=False)
```

```python
import jax
import jax.numpy as jnp
from jax import lax
from jax.sharding import PartitionSpec as P
from jax.experimental import pallas as pl
from jax.experimental.pallas import tpu as pltpu

GRAVITY = 1.0
LON_SPACING = 0.5
LAT_SPACING = 0.6
TIME_STEP = 0.1
WINDOW_LON = 40
WINDOW_LAT = 32
PCR_STEPS = 6


def shifted(block, axis, distance):
    devices = range(lax.axis_size(axis))
    route = [((i - distance) % len(devices), i) for i in devices]
    return lax.ppermute(block, axis, route)


def passed_along(x, axis, by):
    peers = lax.axis_size(axis)
    pairs = [(i, i + by) for i in range(peers) if 0 <= i + by < peers]
    return lax.ppermute(x, axis, pairs)


def extended(cells, sides, width, closed):
    for axis, dim in sides:
        count = lax.axis_size(axis)
        ends = count if closed else count - 1
        head = lax.slice_in_dim(cells, 0, width, axis=dim)
        tail = lax.slice_in_dim(cells, cells.shape[dim] - width, cells.shape[dim], axis=dim)
        cells = jnp.concatenate(
            [
                lax.ppermute(tail, axis, [(i, (i + 1) % count) for i in range(ends)]),
                cells,
                lax.ppermute(head, axis, [((i + 1) % count, i) for i in range(ends)]),
            ],
            axis=dim,
        )
    return cells


def slab_of(values, start, stop, along_axis):
    return lax.slice_in_dim(values, start, stop, axis=along_axis)


def limited(former, latter):
    return jnp.maximum(jnp.minimum(former, latter), 0.0) + jnp.minimum(
        jnp.maximum(former, latter), 0.0
    )


def face_states(values, along_axis):
    length = values.shape[along_axis]
    jumps = slab_of(values, 1, length, along_axis) - slab_of(values, 0, length - 1, along_axis)
    slopes = limited(
        slab_of(jumps, 0, length - 2, along_axis), slab_of(jumps, 1, length - 1, along_axis)
    )
    left_state = slab_of(values, 1, length - 2, along_axis) + 0.5 * slab_of(
        slopes, 0, length - 3, along_axis
    )
    right_state = slab_of(values, 2, length - 1, along_axis) - 0.5 * slab_of(
        slopes, 1, length - 2, along_axis
    )
    return (left_state, right_state)


def wave_flux(
    surface_left,
    surface_right,
    normal_left,
    normal_right,
    tangent_left,
    tangent_right,
    face_depth,
    opened,
):
    height_left = surface_left + face_depth
    height_right = surface_right + face_depth
    celerity_left = jnp.sqrt(GRAVITY * height_left)
    celerity_right = jnp.sqrt(GRAVITY * height_right)
    slowest = jnp.minimum(
        jnp.minimum(normal_left - celerity_left, normal_right - celerity_right), 0.0
    )
    fastest = jnp.maximum(
        jnp.maximum(normal_left + celerity_left, normal_right + celerity_right), 0.0
    )
    spread = fastest - slowest
    product = slowest * fastest
    mass_left = height_left * normal_left
    mass_right = height_right * normal_right
    push_left = mass_left * normal_left + GRAVITY * (
        0.5 * surface_left * surface_left + face_depth * surface_left
    )
    push_right = mass_right * normal_right + GRAVITY * (
        0.5 * surface_right * surface_right + face_depth * surface_right
    )
    carry_left = mass_left * tangent_left
    carry_right = mass_right * tangent_right
    mass_flux = (
        opened
        * (fastest * mass_left - slowest * mass_right + product * (surface_right - surface_left))
        / spread
    )
    push_flux = (
        opened
        * (fastest * push_left - slowest * push_right + product * (mass_right - mass_left))
        / spread
    )
    carry_flux = (
        opened
        * (
            fastest * carry_left
            - slowest * carry_right
            + product * (height_right * tangent_right - height_left * tangent_left)
        )
        / spread
    )
    return (mass_flux, push_flux, carry_flux)


def tendencies(across, along):
    width = across[0].shape[1] - 4
    row_count = along[0].shape[0] - 4
    surface_pair = face_states(across[0], 1)
    east_pair = face_states(across[1], 1)
    north_pair = face_states(across[2], 1)
    depth_lon = 0.5 * (across[3][:, 1 : width + 2] + across[3][:, 2 : width + 3])
    open_lon = across[4][:, 1 : width + 2] * across[4][:, 2 : width + 3]
    mass_lon, push_lon, carry_lon = wave_flux(
        surface_pair[0],
        surface_pair[1],
        east_pair[0],
        east_pair[1],
        north_pair[0],
        north_pair[1],
        depth_lon,
        open_lon,
    )
    surface_pair = face_states(along[0], 0)
    east_pair = face_states(along[1], 0)
    north_pair = face_states(along[2], 0)
    depth_lat = 0.5 * (along[3][1 : row_count + 2] + along[3][2 : row_count + 3])
    open_lat = along[4][1 : row_count + 2] * along[4][2 : row_count + 3]
    mass_lat, push_lat, carry_lat = wave_flux(
        surface_pair[0],
        surface_pair[1],
        north_pair[0],
        north_pair[1],
        east_pair[0],
        east_pair[1],
        depth_lat,
        open_lat,
    )
    surface_mid = across[0][:, 2 : width + 2]
    wet_mid = across[4][:, 2 : width + 2]
    rate_surface = (
        -(mass_lon[:, 1:] - mass_lon[:, :-1]) / LON_SPACING
        - (mass_lat[1:] - mass_lat[:-1]) / LAT_SPACING
    )
    source_east = GRAVITY * surface_mid * (depth_lon[:, 1:] - depth_lon[:, :-1]) / LON_SPACING
    source_north = GRAVITY * surface_mid * (depth_lat[1:] - depth_lat[:-1]) / LAT_SPACING
    rate_east = wet_mid * (
        source_east
        - (push_lon[:, 1:] - push_lon[:, :-1]) / LON_SPACING
        - (carry_lat[1:] - carry_lat[:-1]) / LAT_SPACING
    )
    rate_north = wet_mid * (
        source_north
        - (carry_lon[:, 1:] - carry_lon[:, :-1]) / LON_SPACING
        - (push_lat[1:] - push_lat[:-1]) / LAT_SPACING
    )
    return (rate_surface, rate_east, rate_north)


def from_below(values, stride, along_axis, filler):
    length = values.shape[along_axis]
    padding = jnp.full_like(slab_of(values, 0, stride, along_axis), filler)
    return jnp.concatenate([padding, slab_of(values, 0, length - stride, along_axis)], along_axis)


def from_above(values, stride, along_axis, filler):
    length = values.shape[along_axis]
    padding = jnp.full_like(slab_of(values, 0, stride, along_axis), filler)
    return jnp.concatenate([slab_of(values, stride, length, along_axis), padding], along_axis)


def reduce_lines(lower_band, main_band, upper_band, rights, along_axis):
    length = rights.shape[along_axis]
    position = lax.broadcasted_iota(jnp.int32, rights.shape, along_axis)
    stride = 1
    for _ in range(PCR_STEPS):
        def from_lower(values, fill):
            return jnp.where(position >= stride, pltpu.roll(values, stride, along_axis), fill)

        def from_upper(values, fill):
            return jnp.where(
                position < length - stride, pltpu.roll(values, length - stride, along_axis), fill
            )

        below = [from_lower(band, fill) for band, fill in
                 ((lower_band, 0.0), (main_band, 1.0), (upper_band, 0.0), (rights, 0.0))]
        above = [from_upper(band, fill) for band, fill in
                 ((lower_band, 0.0), (main_band, 1.0), (upper_band, 0.0), (rights, 0.0))]
        weight_below = lower_band / below[1]
        weight_above = upper_band / above[1]
        new_lower = -weight_below * below[0]
        new_main = main_band - weight_below * below[2] - weight_above * above[0]
        new_upper = -weight_above * above[2]
        rights = rights - weight_below * below[3] - weight_above * above[3]
        lower_band, main_band, upper_band = new_lower, new_main, new_upper
        stride = stride * 2
    return rights / main_band


def section_kernel(surface_ref, east_ref, north_ref, depth_ref, wet_ref, keep_ref, mirror_ref,
                   rate_surface_out, rate_east_out, rate_north_out, east_out, north_out, *,
                   first_row, used_cols, tile_offset):
    rows, cols = rate_surface_out.shape
    depth = depth_ref[pl.ds(first_row, rows), :]
    surface = surface_ref[pl.ds(first_row, rows), :]
    coef = depth * depth / (3.0 * LON_SPACING * LON_SPACING)
    keep = lax.broadcasted_iota(jnp.int32, depth.shape, 1) < used_cols
    rights = east_ref[pl.ds(first_row, rows), :] / (depth + surface)
    east_raw = reduce_lines(
        jnp.where(keep, -coef, 0.0),
        jnp.where(keep, 1.0 + 2.0 * coef, 1.0),
        jnp.where(keep, -coef, 0.0),
        jnp.where(keep, rights, 0.0),
        1,
    )
    full_depth = depth_ref[...]
    coef = full_depth * full_depth / (3.0 * LAT_SPACING * LAT_SPACING)
    keep = keep_ref[...] > 0.0
    rights = north_ref[...] / (full_depth + surface_ref[...])
    north_raw = reduce_lines(
        jnp.where(keep, -coef, 0.0),
        jnp.where(keep, 1.0 + 2.0 * coef, 1.0),
        jnp.where(keep, -coef, 0.0),
        jnp.where(keep, rights, 0.0),
        0,
    )[first_row : first_row + rows]

    def wrapped(values):
        values = pltpu.roll(values, rows - (tile_offset[0] - first_row), 0)
        return pltpu.roll(values, cols - tile_offset[1], 1)

    wet = wrapped(wet_ref[pl.ds(first_row, rows), :])
    surface = wrapped(surface)
    depth = wrapped(depth)
    velocity_u = wet * wrapped(east_raw)
    velocity_v = wet * wrapped(north_raw)
    mirror = mirror_ref[...]
    for code, shift in ((1, rows - 1), (2, rows - 3), (3, 1), (4, 3)):
        velocity_v = jnp.where(mirror == code, -pltpu.roll(velocity_v, shift, 0), velocity_v)

    def east_of(values):
        return pltpu.roll(values, cols - 1, 1)

    def west_of(values):
        return pltpu.roll(values, 1, 1)

    def north_of(values):
        return pltpu.roll(values, rows - 1, 0)

    def south_of(values):
        return pltpu.roll(values, 1, 0)

    def face_pair(values, later, earlier):
        jump = later(values) - values
        slope = limited(earlier(jump), jump)
        return values + 0.5 * slope, later(values - 0.5 * slope)

    surface_pair = face_pair(surface, east_of, west_of)
    east_pair = face_pair(velocity_u, east_of, west_of)
    north_pair = face_pair(velocity_v, east_of, west_of)
    depth_lon = 0.5 * (depth + east_of(depth))
    open_lon = wet * east_of(wet)
    mass_lon, push_lon, carry_lon = wave_flux(
        surface_pair[0], surface_pair[1], east_pair[0], east_pair[1],
        north_pair[0], north_pair[1], depth_lon, open_lon,
    )
    surface_pair = face_pair(surface, north_of, south_of)
    east_pair = face_pair(velocity_u, north_of, south_of)
    north_pair = face_pair(velocity_v, north_of, south_of)
    depth_lat = 0.5 * (depth + north_of(depth))
    open_lat = wet * north_of(wet)
    mass_lat, push_lat, carry_lat = wave_flux(
        surface_pair[0], surface_pair[1], north_pair[0], north_pair[1],
        east_pair[0], east_pair[1], depth_lat, open_lat,
    )
    rate_surface_out[...] = (
        -(mass_lon - west_of(mass_lon)) / LON_SPACING - (mass_lat - south_of(mass_lat)) / LAT_SPACING
    )
    source_east = GRAVITY * surface * (depth_lon - west_of(depth_lon)) / LON_SPACING
    source_north = GRAVITY * surface * (depth_lat - south_of(depth_lat)) / LAT_SPACING
    rate_east_out[...] = wet * (
        source_east
        - (push_lon - west_of(push_lon)) / LON_SPACING
        - (carry_lat - south_of(carry_lat)) / LAT_SPACING
    )
    rate_north_out[...] = wet * (
        source_north
        - (carry_lon - west_of(carry_lon)) / LON_SPACING
        - (push_lat - south_of(push_lat)) / LAT_SPACING
    )
    east_out[...] = velocity_u
    north_out[...] = velocity_v


def section_rates(box, keep, mirror, first_row, used_cols, tile_offset):
    spec = pl.BlockSpec(memory_space=pltpu.VMEM)
    shape = jax.ShapeDtypeStruct(mirror.shape, jnp.float32)
    return pl.pallas_call(
        lambda *refs: section_kernel(
            *refs, first_row=first_row, used_cols=used_cols, tile_offset=tile_offset
        ),
        out_shape=(shape,) * 5,
        in_specs=[spec] * 7,
        out_specs=(spec,) * 5,
        name="section_rates",
    )(box[0], box[1], box[2], box[3], box[4], keep, mirror)


def halo_box(fields, wide_x, wide_y, place, count):
    lon_count = lax.axis_size("lon")
    west = lax.ppermute(
        fields[:, :, -wide_x:], "lon", [(i, (i + 1) % lon_count) for i in range(lon_count)]
    )
    east = lax.ppermute(
        fields[:, :, :wide_x], "lon", [((i + 1) % lon_count, i) for i in range(lon_count)]
    )
    wide = jnp.concatenate([west, fields, east], axis=2)
    above = passed_along(wide[:, -wide_y:], "lat", 1)
    below = passed_along(wide[:, :wide_y], "lat", -1)
    above = jnp.where(place == 0, wide[:, wide_y - 1 :: -1], above)
    below = jnp.where(place == count - 1, wide[:, : -wide_y - 1 : -1], below)
    box = jnp.concatenate([above, wide, below], axis=1)
    aligned = [-(-size // unit) * unit for size, unit in zip(box.shape[1:], (8, 128))]
    return jnp.pad(box, ((0, 0), (0, aligned[0] - box.shape[1]), (0, aligned[1] - box.shape[2])))


def local(surface, momentum_x, momentum_y, water_depth, wet_mask, slide_cells, slide_rate):
    wet_float = wet_mask.astype(jnp.float32)
    place = lax.axis_index("lat")
    count = lax.axis_size("lat")
    tile_rows, tile_cols = surface.shape
    wide_x = WINDOW_LON + 2
    wide_y = WINDOW_LAT + 2
    lift = (
        jnp.zeros((tile_rows * tile_cols,), jnp.float32)
        .at[slide_cells.reshape(-1)]
        .add(slide_rate.reshape(-1))
        .reshape(tile_rows, tile_cols)
    )
    box_rows = tile_rows + 2 * wide_y
    box_cols = tile_cols + 2 * wide_x
    core_rows = slice(wide_y - 2, wide_y + tile_rows + 2)
    core_cols = slice(wide_x - 2, wide_x + tile_cols + 2)
    aligned_rows = -(-box_rows // 8) * 8
    aligned_cols = -(-box_cols // 128) * 128
    global_row = place * tile_rows - wide_y + lax.broadcasted_iota(
        jnp.int32, (aligned_rows, aligned_cols), 0
    )
    inside = (global_row >= 0) & (global_row < count * tile_rows) & (global_row < place * tile_rows - wide_y + box_rows)
    keep = inside.astype(jnp.float32)
    first_row = (wide_y - 2) // 8 * 8
    east_rows = -(-(wide_y + tile_rows + 2 - first_row) // 8) * 8
    wrapped_row = lax.broadcasted_iota(jnp.int32, (east_rows, aligned_cols), 0)
    top = place == 0
    bottom = place == count - 1
    mirror = jnp.where(
        top & (wrapped_row == east_rows - 1), 1,
        jnp.where(top & (wrapped_row == east_rows - 2), 2,
        jnp.where(bottom & (wrapped_row == tile_rows), 3,
        jnp.where(bottom & (wrapped_row == tile_rows + 1), 4, 0))),
    ).astype(jnp.int32)

    initial = (surface, momentum_x, momentum_y)
    current = initial
    velocity_u = surface
    velocity_v = surface
    depth_box = None
    for first, second in ((0.0, 1.0), (0.75, 0.25), (1.0 / 3.0, 2.0 / 3.0)):
        if depth_box is None:
            box = halo_box(
                jnp.stack([current[0], current[1], current[2], water_depth, wet_float]),
                wide_x, wide_y, place, count,
            )
            depth_box, wet_box = box[3], box[4]
        else:
            box = halo_box(jnp.stack(list(current)), wide_x, wide_y, place, count)
        rate_surface, rate_east, rate_north, east_wrapped, north_wrapped = section_rates(
            (box[0], box[1], box[2], depth_box, wet_box), keep, mirror, first_row, box_cols,
            (wide_y, wide_x),
        )
        rates = (
            rate_surface[:tile_rows, :tile_cols] + lift,
            rate_east[:tile_rows, :tile_cols],
            rate_north[:tile_rows, :tile_cols],
        )
        velocity_u = east_wrapped[:tile_rows, :tile_cols]
        velocity_v = north_wrapped[:tile_rows, :tile_cols]
        current = tuple(
            (
                first * start_value + second * (now + TIME_STEP * rate)
                for start_value, now, rate in zip(initial, current, rates)
            )
        )
    return (current[0], current[1], current[2], velocity_u, velocity_v)


def solution(mesh):
    in_specs = (P("lat", "lon"),) * 7
    out_specs = (P("lat", "lon"),) * 5
    return jax.shard_map(local, mesh=mesh, in_specs=in_specs, out_specs=out_specs, check_vma=False)
```

```python
import jax
import jax.numpy as jnp
from jax import lax
from jax.sharding import PartitionSpec as P
from jax.experimental import pallas as pl
from jax.experimental.pallas import tpu as pltpu

GRAVITY = 1.0
LON_SPACING = 0.5
LAT_SPACING = 0.6
TIME_STEP = 0.1
WINDOW_LON = 40
WINDOW_LAT = 32
PCR_STEPS = 6


def shifted(block, axis, distance):
    devices = range(lax.axis_size(axis))
    route = [((i - distance) % len(devices), i) for i in devices]
    return lax.ppermute(block, axis, route)


def passed_along(x, axis, by):
    peers = lax.axis_size(axis)
    pairs = [(i, i + by) for i in range(peers) if 0 <= i + by < peers]
    return lax.ppermute(x, axis, pairs)


def extended(cells, sides, width, closed):
    for axis, dim in sides:
        count = lax.axis_size(axis)
        ends = count if closed else count - 1
        head = lax.slice_in_dim(cells, 0, width, axis=dim)
        tail = lax.slice_in_dim(cells, cells.shape[dim] - width, cells.shape[dim], axis=dim)
        cells = jnp.concatenate(
            [
                lax.ppermute(tail, axis, [(i, (i + 1) % count) for i in range(ends)]),
                cells,
                lax.ppermute(head, axis, [((i + 1) % count, i) for i in range(ends)]),
            ],
            axis=dim,
        )
    return cells


def slab_of(values, start, stop, along_axis):
    return lax.slice_in_dim(values, start, stop, axis=along_axis)


def limited(former, latter):
    return jnp.maximum(jnp.minimum(former, latter), 0.0) + jnp.minimum(
        jnp.maximum(former, latter), 0.0
    )


def face_states(values, along_axis):
    length = values.shape[along_axis]
    jumps = slab_of(values, 1, length, along_axis) - slab_of(values, 0, length - 1, along_axis)
    slopes = limited(
        slab_of(jumps, 0, length - 2, along_axis), slab_of(jumps, 1, length - 1, along_axis)
    )
    left_state = slab_of(values, 1, length - 2, along_axis) + 0.5 * slab_of(
        slopes, 0, length - 3, along_axis
    )
    right_state = slab_of(values, 2, length - 1, along_axis) - 0.5 * slab_of(
        slopes, 1, length - 2, along_axis
    )
    return (left_state, right_state)


def wave_flux(
    surface_left,
    surface_right,
    normal_left,
    normal_right,
    tangent_left,
    tangent_right,
    face_depth,
    opened,
):
    height_left = surface_left + face_depth
    height_right = surface_right + face_depth
    celerity_left = jnp.sqrt(GRAVITY * height_left)
    celerity_right = jnp.sqrt(GRAVITY * height_right)
    slowest = jnp.minimum(
        jnp.minimum(normal_left - celerity_left, normal_right - celerity_right), 0.0
    )
    fastest = jnp.maximum(
        jnp.maximum(normal_left + celerity_left, normal_right + celerity_right), 0.0
    )
    spread = fastest - slowest
    product = slowest * fastest
    mass_left = height_left * normal_left
    mass_right = height_right * normal_right
    push_left = mass_left * normal_left + GRAVITY * (
        0.5 * surface_left * surface_left + face_depth * surface_left
    )
    push_right = mass_right * normal_right + GRAVITY * (
        0.5 * surface_right * surface_right + face_depth * surface_right
    )
    carry_left = mass_left * tangent_left
    carry_right = mass_right * tangent_right
    mass_flux = (
        opened
        * (fastest * mass_left - slowest * mass_right + product * (surface_right - surface_left))
        / spread
    )
    push_flux = (
        opened
        * (fastest * push_left - slowest * push_right + product * (mass_right - mass_left))
        / spread
    )
    carry_flux = (
        opened
        * (
            fastest * carry_left
            - slowest * carry_right
            + product * (height_right * tangent_right - height_left * tangent_left)
        )
        / spread
    )
    return (mass_flux, push_flux, carry_flux)


def tendencies(across, along):
    width = across[0].shape[1] - 4
    row_count = along[0].shape[0] - 4
    surface_pair = face_states(across[0], 1)
    east_pair = face_states(across[1], 1)
    north_pair = face_states(across[2], 1)
    depth_lon = 0.5 * (across[3][:, 1 : width + 2] + across[3][:, 2 : width + 3])
    open_lon = across[4][:, 1 : width + 2] * across[4][:, 2 : width + 3]
    mass_lon, push_lon, carry_lon = wave_flux(
        surface_pair[0],
        surface_pair[1],
        east_pair[0],
        east_pair[1],
        north_pair[0],
        north_pair[1],
        depth_lon,
        open_lon,
    )
    surface_pair = face_states(along[0], 0)
    east_pair = face_states(along[1], 0)
    north_pair = face_states(along[2], 0)
    depth_lat = 0.5 * (along[3][1 : row_count + 2] + along[3][2 : row_count + 3])
    open_lat = along[4][1 : row_count + 2] * along[4][2 : row_count + 3]
    mass_lat, push_lat, carry_lat = wave_flux(
        surface_pair[0],
        surface_pair[1],
        north_pair[0],
        north_pair[1],
        east_pair[0],
        east_pair[1],
        depth_lat,
        open_lat,
    )
    surface_mid = across[0][:, 2 : width + 2]
    wet_mid = across[4][:, 2 : width + 2]
    rate_surface = (
        -(mass_lon[:, 1:] - mass_lon[:, :-1]) / LON_SPACING
        - (mass_lat[1:] - mass_lat[:-1]) / LAT_SPACING
    )
    source_east = GRAVITY * surface_mid * (depth_lon[:, 1:] - depth_lon[:, :-1]) / LON_SPACING
    source_north = GRAVITY * surface_mid * (depth_lat[1:] - depth_lat[:-1]) / LAT_SPACING
    rate_east = wet_mid * (
        source_east
        - (push_lon[:, 1:] - push_lon[:, :-1]) / LON_SPACING
        - (carry_lat[1:] - carry_lat[:-1]) / LAT_SPACING
    )
    rate_north = wet_mid * (
        source_north
        - (carry_lon[:, 1:] - carry_lon[:, :-1]) / LON_SPACING
        - (push_lat[1:] - push_lat[:-1]) / LAT_SPACING
    )
    return (rate_surface, rate_east, rate_north)


def from_below(values, stride, along_axis, filler):
    length = values.shape[along_axis]
    padding = jnp.full_like(slab_of(values, 0, stride, along_axis), filler)
    return jnp.concatenate([padding, slab_of(values, 0, length - stride, along_axis)], along_axis)


def from_above(values, stride, along_axis, filler):
    length = values.shape[along_axis]
    padding = jnp.full_like(slab_of(values, 0, stride, along_axis), filler)
    return jnp.concatenate([slab_of(values, stride, length, along_axis), padding], along_axis)


def reduce_lines(lower_band, main_band, upper_band, rights, along_axis):
    length = rights.shape[along_axis]
    position = lax.broadcasted_iota(jnp.int32, rights.shape, along_axis)
    stride = 1
    for _ in range(PCR_STEPS):
        def from_lower(values, fill):
            return jnp.where(position >= stride, pltpu.roll(values, stride, along_axis), fill)

        def from_upper(values, fill):
            return jnp.where(
                position < length - stride, pltpu.roll(values, length - stride, along_axis), fill
            )

        below = [from_lower(band, fill) for band, fill in
                 ((lower_band, 0.0), (main_band, 1.0), (upper_band, 0.0), (rights, 0.0))]
        above = [from_upper(band, fill) for band, fill in
                 ((lower_band, 0.0), (main_band, 1.0), (upper_band, 0.0), (rights, 0.0))]
        weight_below = lower_band / below[1]
        weight_above = upper_band / above[1]
        new_lower = -weight_below * below[0]
        new_main = main_band - weight_below * below[2] - weight_above * above[0]
        new_upper = -weight_above * above[2]
        rights = rights - weight_below * below[3] - weight_above * above[3]
        lower_band, main_band, upper_band = new_lower, new_main, new_upper
        stride = stride * 2
    return rights / main_band


def section_kernel(surface_ref, east_ref, north_ref, depth_ref, wet_ref, keep_ref, mirror_ref,
                   lift_ref, start_surface, start_east, start_north, now_surface, now_east,
                   now_north, next_surface, next_east, next_north, east_out, north_out, *,
                   first_row, used_cols, tile_offset, weights):
    rows, cols = mirror_ref.shape
    tile_rows, tile_cols = lift_ref.shape
    depth = depth_ref[pl.ds(first_row, rows), :]
    surface = surface_ref[pl.ds(first_row, rows), :]
    coef = depth * depth / (3.0 * LON_SPACING * LON_SPACING)
    keep = lax.broadcasted_iota(jnp.int32, depth.shape, 1) < used_cols
    rights = east_ref[pl.ds(first_row, rows), :] / (depth + surface)
    east_raw = reduce_lines(
        jnp.where(keep, -coef, 0.0),
        jnp.where(keep, 1.0 + 2.0 * coef, 1.0),
        jnp.where(keep, -coef, 0.0),
        jnp.where(keep, rights, 0.0),
        1,
    )
    full_depth = depth_ref[...]
    coef = full_depth * full_depth / (3.0 * LAT_SPACING * LAT_SPACING)
    keep = keep_ref[...] > 0.0
    rights = north_ref[...] / (full_depth + surface_ref[...])
    north_raw = reduce_lines(
        jnp.where(keep, -coef, 0.0),
        jnp.where(keep, 1.0 + 2.0 * coef, 1.0),
        jnp.where(keep, -coef, 0.0),
        jnp.where(keep, rights, 0.0),
        0,
    )[first_row : first_row + rows]

    def wrapped(values):
        values = pltpu.roll(values, rows - (tile_offset[0] - first_row), 0)
        return pltpu.roll(values, cols - tile_offset[1], 1)

    wet = wrapped(wet_ref[pl.ds(first_row, rows), :])
    surface = wrapped(surface)
    depth = wrapped(depth)
    velocity_u = wet * wrapped(east_raw)
    velocity_v = wet * wrapped(north_raw)
    mirror = mirror_ref[...]
    for code, shift in ((1, rows - 1), (2, rows - 3), (3, 1), (4, 3)):
        velocity_v = jnp.where(mirror == code, -pltpu.roll(velocity_v, shift, 0), velocity_v)

    def east_of(values):
        return pltpu.roll(values, cols - 1, 1)

    def west_of(values):
        return pltpu.roll(values, 1, 1)

    def north_of(values):
        return pltpu.roll(values, rows - 1, 0)

    def south_of(values):
        return pltpu.roll(values, 1, 0)

    def face_pair(values, later, earlier):
        jump = later(values) - values
        slope = limited(earlier(jump), jump)
        return values + 0.5 * slope, later(values - 0.5 * slope)

    surface_pair = face_pair(surface, east_of, west_of)
    east_pair = face_pair(velocity_u, east_of, west_of)
    north_pair = face_pair(velocity_v, east_of, west_of)
    depth_lon = 0.5 * (depth + east_of(depth))
    open_lon = wet * east_of(wet)
    mass_lon, push_lon, carry_lon = wave_flux(
        surface_pair[0], surface_pair[1], east_pair[0], east_pair[1],
        north_pair[0], north_pair[1], depth_lon, open_lon,
    )
    surface_pair = face_pair(surface, north_of, south_of)
    east_pair = face_pair(velocity_u, north_of, south_of)
    north_pair = face_pair(velocity_v, north_of, south_of)
    depth_lat = 0.5 * (depth + north_of(depth))
    open_lat = wet * north_of(wet)
    mass_lat, push_lat, carry_lat = wave_flux(
        surface_pair[0], surface_pair[1], north_pair[0], north_pair[1],
        east_pair[0], east_pair[1], depth_lat, open_lat,
    )
    rate_surface = (
        -(mass_lon - west_of(mass_lon)) / LON_SPACING - (mass_lat - south_of(mass_lat)) / LAT_SPACING
    )
    source_east = GRAVITY * surface * (depth_lon - west_of(depth_lon)) / LON_SPACING
    source_north = GRAVITY * surface * (depth_lat - south_of(depth_lat)) / LAT_SPACING
    rate_east = wet * (
        source_east
        - (push_lon - west_of(push_lon)) / LON_SPACING
        - (carry_lat - south_of(carry_lat)) / LAT_SPACING
    )
    rate_north = wet * (
        source_north
        - (carry_lon - west_of(carry_lon)) / LON_SPACING
        - (push_lat - south_of(push_lat)) / LAT_SPACING
    )
    first, second = weights
    rates = (
        rate_surface[:tile_rows, :tile_cols] + lift_ref[...],
        rate_east[:tile_rows, :tile_cols],
        rate_north[:tile_rows, :tile_cols],
    )
    for out, start, now, rate in zip(
        (next_surface, next_east, next_north),
        (start_surface, start_east, start_north),
        (now_surface, now_east, now_north),
        rates,
    ):
        out[...] = first * start[...] + second * (now[...] + TIME_STEP * rate)
    east_out[...] = velocity_u[:tile_rows, :tile_cols]
    north_out[...] = velocity_v[:tile_rows, :tile_cols]


def section_step(fields, keep, mirror, lift, initial, current, first_row, used_cols, tile_offset,
                 weights):
    spec = pl.BlockSpec(memory_space=pltpu.VMEM)
    shape = jax.ShapeDtypeStruct(lift.shape, jnp.float32)
    return pl.pallas_call(
        lambda *refs: section_kernel(
            *refs, first_row=first_row, used_cols=used_cols, tile_offset=tile_offset,
            weights=weights,
        ),
        out_shape=(shape,) * 5,
        in_specs=[spec] * 14,
        out_specs=(spec,) * 5,
        name="section_step",
    )(*fields, keep, mirror, lift, *initial, *current)


def halo_box(fields, wide_x, wide_y, place, count):
    lon_count = lax.axis_size("lon")
    west = lax.ppermute(
        fields[:, :, -wide_x:], "lon", [(i, (i + 1) % lon_count) for i in range(lon_count)]
    )
    east = lax.ppermute(
        fields[:, :, :wide_x], "lon", [((i + 1) % lon_count, i) for i in range(lon_count)]
    )
    wide = jnp.concatenate([west, fields, east], axis=2)
    above = passed_along(wide[:, -wide_y:], "lat", 1)
    below = passed_along(wide[:, :wide_y], "lat", -1)
    above = jnp.where(place == 0, wide[:, wide_y - 1 :: -1], above)
    below = jnp.where(place == count - 1, wide[:, : -wide_y - 1 : -1], below)
    box = jnp.concatenate([above, wide, below], axis=1)
    aligned = [-(-size // unit) * unit for size, unit in zip(box.shape[1:], (8, 128))]
    return jnp.pad(box, ((0, 0), (0, aligned[0] - box.shape[1]), (0, aligned[1] - box.shape[2])))


def local(surface, momentum_x, momentum_y, water_depth, wet_mask, slide_cells, slide_rate):
    wet_float = wet_mask.astype(jnp.float32)
    place = lax.axis_index("lat")
    count = lax.axis_size("lat")
    tile_rows, tile_cols = surface.shape
    wide_x = WINDOW_LON + 2
    wide_y = WINDOW_LAT + 2
    lift = (
        jnp.zeros((tile_rows * tile_cols,), jnp.float32)
        .at[slide_cells.reshape(-1)]
        .add(slide_rate.reshape(-1))
        .reshape(tile_rows, tile_cols)
    )
    box_rows = tile_rows + 2 * wide_y
    box_cols = tile_cols + 2 * wide_x
    core_rows = slice(wide_y - 2, wide_y + tile_rows + 2)
    core_cols = slice(wide_x - 2, wide_x + tile_cols + 2)
    aligned_rows = -(-box_rows // 8) * 8
    aligned_cols = -(-box_cols // 128) * 128
    global_row = place * tile_rows - wide_y + lax.broadcasted_iota(
        jnp.int32, (aligned_rows, aligned_cols), 0
    )
    inside = (global_row >= 0) & (global_row < count * tile_rows) & (global_row < place * tile_rows - wide_y + box_rows)
    keep = inside.astype(jnp.float32)
    first_row = (wide_y - 2) // 8 * 8
    east_rows = -(-(wide_y + tile_rows + 2 - first_row) // 8) * 8
    wrapped_row = lax.broadcasted_iota(jnp.int32, (east_rows, aligned_cols), 0)
    top = place == 0
    bottom = place == count - 1
    mirror = jnp.where(
        top & (wrapped_row == east_rows - 1), 1,
        jnp.where(top & (wrapped_row == east_rows - 2), 2,
        jnp.where(bottom & (wrapped_row == tile_rows), 3,
        jnp.where(bottom & (wrapped_row == tile_rows + 1), 4, 0))),
    ).astype(jnp.int32)

    initial = (surface, momentum_x, momentum_y)
    current = initial
    velocity_u = surface
    velocity_v = surface
    depth_box = None
    for first, second in ((0.0, 1.0), (0.75, 0.25), (1.0 / 3.0, 2.0 / 3.0)):
        if depth_box is None:
            box = halo_box(
                jnp.stack([current[0], current[1], current[2], water_depth, wet_float]),
                wide_x, wide_y, place, count,
            )
            depth_box, wet_box = box[3], box[4]
        else:
            box = halo_box(jnp.stack(list(current)), wide_x, wide_y, place, count)
        next_surface, next_east, next_north, velocity_u, velocity_v = section_step(
            (box[0], box[1], box[2], depth_box, wet_box), keep, mirror, lift, initial, current,
            first_row, box_cols, (wide_y, wide_x), (first, second),
        )
        current = (next_surface, next_east, next_north)
    return (current[0], current[1], current[2], velocity_u, velocity_v)


def solution(mesh):
    in_specs = (P("lat", "lon"),) * 7
    out_specs = (P("lat", "lon"),) * 5
    return jax.shard_map(local, mesh=mesh, in_specs=in_specs, out_specs=out_specs, check_vma=False)
```

```python
import jax
import jax.numpy as jnp
from jax import lax
from jax.sharding import PartitionSpec as P
from jax.experimental import pallas as pl
from jax.experimental.pallas import tpu as pltpu

GRAVITY = 1.0
LON_SPACING = 0.5
LAT_SPACING = 0.6
TIME_STEP = 0.1
WINDOW_LON = 40
WINDOW_LAT = 32
PCR_STEPS = 6


def shifted(block, axis, distance):
    devices = range(lax.axis_size(axis))
    route = [((i - distance) % len(devices), i) for i in devices]
    return lax.ppermute(block, axis, route)


def passed_along(x, axis, by):
    peers = lax.axis_size(axis)
    pairs = [(i, i + by) for i in range(peers) if 0 <= i + by < peers]
    return lax.ppermute(x, axis, pairs)


def extended(cells, sides, width, closed):
    for axis, dim in sides:
        count = lax.axis_size(axis)
        ends = count if closed else count - 1
        head = lax.slice_in_dim(cells, 0, width, axis=dim)
        tail = lax.slice_in_dim(cells, cells.shape[dim] - width, cells.shape[dim], axis=dim)
        cells = jnp.concatenate(
            [
                lax.ppermute(tail, axis, [(i, (i + 1) % count) for i in range(ends)]),
                cells,
                lax.ppermute(head, axis, [((i + 1) % count, i) for i in range(ends)]),
            ],
            axis=dim,
        )
    return cells


def slab_of(values, start, stop, along_axis):
    return lax.slice_in_dim(values, start, stop, axis=along_axis)


def limited(former, latter):
    return jnp.maximum(jnp.minimum(former, latter), 0.0) + jnp.minimum(
        jnp.maximum(former, latter), 0.0
    )


def face_states(values, along_axis):
    length = values.shape[along_axis]
    jumps = slab_of(values, 1, length, along_axis) - slab_of(values, 0, length - 1, along_axis)
    slopes = limited(
        slab_of(jumps, 0, length - 2, along_axis), slab_of(jumps, 1, length - 1, along_axis)
    )
    left_state = slab_of(values, 1, length - 2, along_axis) + 0.5 * slab_of(
        slopes, 0, length - 3, along_axis
    )
    right_state = slab_of(values, 2, length - 1, along_axis) - 0.5 * slab_of(
        slopes, 1, length - 2, along_axis
    )
    return (left_state, right_state)


def wave_flux(
    surface_left,
    surface_right,
    normal_left,
    normal_right,
    tangent_left,
    tangent_right,
    face_depth,
    opened,
):
    height_left = surface_left + face_depth
    height_right = surface_right + face_depth
    celerity_left = jnp.sqrt(GRAVITY * height_left)
    celerity_right = jnp.sqrt(GRAVITY * height_right)
    slowest = jnp.minimum(
        jnp.minimum(normal_left - celerity_left, normal_right - celerity_right), 0.0
    )
    fastest = jnp.maximum(
        jnp.maximum(normal_left + celerity_left, normal_right + celerity_right), 0.0
    )
    spread = fastest - slowest
    product = slowest * fastest
    mass_left = height_left * normal_left
    mass_right = height_right * normal_right
    push_left = mass_left * normal_left + GRAVITY * (
        0.5 * surface_left * surface_left + face_depth * surface_left
    )
    push_right = mass_right * normal_right + GRAVITY * (
        0.5 * surface_right * surface_right + face_depth * surface_right
    )
    carry_left = mass_left * tangent_left
    carry_right = mass_right * tangent_right
    mass_flux = (
        opened
        * (fastest * mass_left - slowest * mass_right + product * (surface_right - surface_left))
        / spread
    )
    push_flux = (
        opened
        * (fastest * push_left - slowest * push_right + product * (mass_right - mass_left))
        / spread
    )
    carry_flux = (
        opened
        * (
            fastest * carry_left
            - slowest * carry_right
            + product * (height_right * tangent_right - height_left * tangent_left)
        )
        / spread
    )
    return (mass_flux, push_flux, carry_flux)


def tendencies(across, along):
    width = across[0].shape[1] - 4
    row_count = along[0].shape[0] - 4
    surface_pair = face_states(across[0], 1)
    east_pair = face_states(across[1], 1)
    north_pair = face_states(across[2], 1)
    depth_lon = 0.5 * (across[3][:, 1 : width + 2] + across[3][:, 2 : width + 3])
    open_lon = across[4][:, 1 : width + 2] * across[4][:, 2 : width + 3]
    mass_lon, push_lon, carry_lon = wave_flux(
        surface_pair[0],
        surface_pair[1],
        east_pair[0],
        east_pair[1],
        north_pair[0],
        north_pair[1],
        depth_lon,
        open_lon,
    )
    surface_pair = face_states(along[0], 0)
    east_pair = face_states(along[1], 0)
    north_pair = face_states(along[2], 0)
    depth_lat = 0.5 * (along[3][1 : row_count + 2] + along[3][2 : row_count + 3])
    open_lat = along[4][1 : row_count + 2] * along[4][2 : row_count + 3]
    mass_lat, push_lat, carry_lat = wave_flux(
        surface_pair[0],
        surface_pair[1],
        north_pair[0],
        north_pair[1],
        east_pair[0],
        east_pair[1],
        depth_lat,
        open_lat,
    )
    surface_mid = across[0][:, 2 : width + 2]
    wet_mid = across[4][:, 2 : width + 2]
    rate_surface = (
        -(mass_lon[:, 1:] - mass_lon[:, :-1]) / LON_SPACING
        - (mass_lat[1:] - mass_lat[:-1]) / LAT_SPACING
    )
    source_east = GRAVITY * surface_mid * (depth_lon[:, 1:] - depth_lon[:, :-1]) / LON_SPACING
    source_north = GRAVITY * surface_mid * (depth_lat[1:] - depth_lat[:-1]) / LAT_SPACING
    rate_east = wet_mid * (
        source_east
        - (push_lon[:, 1:] - push_lon[:, :-1]) / LON_SPACING
        - (carry_lat[1:] - carry_lat[:-1]) / LAT_SPACING
    )
    rate_north = wet_mid * (
        source_north
        - (carry_lon[:, 1:] - carry_lon[:, :-1]) / LON_SPACING
        - (push_lat[1:] - push_lat[:-1]) / LAT_SPACING
    )
    return (rate_surface, rate_east, rate_north)


def from_below(values, stride, along_axis, filler):
    length = values.shape[along_axis]
    padding = jnp.full_like(slab_of(values, 0, stride, along_axis), filler)
    return jnp.concatenate([padding, slab_of(values, 0, length - stride, along_axis)], along_axis)


def from_above(values, stride, along_axis, filler):
    length = values.shape[along_axis]
    padding = jnp.full_like(slab_of(values, 0, stride, along_axis), filler)
    return jnp.concatenate([slab_of(values, stride, length, along_axis), padding], along_axis)


def reduce_lines(lower_band, main_band, upper_band, rights, along_axis):
    length = rights.shape[along_axis]
    position = lax.broadcasted_iota(jnp.int32, rights.shape, along_axis)
    stride = 1
    for _ in range(PCR_STEPS):
        def from_lower(values, fill):
            return jnp.where(position >= stride, pltpu.roll(values, stride, along_axis), fill)

        def from_upper(values, fill):
            return jnp.where(
                position < length - stride, pltpu.roll(values, length - stride, along_axis), fill
            )

        below = [from_lower(band, fill) for band, fill in
                 ((lower_band, 0.0), (main_band, 1.0), (upper_band, 0.0), (rights, 0.0))]
        above = [from_upper(band, fill) for band, fill in
                 ((lower_band, 0.0), (main_band, 1.0), (upper_band, 0.0), (rights, 0.0))]
        weight_below = lower_band / below[1]
        weight_above = upper_band / above[1]
        new_lower = -weight_below * below[0]
        new_main = main_band - weight_below * below[2] - weight_above * above[0]
        new_upper = -weight_above * above[2]
        rights = rights - weight_below * below[3] - weight_above * above[3]
        lower_band, main_band, upper_band = new_lower, new_main, new_upper
        stride = stride * 2
    return rights / main_band


def section_kernel(surface_ref, east_ref, north_ref, depth_ref, wet_ref, keep_ref, mirror_ref,
                   lift_ref, start_surface, start_east, start_north, now_surface, now_east,
                   now_north, next_surface, next_east, next_north, east_out, north_out, *,
                   first_row, used_cols, tile_offset, weights):
    rows, cols = mirror_ref.shape
    tile_rows, tile_cols = lift_ref.shape
    depth = depth_ref[pl.ds(first_row, rows), :]
    surface = surface_ref[pl.ds(first_row, rows), :]
    coef = depth * depth / (3.0 * LON_SPACING * LON_SPACING)
    keep = lax.broadcasted_iota(jnp.int32, depth.shape, 1) < used_cols
    rights = east_ref[pl.ds(first_row, rows), :] / (depth + surface)
    east_raw = reduce_lines(
        jnp.where(keep, -coef, 0.0),
        jnp.where(keep, 1.0 + 2.0 * coef, 1.0),
        jnp.where(keep, -coef, 0.0),
        jnp.where(keep, rights, 0.0),
        1,
    )
    full_depth = depth_ref[...]
    coef = full_depth * full_depth / (3.0 * LAT_SPACING * LAT_SPACING)
    keep = keep_ref[...] > 0.0
    rights = north_ref[...] / (full_depth + surface_ref[...])
    north_raw = reduce_lines(
        jnp.where(keep, -coef, 0.0),
        jnp.where(keep, 1.0 + 2.0 * coef, 1.0),
        jnp.where(keep, -coef, 0.0),
        jnp.where(keep, rights, 0.0),
        0,
    )[first_row : first_row + rows]

    def wrapped(values):
        values = pltpu.roll(values, rows - (tile_offset[0] - first_row), 0)
        return pltpu.roll(values, cols - tile_offset[1], 1)

    wet = wrapped(wet_ref[pl.ds(first_row, rows), :])
    surface = wrapped(surface)
    depth = wrapped(depth)
    velocity_u = wet * wrapped(east_raw)
    velocity_v = wet * wrapped(north_raw)
    mirror = mirror_ref[...]
    for code, shift in ((1, rows - 1), (2, rows - 3), (3, 1), (4, 3)):
        velocity_v = jnp.where(mirror == code, -pltpu.roll(velocity_v, shift, 0), velocity_v)

    def east_of(values):
        return pltpu.roll(values, cols - 1, 1)

    def west_of(values):
        return pltpu.roll(values, 1, 1)

    def north_of(values):
        return pltpu.roll(values, rows - 1, 0)

    def south_of(values):
        return pltpu.roll(values, 1, 0)

    def face_pair(values, later, earlier):
        jump = later(values) - values
        slope = limited(earlier(jump), jump)
        return values + 0.5 * slope, later(values - 0.5 * slope)

    surface_pair = face_pair(surface, east_of, west_of)
    east_pair = face_pair(velocity_u, east_of, west_of)
    north_pair = face_pair(velocity_v, east_of, west_of)
    depth_lon = 0.5 * (depth + east_of(depth))
    open_lon = wet * east_of(wet)
    mass_lon, push_lon, carry_lon = wave_flux(
        surface_pair[0], surface_pair[1], east_pair[0], east_pair[1],
        north_pair[0], north_pair[1], depth_lon, open_lon,
    )
    surface_pair = face_pair(surface, north_of, south_of)
    east_pair = face_pair(velocity_u, north_of, south_of)
    north_pair = face_pair(velocity_v, north_of, south_of)
    depth_lat = 0.5 * (depth + north_of(depth))
    open_lat = wet * north_of(wet)
    mass_lat, push_lat, carry_lat = wave_flux(
        surface_pair[0], surface_pair[1], north_pair[0], north_pair[1],
        east_pair[0], east_pair[1], depth_lat, open_lat,
    )
    rate_surface = (
        -(mass_lon - west_of(mass_lon)) / LON_SPACING - (mass_lat - south_of(mass_lat)) / LAT_SPACING
    )
    source_east = GRAVITY * surface * (depth_lon - west_of(depth_lon)) / LON_SPACING
    source_north = GRAVITY * surface * (depth_lat - south_of(depth_lat)) / LAT_SPACING
    rate_east = wet * (
        source_east
        - (push_lon - west_of(push_lon)) / LON_SPACING
        - (carry_lat - south_of(carry_lat)) / LAT_SPACING
    )
    rate_north = wet * (
        source_north
        - (carry_lon - west_of(carry_lon)) / LON_SPACING
        - (push_lat - south_of(push_lat)) / LAT_SPACING
    )
    first, second = weights
    rates = (
        rate_surface[:tile_rows, :tile_cols] + lift_ref[...],
        rate_east[:tile_rows, :tile_cols],
        rate_north[:tile_rows, :tile_cols],
    )
    for out, start, now, rate in zip(
        (next_surface, next_east, next_north),
        (start_surface, start_east, start_north),
        (now_surface, now_east, now_north),
        rates,
    ):
        out[...] = first * start[...] + second * (now[...] + TIME_STEP * rate)
    east_out[...] = velocity_u[:tile_rows, :tile_cols]
    north_out[...] = velocity_v[:tile_rows, :tile_cols]


def section_step(fields, keep, mirror, lift, initial, current, first_row, used_cols, tile_offset,
                 weights):
    spec = pl.BlockSpec(memory_space=pltpu.VMEM)
    shape = jax.ShapeDtypeStruct(lift.shape, jnp.float32)
    return pl.pallas_call(
        lambda *refs: section_kernel(
            *refs, first_row=first_row, used_cols=used_cols, tile_offset=tile_offset,
            weights=weights,
        ),
        out_shape=(shape,) * 5,
        in_specs=[spec] * 14,
        out_specs=(spec,) * 5,
        name="section_step",
    )(*fields, keep, mirror, lift, *initial, *current)


def halo_box(fields, wide_x, wide_y, place, count, padded_shape):
    lon_count = lax.axis_size("lon")
    west = lax.ppermute(
        fields[:, :, -wide_x:], "lon", [(i, (i + 1) % lon_count) for i in range(lon_count)]
    )
    east = lax.ppermute(
        fields[:, :, :wide_x], "lon", [((i + 1) % lon_count, i) for i in range(lon_count)]
    )
    wide = jnp.concatenate([west, fields, east], axis=2)
    above = passed_along(wide[:, -wide_y:], "lat", 1)
    below = passed_along(wide[:, :wide_y], "lat", -1)
    above = jnp.where(place == 0, wide[:, wide_y - 1 :: -1], above)
    below = jnp.where(place == count - 1, wide[:, : -wide_y - 1 : -1], below)
    box = jnp.concatenate([above, wide, below], axis=1)
    return pad_to(box, padded_shape)


def pad_to(values, shape):
    widths = [(0, 0)] * (values.ndim - 2) + [
        (0, want - have) for want, have in zip(shape, values.shape[-2:])
    ]
    return jnp.pad(values, widths)


def wall_mirrored(values, halo, place, count):
    rows = values.shape[-2]
    top = jnp.concatenate([values[..., 2 * halo - 1 : halo - 1 : -1, :], values[..., halo:, :]], axis=-2)
    values = jnp.where(place == 0, top, values)
    bottom = jnp.concatenate(
        [values[..., : rows - halo, :], values[..., rows - halo - 1 : rows - 2 * halo - 1 : -1, :]],
        axis=-2,
    )
    return jnp.where(place == count - 1, bottom, values)


class Geometry:
    def __init__(self, out_rows, out_cols, halo_y, halo_x):
        self.box_rows = out_rows + 2 * halo_y
        self.box_cols = out_cols + 2 * halo_x
        self.first_row = (halo_y - 2) // 8 * 8
        self.rows = -(-(halo_y + out_rows + 2 - self.first_row) // 8) * 8
        self.padded = (
            max(-(-self.box_rows // 8) * 8, self.first_row + self.rows),
            -(-self.box_cols // 128) * 128,
        )
        self.offset = (halo_y, halo_x)

    def masks(self, region_above, place, count, tile_rows):
        box_row = lax.broadcasted_iota(jnp.int32, self.padded, 0)
        global_row = place * tile_rows - region_above - self.offset[0] + box_row
        inside = (global_row >= 0) & (global_row < count * tile_rows) & (box_row < self.box_rows)
        wrapped_row = lax.broadcasted_iota(jnp.int32, (self.rows, self.padded[1]), 0)
        tile_row = jnp.where(wrapped_row >= self.rows - 2, wrapped_row - self.rows, wrapped_row)
        tile_row = tile_row - region_above
        top = place == 0
        bottom = place == count - 1
        mirror = jnp.where(
            top & (tile_row == -1), 1,
            jnp.where(top & (tile_row == -2), 2,
            jnp.where(bottom & (tile_row == tile_rows), 3,
            jnp.where(bottom & (tile_row == tile_rows + 1), 4, 0))),
        ).astype(jnp.int32)
        return inside.astype(jnp.float32), mirror


def local(surface, momentum_x, momentum_y, water_depth, wet_mask, slide_cells, slide_rate):
    wet_float = wet_mask.astype(jnp.float32)
    place = lax.axis_index("lat")
    count = lax.axis_size("lat")
    tile_rows, tile_cols = surface.shape
    wide_x = WINDOW_LON + 2
    wide_y = WINDOW_LAT + 2
    lift = (
        jnp.zeros((tile_rows * tile_cols,), jnp.float32)
        .at[slide_cells.reshape(-1)]
        .add(slide_rate.reshape(-1))
        .reshape(tile_rows, tile_cols)
    )
    ring = Geometry(tile_rows + 2 * wide_y, tile_cols + 2 * wide_x, wide_y, wide_x)
    plain = Geometry(tile_rows, tile_cols, wide_y, wide_x)
    ring_keep, ring_mirror = ring.masks(wide_y, place, count, tile_rows)
    plain_keep, plain_mirror = plain.masks(0, place, count, tile_rows)
    initial = (surface, momentum_x, momentum_y)

    big = halo_box(
        jnp.stack([surface, momentum_x, momentum_y, water_depth, wet_float, lift]),
        2 * wide_x, 2 * wide_y, place, count, ring.padded,
    )
    region = (slice(wide_y, wide_y + plain.box_rows), slice(wide_x, wide_x + plain.box_cols))
    start_ring = tuple(big[k][region] for k in range(3))
    first_state = section_step(
        tuple(big[k] for k in range(5)), ring_keep, ring_mirror, big[5][region], start_ring,
        start_ring, ring.first_row, ring.box_cols, ring.offset, (0.0, 1.0),
    )[:3]
    first_state = wall_mirrored(jnp.stack(first_state), wide_y, place, count)
    depth_box = pad_to(big[3][region], plain.padded)
    wet_box = pad_to(big[4][region], plain.padded)
    tile = (slice(wide_y, wide_y + tile_rows), slice(wide_x, wide_x + tile_cols))
    current = tuple(first_state[k][tile] for k in range(3))
    box = pad_to(first_state, plain.padded)
    for first, second in ((0.75, 0.25), (1.0 / 3.0, 2.0 / 3.0)):
        if box is None:
            box = halo_box(jnp.stack(list(current)), wide_x, wide_y, place, count, plain.padded)
        next_surface, next_east, next_north, velocity_u, velocity_v = section_step(
            (box[0], box[1], box[2], depth_box, wet_box), plain_keep, plain_mirror, lift, initial,
            current, plain.first_row, plain.box_cols, plain.offset, (first, second),
        )
        current = (next_surface, next_east, next_north)
        box = None
    return (current[0], current[1], current[2], velocity_u, velocity_v)


def solution(mesh):
    in_specs = (P("lat", "lon"),) * 7
    out_specs = (P("lat", "lon"),) * 5
    return jax.shard_map(local, mesh=mesh, in_specs=in_specs, out_specs=out_specs, check_vma=False)
```

```python
import jax
import jax.numpy as jnp
from jax import lax
from jax.sharding import PartitionSpec as P
from jax.experimental import pallas as pl
from jax.experimental.pallas import tpu as pltpu

GRAVITY = 1.0
LON_SPACING = 0.5
LAT_SPACING = 0.6
TIME_STEP = 0.1
WINDOW_LON = 40
WINDOW_LAT = 32
PCR_STEPS = 6


def shifted(block, axis, distance):
    devices = range(lax.axis_size(axis))
    route = [((i - distance) % len(devices), i) for i in devices]
    return lax.ppermute(block, axis, route)


def passed_along(x, axis, by):
    peers = lax.axis_size(axis)
    pairs = [(i, i + by) for i in range(peers) if 0 <= i + by < peers]
    return lax.ppermute(x, axis, pairs)


def extended(cells, sides, width, closed):
    for axis, dim in sides:
        count = lax.axis_size(axis)
        ends = count if closed else count - 1
        head = lax.slice_in_dim(cells, 0, width, axis=dim)
        tail = lax.slice_in_dim(cells, cells.shape[dim] - width, cells.shape[dim], axis=dim)
        cells = jnp.concatenate(
            [
                lax.ppermute(tail, axis, [(i, (i + 1) % count) for i in range(ends)]),
                cells,
                lax.ppermute(head, axis, [((i + 1) % count, i) for i in range(ends)]),
            ],
            axis=dim,
        )
    return cells


def slab_of(values, start, stop, along_axis):
    return lax.slice_in_dim(values, start, stop, axis=along_axis)


def limited(former, latter):
    return jnp.maximum(jnp.minimum(former, latter), 0.0) + jnp.minimum(
        jnp.maximum(former, latter), 0.0
    )


def face_states(values, along_axis):
    length = values.shape[along_axis]
    jumps = slab_of(values, 1, length, along_axis) - slab_of(values, 0, length - 1, along_axis)
    slopes = limited(
        slab_of(jumps, 0, length - 2, along_axis), slab_of(jumps, 1, length - 1, along_axis)
    )
    left_state = slab_of(values, 1, length - 2, along_axis) + 0.5 * slab_of(
        slopes, 0, length - 3, along_axis
    )
    right_state = slab_of(values, 2, length - 1, along_axis) - 0.5 * slab_of(
        slopes, 1, length - 2, along_axis
    )
    return (left_state, right_state)


def wave_flux(
    surface_left,
    surface_right,
    normal_left,
    normal_right,
    tangent_left,
    tangent_right,
    face_depth,
    opened,
):
    height_left = surface_left + face_depth
    height_right = surface_right + face_depth
    celerity_left = jnp.sqrt(GRAVITY * height_left)
    celerity_right = jnp.sqrt(GRAVITY * height_right)
    slowest = jnp.minimum(
        jnp.minimum(normal_left - celerity_left, normal_right - celerity_right), 0.0
    )
    fastest = jnp.maximum(
        jnp.maximum(normal_left + celerity_left, normal_right + celerity_right), 0.0
    )
    spread = fastest - slowest
    product = slowest * fastest
    mass_left = height_left * normal_left
    mass_right = height_right * normal_right
    push_left = mass_left * normal_left + GRAVITY * (
        0.5 * surface_left * surface_left + face_depth * surface_left
    )
    push_right = mass_right * normal_right + GRAVITY * (
        0.5 * surface_right * surface_right + face_depth * surface_right
    )
    carry_left = mass_left * tangent_left
    carry_right = mass_right * tangent_right
    mass_flux = (
        opened
        * (fastest * mass_left - slowest * mass_right + product * (surface_right - surface_left))
        / spread
    )
    push_flux = (
        opened
        * (fastest * push_left - slowest * push_right + product * (mass_right - mass_left))
        / spread
    )
    carry_flux = (
        opened
        * (
            fastest * carry_left
            - slowest * carry_right
            + product * (height_right * tangent_right - height_left * tangent_left)
        )
        / spread
    )
    return (mass_flux, push_flux, carry_flux)


def tendencies(across, along):
    width = across[0].shape[1] - 4
    row_count = along[0].shape[0] - 4
    surface_pair = face_states(across[0], 1)
    east_pair = face_states(across[1], 1)
    north_pair = face_states(across[2], 1)
    depth_lon = 0.5 * (across[3][:, 1 : width + 2] + across[3][:, 2 : width + 3])
    open_lon = across[4][:, 1 : width + 2] * across[4][:, 2 : width + 3]
    mass_lon, push_lon, carry_lon = wave_flux(
        surface_pair[0],
        surface_pair[1],
        east_pair[0],
        east_pair[1],
        north_pair[0],
        north_pair[1],
        depth_lon,
        open_lon,
    )
    surface_pair = face_states(along[0], 0)
    east_pair = face_states(along[1], 0)
    north_pair = face_states(along[2], 0)
    depth_lat = 0.5 * (along[3][1 : row_count + 2] + along[3][2 : row_count + 3])
    open_lat = along[4][1 : row_count + 2] * along[4][2 : row_count + 3]
    mass_lat, push_lat, carry_lat = wave_flux(
        surface_pair[0],
        surface_pair[1],
        north_pair[0],
        north_pair[1],
        east_pair[0],
        east_pair[1],
        depth_lat,
        open_lat,
    )
    surface_mid = across[0][:, 2 : width + 2]
    wet_mid = across[4][:, 2 : width + 2]
    rate_surface = (
        -(mass_lon[:, 1:] - mass_lon[:, :-1]) / LON_SPACING
        - (mass_lat[1:] - mass_lat[:-1]) / LAT_SPACING
    )
    source_east = GRAVITY * surface_mid * (depth_lon[:, 1:] - depth_lon[:, :-1]) / LON_SPACING
    source_north = GRAVITY * surface_mid * (depth_lat[1:] - depth_lat[:-1]) / LAT_SPACING
    rate_east = wet_mid * (
        source_east
        - (push_lon[:, 1:] - push_lon[:, :-1]) / LON_SPACING
        - (carry_lat[1:] - carry_lat[:-1]) / LAT_SPACING
    )
    rate_north = wet_mid * (
        source_north
        - (carry_lon[:, 1:] - carry_lon[:, :-1]) / LON_SPACING
        - (push_lat[1:] - push_lat[:-1]) / LAT_SPACING
    )
    return (rate_surface, rate_east, rate_north)


def from_below(values, stride, along_axis, filler):
    length = values.shape[along_axis]
    padding = jnp.full_like(slab_of(values, 0, stride, along_axis), filler)
    return jnp.concatenate([padding, slab_of(values, 0, length - stride, along_axis)], along_axis)


def from_above(values, stride, along_axis, filler):
    length = values.shape[along_axis]
    padding = jnp.full_like(slab_of(values, 0, stride, along_axis), filler)
    return jnp.concatenate([slab_of(values, stride, length, along_axis), padding], along_axis)


def reduce_lines(lower_band, main_band, upper_band, rights, along_axis):
    length = rights.shape[along_axis]
    position = lax.broadcasted_iota(jnp.int32, rights.shape, along_axis)
    stride = 1
    for _ in range(PCR_STEPS):
        def from_lower(values, fill):
            return jnp.where(position >= stride, pltpu.roll(values, stride, along_axis), fill)

        def from_upper(values, fill):
            return jnp.where(
                position < length - stride, pltpu.roll(values, length - stride, along_axis), fill
            )

        below = [from_lower(band, fill) for band, fill in
                 ((lower_band, 0.0), (main_band, 1.0), (upper_band, 0.0), (rights, 0.0))]
        above = [from_upper(band, fill) for band, fill in
                 ((lower_band, 0.0), (main_band, 1.0), (upper_band, 0.0), (rights, 0.0))]
        weight_below = lower_band / below[1]
        weight_above = upper_band / above[1]
        new_lower = -weight_below * below[0]
        new_main = main_band - weight_below * below[2] - weight_above * above[0]
        new_upper = -weight_above * above[2]
        rights = rights - weight_below * below[3] - weight_above * above[3]
        lower_band, main_band, upper_band = new_lower, new_main, new_upper
        stride = stride * 2
    return rights / main_band


def tendency_body(surface_ref, east_ref, north_ref, depth_ref, wet_ref, keep_ref, mirror_ref,
                  first_row, used_cols, tile_offset):
    rows, cols = mirror_ref.shape
    depth = depth_ref[pl.ds(first_row, rows), :]
    surface = surface_ref[pl.ds(first_row, rows), :]
    coef = depth * depth / (3.0 * LON_SPACING * LON_SPACING)
    keep = lax.broadcasted_iota(jnp.int32, depth.shape, 1) < used_cols
    rights = east_ref[pl.ds(first_row, rows), :] / (depth + surface)
    east_raw = reduce_lines(
        jnp.where(keep, -coef, 0.0),
        jnp.where(keep, 1.0 + 2.0 * coef, 1.0),
        jnp.where(keep, -coef, 0.0),
        jnp.where(keep, rights, 0.0),
        1,
    )
    full_depth = depth_ref[...]
    coef = full_depth * full_depth / (3.0 * LAT_SPACING * LAT_SPACING)
    keep = keep_ref[...] > 0.0
    rights = north_ref[...] / (full_depth + surface_ref[...])
    north_raw = reduce_lines(
        jnp.where(keep, -coef, 0.0),
        jnp.where(keep, 1.0 + 2.0 * coef, 1.0),
        jnp.where(keep, -coef, 0.0),
        jnp.where(keep, rights, 0.0),
        0,
    )[first_row : first_row + rows]

    def wrapped(values):
        values = pltpu.roll(values, rows - (tile_offset[0] - first_row), 0)
        return pltpu.roll(values, cols - tile_offset[1], 1)

    wet = wrapped(wet_ref[pl.ds(first_row, rows), :])
    surface = wrapped(surface)
    depth = wrapped(depth)
    velocity_u = wet * wrapped(east_raw)
    velocity_v = wet * wrapped(north_raw)
    mirror = mirror_ref[...]
    for code, shift in ((1, rows - 1), (2, rows - 3), (3, 1), (4, 3)):
        velocity_v = jnp.where(mirror == code, -pltpu.roll(velocity_v, shift, 0), velocity_v)

    def east_of(values):
        return pltpu.roll(values, cols - 1, 1)

    def west_of(values):
        return pltpu.roll(values, 1, 1)

    def north_of(values):
        return pltpu.roll(values, rows - 1, 0)

    def south_of(values):
        return pltpu.roll(values, 1, 0)

    def face_pair(values, later, earlier):
        jump = later(values) - values
        slope = limited(earlier(jump), jump)
        return values + 0.5 * slope, later(values - 0.5 * slope)

    surface_pair = face_pair(surface, east_of, west_of)
    east_pair = face_pair(velocity_u, east_of, west_of)
    north_pair = face_pair(velocity_v, east_of, west_of)
    depth_lon = 0.5 * (depth + east_of(depth))
    open_lon = wet * east_of(wet)
    mass_lon, push_lon, carry_lon = wave_flux(
        surface_pair[0], surface_pair[1], east_pair[0], east_pair[1],
        north_pair[0], north_pair[1], depth_lon, open_lon,
    )
    surface_pair = face_pair(surface, north_of, south_of)
    east_pair = face_pair(velocity_u, north_of, south_of)
    north_pair = face_pair(velocity_v, north_of, south_of)
    depth_lat = 0.5 * (depth + north_of(depth))
    open_lat = wet * north_of(wet)
    mass_lat, push_lat, carry_lat = wave_flux(
        surface_pair[0], surface_pair[1], north_pair[0], north_pair[1],
        east_pair[0], east_pair[1], depth_lat, open_lat,
    )
    rate_surface = (
        -(mass_lon - west_of(mass_lon)) / LON_SPACING - (mass_lat - south_of(mass_lat)) / LAT_SPACING
    )
    source_east = GRAVITY * surface * (depth_lon - west_of(depth_lon)) / LON_SPACING
    source_north = GRAVITY * surface * (depth_lat - south_of(depth_lat)) / LAT_SPACING
    rate_east = wet * (
        source_east
        - (push_lon - west_of(push_lon)) / LON_SPACING
        - (carry_lat - south_of(carry_lat)) / LAT_SPACING
    )
    rate_north = wet * (
        source_north
        - (carry_lon - west_of(carry_lon)) / LON_SPACING
        - (push_lat - south_of(push_lat)) / LAT_SPACING
    )
    return (rate_surface, rate_east, rate_north), (surface, velocity_u, velocity_v), wrapped


def section_kernel(surface_ref, east_ref, north_ref, depth_ref, wet_ref, keep_ref, mirror_ref,
                   lift_ref, start_surface, start_east, start_north,
                   next_surface, next_east, next_north, east_out, north_out, *,
                   first_row, used_cols, tile_offset, weights):
    tile_rows, tile_cols = lift_ref.shape
    rates, (surface, velocity_u, velocity_v), wrapped = tendency_body(
        surface_ref, east_ref, north_ref, depth_ref, wet_ref, keep_ref, mirror_ref,
        first_row, used_cols, tile_offset,
    )
    rows = mirror_ref.shape[0]
    nows = (
        surface,
        wrapped(east_ref[pl.ds(first_row, rows), :]),
        wrapped(north_ref[pl.ds(first_row, rows), :]),
    )
    first, second = weights
    rates = (
        rates[0][:tile_rows, :tile_cols] + lift_ref[...],
        rates[1][:tile_rows, :tile_cols],
        rates[2][:tile_rows, :tile_cols],
    )
    for out, start, now, rate in zip(
        (next_surface, next_east, next_north),
        (start_surface, start_east, start_north),
        nows,
        rates,
    ):
        out[...] = first * start[...] + second * (now[:tile_rows, :tile_cols] + TIME_STEP * rate)
    east_out[...] = velocity_u[:tile_rows, :tile_cols]
    north_out[...] = velocity_v[:tile_rows, :tile_cols]


def ring_kernel(surface_ref, east_ref, north_ref, depth_ref, wet_ref, keep_ref, mirror_ref,
                lift_ref, next_surface, next_east, next_north, depth_out, wet_out, *,
                first_row, used_cols, tile_offset):
    rows = mirror_ref.shape[0]
    out_rows, out_cols = next_surface.shape
    rates, (surface, _, _), wrapped = tendency_body(
        surface_ref, east_ref, north_ref, depth_ref, wet_ref, keep_ref, mirror_ref,
        first_row, used_cols, tile_offset,
    )
    lift = wrapped(lift_ref[pl.ds(first_row, rows), :])
    nows = (
        surface,
        wrapped(east_ref[pl.ds(first_row, rows), :]),
        wrapped(north_ref[pl.ds(first_row, rows), :]),
    )
    rates = (rates[0] + lift, rates[1], rates[2])
    for out, now, rate in zip((next_surface, next_east, next_north), nows, rates):
        out[...] = (0.0 * now + 1.0 * (now + TIME_STEP * rate))[:out_rows, :out_cols]
    depth_out[...] = wrapped(depth_ref[pl.ds(first_row, rows), :])[:out_rows, :out_cols]
    wet_out[...] = wrapped(wet_ref[pl.ds(first_row, rows), :])[:out_rows, :out_cols]


def ring_step(fields, keep, mirror, out_shape, first_row, used_cols, tile_offset):
    spec = pl.BlockSpec(memory_space=pltpu.VMEM)
    shape = jax.ShapeDtypeStruct(out_shape, jnp.float32)
    return pl.pallas_call(
        lambda *refs: ring_kernel(
            *refs, first_row=first_row, used_cols=used_cols, tile_offset=tile_offset
        ),
        out_shape=(shape,) * 5,
        in_specs=[spec] * 8,
        out_specs=(spec,) * 5,
        name="ring_step",
    )(*fields[:5], keep, mirror, fields[5])


def section_step(fields, keep, mirror, lift, initial, first_row, used_cols, tile_offset,
                 weights):
    spec = pl.BlockSpec(memory_space=pltpu.VMEM)
    shape = jax.ShapeDtypeStruct(lift.shape, jnp.float32)
    return pl.pallas_call(
        lambda *refs: section_kernel(
            *refs, first_row=first_row, used_cols=used_cols, tile_offset=tile_offset,
            weights=weights,
        ),
        out_shape=(shape,) * 5,
        in_specs=[spec] * 11,
        out_specs=(spec,) * 5,
        name="section_step",
    )(*fields, keep, mirror, lift, *initial)


def halo_box(fields, wide_x, wide_y, place, count, padded_shape):
    lon_count = lax.axis_size("lon")
    west = lax.ppermute(
        fields[:, :, -wide_x:], "lon", [(i, (i + 1) % lon_count) for i in range(lon_count)]
    )
    east = lax.ppermute(
        fields[:, :, :wide_x], "lon", [((i + 1) % lon_count, i) for i in range(lon_count)]
    )
    wide = jnp.concatenate([west, fields, east], axis=2)
    above = passed_along(wide[:, -wide_y:], "lat", 1)
    below = passed_along(wide[:, :wide_y], "lat", -1)
    above = jnp.where(place == 0, wide[:, wide_y - 1 :: -1], above)
    below = jnp.where(place == count - 1, wide[:, : -wide_y - 1 : -1], below)
    box = jnp.concatenate([above, wide, below], axis=1)
    return pad_to(box, padded_shape)


def pad_to(values, shape):
    widths = [(0, 0)] * (values.ndim - 2) + [
        (0, want - have) for want, have in zip(shape, values.shape[-2:])
    ]
    return jnp.pad(values, widths)


def wall_mirrored(values, halo, place, count, rows):
    top = jnp.concatenate([values[..., 2 * halo - 1 : halo - 1 : -1, :], values[..., halo:, :]], axis=-2)
    values = jnp.where(place == 0, top, values)
    bottom = jnp.concatenate(
        [
            values[..., : rows - halo, :],
            values[..., rows - halo - 1 : rows - 2 * halo - 1 : -1, :],
            values[..., rows:, :],
        ],
        axis=-2,
    )
    return jnp.where(place == count - 1, bottom, values)


class Geometry:
    def __init__(self, out_rows, out_cols, halo_y, halo_x):
        self.box_rows = out_rows + 2 * halo_y
        self.box_cols = out_cols + 2 * halo_x
        self.first_row = (halo_y - 2) // 8 * 8
        self.rows = -(-(halo_y + out_rows + 2 - self.first_row) // 8) * 8
        self.padded = (
            max(-(-self.box_rows // 8) * 8, self.first_row + self.rows),
            -(-self.box_cols // 128) * 128,
        )
        self.offset = (halo_y, halo_x)

    def masks(self, region_above, place, count, tile_rows):
        box_row = lax.broadcasted_iota(jnp.int32, self.padded, 0)
        global_row = place * tile_rows - region_above - self.offset[0] + box_row
        inside = (global_row >= 0) & (global_row < count * tile_rows) & (box_row < self.box_rows)
        wrapped_row = lax.broadcasted_iota(jnp.int32, (self.rows, self.padded[1]), 0)
        tile_row = jnp.where(wrapped_row >= self.rows - 2, wrapped_row - self.rows, wrapped_row)
        tile_row = tile_row - region_above
        top = place == 0
        bottom = place == count - 1
        mirror = jnp.where(
            top & (tile_row == -1), 1,
            jnp.where(top & (tile_row == -2), 2,
            jnp.where(bottom & (tile_row == tile_rows), 3,
            jnp.where(bottom & (tile_row == tile_rows + 1), 4, 0))),
        ).astype(jnp.int32)
        return inside.astype(jnp.float32), mirror


def local(surface, momentum_x, momentum_y, water_depth, wet_mask, slide_cells, slide_rate):
    wet_float = wet_mask.astype(jnp.float32)
    place = lax.axis_index("lat")
    count = lax.axis_size("lat")
    tile_rows, tile_cols = surface.shape
    wide_x = WINDOW_LON + 2
    wide_y = WINDOW_LAT + 2
    lift = (
        jnp.zeros((tile_rows * tile_cols,), jnp.float32)
        .at[slide_cells.reshape(-1)]
        .add(slide_rate.reshape(-1))
        .reshape(tile_rows, tile_cols)
    )
    ring = Geometry(tile_rows + 2 * wide_y, tile_cols + 2 * wide_x, wide_y, wide_x)
    plain = Geometry(tile_rows, tile_cols, wide_y, wide_x)
    ring_keep, ring_mirror = ring.masks(wide_y, place, count, tile_rows)
    plain_keep, plain_mirror = plain.masks(0, place, count, tile_rows)
    initial = (surface, momentum_x, momentum_y)

    big = halo_box(
        jnp.stack([surface, momentum_x, momentum_y, water_depth, wet_float, lift]),
        2 * wide_x, 2 * wide_y, place, count, ring.padded,
    )
    ring_state = ring_step(
        tuple(big[k] for k in range(6)), ring_keep, ring_mirror, plain.padded,
        ring.first_row, ring.box_cols, ring.offset,
    )
    box = wall_mirrored(jnp.stack(ring_state[:3]), wide_y, place, count, plain.box_rows)
    depth_box, wet_box = ring_state[3], ring_state[4]
    for first, second in ((0.75, 0.25), (1.0 / 3.0, 2.0 / 3.0)):
        if box is None:
            box = halo_box(jnp.stack(list(current)), wide_x, wide_y, place, count, plain.padded)
        next_surface, next_east, next_north, velocity_u, velocity_v = section_step(
            (box[0], box[1], box[2], depth_box, wet_box), plain_keep, plain_mirror, lift, initial,
            plain.first_row, plain.box_cols, plain.offset, (first, second),
        )
        current = (next_surface, next_east, next_north)
        box = None
    return (current[0], current[1], current[2], velocity_u, velocity_v)


def solution(mesh):
    in_specs = (P("lat", "lon"),) * 7
    out_specs = (P("lat", "lon"),) * 5
    return jax.shard_map(local, mesh=mesh, in_specs=in_specs, out_specs=out_specs, check_vma=False)
```

```python
import jax
import jax.numpy as jnp
from jax import lax
from jax.sharding import PartitionSpec as P
from jax.experimental import pallas as pl
from jax.experimental.pallas import tpu as pltpu

GRAVITY = 1.0
LON_SPACING = 0.5
LAT_SPACING = 0.6
TIME_STEP = 0.1
WINDOW_LON = 40
WINDOW_LAT = 32
PCR_STEPS = 6


def shifted(block, axis, distance):
    devices = range(lax.axis_size(axis))
    route = [((i - distance) % len(devices), i) for i in devices]
    return lax.ppermute(block, axis, route)


def passed_along(x, axis, by):
    peers = lax.axis_size(axis)
    pairs = [(i, i + by) for i in range(peers) if 0 <= i + by < peers]
    return lax.ppermute(x, axis, pairs)


def extended(cells, sides, width, closed):
    for axis, dim in sides:
        count = lax.axis_size(axis)
        ends = count if closed else count - 1
        head = lax.slice_in_dim(cells, 0, width, axis=dim)
        tail = lax.slice_in_dim(cells, cells.shape[dim] - width, cells.shape[dim], axis=dim)
        cells = jnp.concatenate(
            [
                lax.ppermute(tail, axis, [(i, (i + 1) % count) for i in range(ends)]),
                cells,
                lax.ppermute(head, axis, [((i + 1) % count, i) for i in range(ends)]),
            ],
            axis=dim,
        )
    return cells


def slab_of(values, start, stop, along_axis):
    return lax.slice_in_dim(values, start, stop, axis=along_axis)


def limited(former, latter):
    return jnp.maximum(jnp.minimum(former, latter), 0.0) + jnp.minimum(
        jnp.maximum(former, latter), 0.0
    )


def face_states(values, along_axis):
    length = values.shape[along_axis]
    jumps = slab_of(values, 1, length, along_axis) - slab_of(values, 0, length - 1, along_axis)
    slopes = limited(
        slab_of(jumps, 0, length - 2, along_axis), slab_of(jumps, 1, length - 1, along_axis)
    )
    left_state = slab_of(values, 1, length - 2, along_axis) + 0.5 * slab_of(
        slopes, 0, length - 3, along_axis
    )
    right_state = slab_of(values, 2, length - 1, along_axis) - 0.5 * slab_of(
        slopes, 1, length - 2, along_axis
    )
    return (left_state, right_state)


def wave_flux(
    surface_left,
    surface_right,
    normal_left,
    normal_right,
    tangent_left,
    tangent_right,
    face_depth,
    opened,
):
    height_left = surface_left + face_depth
    height_right = surface_right + face_depth
    celerity_left = jnp.sqrt(GRAVITY * height_left)
    celerity_right = jnp.sqrt(GRAVITY * height_right)
    slowest = jnp.minimum(
        jnp.minimum(normal_left - celerity_left, normal_right - celerity_right), 0.0
    )
    fastest = jnp.maximum(
        jnp.maximum(normal_left + celerity_left, normal_right + celerity_right), 0.0
    )
    spread = fastest - slowest
    product = slowest * fastest
    mass_left = height_left * normal_left
    mass_right = height_right * normal_right
    push_left = mass_left * normal_left + GRAVITY * (
        0.5 * surface_left * surface_left + face_depth * surface_left
    )
    push_right = mass_right * normal_right + GRAVITY * (
        0.5 * surface_right * surface_right + face_depth * surface_right
    )
    carry_left = mass_left * tangent_left
    carry_right = mass_right * tangent_right
    mass_flux = (
        opened
        * (fastest * mass_left - slowest * mass_right + product * (surface_right - surface_left))
        / spread
    )
    push_flux = (
        opened
        * (fastest * push_left - slowest * push_right + product * (mass_right - mass_left))
        / spread
    )
    carry_flux = (
        opened
        * (
            fastest * carry_left
            - slowest * carry_right
            + product * (height_right * tangent_right - height_left * tangent_left)
        )
        / spread
    )
    return (mass_flux, push_flux, carry_flux)


def tendencies(across, along):
    width = across[0].shape[1] - 4
    row_count = along[0].shape[0] - 4
    surface_pair = face_states(across[0], 1)
    east_pair = face_states(across[1], 1)
    north_pair = face_states(across[2], 1)
    depth_lon = 0.5 * (across[3][:, 1 : width + 2] + across[3][:, 2 : width + 3])
    open_lon = across[4][:, 1 : width + 2] * across[4][:, 2 : width + 3]
    mass_lon, push_lon, carry_lon = wave_flux(
        surface_pair[0],
        surface_pair[1],
        east_pair[0],
        east_pair[1],
        north_pair[0],
        north_pair[1],
        depth_lon,
        open_lon,
    )
    surface_pair = face_states(along[0], 0)
    east_pair = face_states(along[1], 0)
    north_pair = face_states(along[2], 0)
    depth_lat = 0.5 * (along[3][1 : row_count + 2] + along[3][2 : row_count + 3])
    open_lat = along[4][1 : row_count + 2] * along[4][2 : row_count + 3]
    mass_lat, push_lat, carry_lat = wave_flux(
        surface_pair[0],
        surface_pair[1],
        north_pair[0],
        north_pair[1],
        east_pair[0],
        east_pair[1],
        depth_lat,
        open_lat,
    )
    surface_mid = across[0][:, 2 : width + 2]
    wet_mid = across[4][:, 2 : width + 2]
    rate_surface = (
        -(mass_lon[:, 1:] - mass_lon[:, :-1]) / LON_SPACING
        - (mass_lat[1:] - mass_lat[:-1]) / LAT_SPACING
    )
    source_east = GRAVITY * surface_mid * (depth_lon[:, 1:] - depth_lon[:, :-1]) / LON_SPACING
    source_north = GRAVITY * surface_mid * (depth_lat[1:] - depth_lat[:-1]) / LAT_SPACING
    rate_east = wet_mid * (
        source_east
        - (push_lon[:, 1:] - push_lon[:, :-1]) / LON_SPACING
        - (carry_lat[1:] - carry_lat[:-1]) / LAT_SPACING
    )
    rate_north = wet_mid * (
        source_north
        - (carry_lon[:, 1:] - carry_lon[:, :-1]) / LON_SPACING
        - (push_lat[1:] - push_lat[:-1]) / LAT_SPACING
    )
    return (rate_surface, rate_east, rate_north)


def from_below(values, stride, along_axis, filler):
    length = values.shape[along_axis]
    padding = jnp.full_like(slab_of(values, 0, stride, along_axis), filler)
    return jnp.concatenate([padding, slab_of(values, 0, length - stride, along_axis)], along_axis)


def from_above(values, stride, along_axis, filler):
    length = values.shape[along_axis]
    padding = jnp.full_like(slab_of(values, 0, stride, along_axis), filler)
    return jnp.concatenate([slab_of(values, stride, length, along_axis), padding], along_axis)


def reduce_lines(lower_band, main_band, upper_band, rights, along_axis):
    length = rights.shape[along_axis]
    position = lax.broadcasted_iota(jnp.int32, rights.shape, along_axis)
    stride = 1
    for _ in range(PCR_STEPS):
        def from_lower(values, fill):
            return jnp.where(position >= stride, pltpu.roll(values, stride, along_axis), fill)

        def from_upper(values, fill):
            return jnp.where(
                position < length - stride, pltpu.roll(values, length - stride, along_axis), fill
            )

        below = [from_lower(band, fill) for band, fill in
                 ((lower_band, 0.0), (main_band, 1.0), (upper_band, 0.0), (rights, 0.0))]
        above = [from_upper(band, fill) for band, fill in
                 ((lower_band, 0.0), (main_band, 1.0), (upper_band, 0.0), (rights, 0.0))]
        weight_below = lower_band / below[1]
        weight_above = upper_band / above[1]
        new_lower = -weight_below * below[0]
        new_main = main_band - weight_below * below[2] - weight_above * above[0]
        new_upper = -weight_above * above[2]
        rights = rights - weight_below * below[3] - weight_above * above[3]
        lower_band, main_band, upper_band = new_lower, new_main, new_upper
        stride = stride * 2
    return rights / main_band


def tendency_body(surface_ref, east_ref, north_ref, depth_ref, wet_ref, keep_ref, mirror_ref,
                  first_row, used_cols, tile_offset):
    rows, cols = mirror_ref.shape
    depth = depth_ref[pl.ds(first_row, rows), :]
    surface = surface_ref[pl.ds(first_row, rows), :]
    coef = depth * depth / (3.0 * LON_SPACING * LON_SPACING)
    keep = lax.broadcasted_iota(jnp.int32, depth.shape, 1) < used_cols
    rights = east_ref[pl.ds(first_row, rows), :] / (depth + surface)
    east_raw = reduce_lines(
        jnp.where(keep, -coef, 0.0),
        jnp.where(keep, 1.0 + 2.0 * coef, 1.0),
        jnp.where(keep, -coef, 0.0),
        jnp.where(keep, rights, 0.0),
        1,
    )
    full_depth = depth_ref[...]
    coef = full_depth * full_depth / (3.0 * LAT_SPACING * LAT_SPACING)
    keep = keep_ref[...] > 0.0
    rights = north_ref[...] / (full_depth + surface_ref[...])
    north_raw = reduce_lines(
        jnp.where(keep, -coef, 0.0),
        jnp.where(keep, 1.0 + 2.0 * coef, 1.0),
        jnp.where(keep, -coef, 0.0),
        jnp.where(keep, rights, 0.0),
        0,
    )[first_row : first_row + rows]

    def wrapped(values):
        values = pltpu.roll(values, rows - (tile_offset[0] - first_row), 0)
        return pltpu.roll(values, cols - tile_offset[1], 1)

    wet = wrapped(wet_ref[pl.ds(first_row, rows), :])
    surface = wrapped(surface)
    depth = wrapped(depth)
    velocity_u = wet * wrapped(east_raw)
    velocity_v = wet * wrapped(north_raw)
    mirror = mirror_ref[...]
    for code, shift in ((1, rows - 1), (2, rows - 3), (3, 1), (4, 3)):
        velocity_v = jnp.where(mirror == code, -pltpu.roll(velocity_v, shift, 0), velocity_v)

    def east_of(values):
        return pltpu.roll(values, cols - 1, 1)

    def west_of(values):
        return pltpu.roll(values, 1, 1)

    def north_of(values):
        return pltpu.roll(values, rows - 1, 0)

    def south_of(values):
        return pltpu.roll(values, 1, 0)

    def face_pair(values, later, earlier):
        jump = later(values) - values
        slope = limited(earlier(jump), jump)
        return values + 0.5 * slope, later(values - 0.5 * slope)

    surface_pair = face_pair(surface, east_of, west_of)
    east_pair = face_pair(velocity_u, east_of, west_of)
    north_pair = face_pair(velocity_v, east_of, west_of)
    depth_lon = 0.5 * (depth + east_of(depth))
    open_lon = wet * east_of(wet)
    mass_lon, push_lon, carry_lon = wave_flux(
        surface_pair[0], surface_pair[1], east_pair[0], east_pair[1],
        north_pair[0], north_pair[1], depth_lon, open_lon,
    )
    surface_pair = face_pair(surface, north_of, south_of)
    east_pair = face_pair(velocity_u, north_of, south_of)
    north_pair = face_pair(velocity_v, north_of, south_of)
    depth_lat = 0.5 * (depth + north_of(depth))
    open_lat = wet * north_of(wet)
    mass_lat, push_lat, carry_lat = wave_flux(
        surface_pair[0], surface_pair[1], north_pair[0], north_pair[1],
        east_pair[0], east_pair[1], depth_lat, open_lat,
    )
    rate_surface = (
        -(mass_lon - west_of(mass_lon)) / LON_SPACING - (mass_lat - south_of(mass_lat)) / LAT_SPACING
    )
    source_east = GRAVITY * surface * (depth_lon - west_of(depth_lon)) / LON_SPACING
    source_north = GRAVITY * surface * (depth_lat - south_of(depth_lat)) / LAT_SPACING
    rate_east = wet * (
        source_east
        - (push_lon - west_of(push_lon)) / LON_SPACING
        - (carry_lat - south_of(carry_lat)) / LAT_SPACING
    )
    rate_north = wet * (
        source_north
        - (carry_lon - west_of(carry_lon)) / LON_SPACING
        - (push_lat - south_of(push_lat)) / LAT_SPACING
    )
    return (rate_surface, rate_east, rate_north), (surface, velocity_u, velocity_v), wrapped


def section_kernel(surface_ref, east_ref, north_ref, depth_ref, wet_ref, keep_ref, mirror_ref,
                   lift_ref, start_surface, start_east, start_north,
                   next_surface, next_east, next_north, east_out, north_out, *,
                   first_row, used_cols, tile_offset, weights):
    tile_rows, tile_cols = lift_ref.shape
    rates, (surface, velocity_u, velocity_v), wrapped = tendency_body(
        surface_ref, east_ref, north_ref, depth_ref, wet_ref, keep_ref, mirror_ref,
        first_row, used_cols, tile_offset,
    )
    rows = mirror_ref.shape[0]
    nows = (
        surface,
        wrapped(east_ref[pl.ds(first_row, rows), :]),
        wrapped(north_ref[pl.ds(first_row, rows), :]),
    )
    first, second = weights
    rates = (
        rates[0][:tile_rows, :tile_cols] + lift_ref[...],
        rates[1][:tile_rows, :tile_cols],
        rates[2][:tile_rows, :tile_cols],
    )
    for out, start, now, rate in zip(
        (next_surface, next_east, next_north),
        (start_surface, start_east, start_north),
        nows,
        rates,
    ):
        out[...] = first * start[...] + second * (now[:tile_rows, :tile_cols] + TIME_STEP * rate)
    east_out[...] = velocity_u[:tile_rows, :tile_cols]
    north_out[...] = velocity_v[:tile_rows, :tile_cols]


def ring_kernel(surface_ref, east_ref, north_ref, depth_ref, wet_ref, keep_ref, mirror_ref,
                lift_ref, next_surface, next_east, next_north, depth_out, wet_out, *,
                first_row, used_cols, tile_offset):
    rows = mirror_ref.shape[0]
    out_rows, out_cols = next_surface.shape
    rates, (surface, _, _), wrapped = tendency_body(
        surface_ref, east_ref, north_ref, depth_ref, wet_ref, keep_ref, mirror_ref,
        first_row, used_cols, tile_offset,
    )
    lift = wrapped(lift_ref[pl.ds(first_row, rows), :])
    nows = (
        surface,
        wrapped(east_ref[pl.ds(first_row, rows), :]),
        wrapped(north_ref[pl.ds(first_row, rows), :]),
    )
    rates = (rates[0] + lift, rates[1], rates[2])
    for out, now, rate in zip((next_surface, next_east, next_north), nows, rates):
        out[...] = (0.0 * now + 1.0 * (now + TIME_STEP * rate))[:out_rows, :out_cols]
    depth_out[...] = wrapped(depth_ref[pl.ds(first_row, rows), :])[:out_rows, :out_cols]
    wet_out[...] = wrapped(wet_ref[pl.ds(first_row, rows), :])[:out_rows, :out_cols]


def ring_step(fields, keep, mirror, out_shape, first_row, used_cols, tile_offset):
    spec = pl.BlockSpec(memory_space=pltpu.VMEM)
    shape = jax.ShapeDtypeStruct(out_shape, jnp.float32)
    return pl.pallas_call(
        lambda *refs: ring_kernel(
            *refs, first_row=first_row, used_cols=used_cols, tile_offset=tile_offset
        ),
        out_shape=(shape,) * 5,
        in_specs=[spec] * 8,
        out_specs=(spec,) * 5,
        name="ring_step",
    )(*fields[:5], keep, mirror, fields[5])


def section_step(fields, keep, mirror, lift, initial, first_row, used_cols, tile_offset,
                 weights):
    spec = pl.BlockSpec(memory_space=pltpu.VMEM)
    shape = jax.ShapeDtypeStruct(lift.shape, jnp.float32)
    return pl.pallas_call(
        lambda *refs: section_kernel(
            *refs, first_row=first_row, used_cols=used_cols, tile_offset=tile_offset,
            weights=weights,
        ),
        out_shape=(shape,) * 5,
        in_specs=[spec] * 11,
        out_specs=(spec,) * 5,
        name="section_step",
    )(*fields, keep, mirror, lift, *initial)


def halo_box(fields, wide_x, wide_y, place, count, padded_shape):
    lon_count = lax.axis_size("lon")
    west = lax.ppermute(
        jnp.stack([field[:, -wide_x:] for field in fields]), "lon",
        [(i, (i + 1) % lon_count) for i in range(lon_count)],
    )
    east = lax.ppermute(
        jnp.stack([field[:, :wide_x] for field in fields]), "lon",
        [((i + 1) % lon_count, i) for i in range(lon_count)],
    )
    wide = [jnp.concatenate([west[k], field, east[k]], axis=1) for k, field in enumerate(fields)]
    above = passed_along(jnp.stack([field[-wide_y:] for field in wide]), "lat", 1)
    below = passed_along(jnp.stack([field[:wide_y] for field in wide]), "lat", -1)
    boxes = []
    for k, field in enumerate(wide):
        top = jnp.where(place == 0, field[wide_y - 1 :: -1], above[k])
        bottom = jnp.where(place == count - 1, field[: -wide_y - 1 : -1], below[k])
        boxes.append(pad_to(jnp.concatenate([top, field, bottom], axis=0), padded_shape))
    return boxes


def pad_to(values, shape):
    widths = [(0, 0)] * (values.ndim - 2) + [
        (0, want - have) for want, have in zip(shape, values.shape[-2:])
    ]
    return jnp.pad(values, widths)


def wall_mirrored(values, halo, place, count, rows):
    top = jnp.concatenate([values[..., 2 * halo - 1 : halo - 1 : -1, :], values[..., halo:, :]], axis=-2)
    values = jnp.where(place == 0, top, values)
    bottom = jnp.concatenate(
        [
            values[..., : rows - halo, :],
            values[..., rows - halo - 1 : rows - 2 * halo - 1 : -1, :],
            values[..., rows:, :],
        ],
        axis=-2,
    )
    return jnp.where(place == count - 1, bottom, values)


class Geometry:
    def __init__(self, out_rows, out_cols, halo_y, halo_x):
        self.box_rows = out_rows + 2 * halo_y
        self.box_cols = out_cols + 2 * halo_x
        self.first_row = (halo_y - 2) // 8 * 8
        self.rows = -(-(halo_y + out_rows + 2 - self.first_row) // 8) * 8
        self.padded = (
            max(-(-self.box_rows // 8) * 8, self.first_row + self.rows),
            -(-self.box_cols // 128) * 128,
        )
        self.offset = (halo_y, halo_x)

    def masks(self, region_above, place, count, tile_rows):
        box_row = lax.broadcasted_iota(jnp.int32, self.padded, 0)
        global_row = place * tile_rows - region_above - self.offset[0] + box_row
        inside = (global_row >= 0) & (global_row < count * tile_rows) & (box_row < self.box_rows)
        wrapped_row = lax.broadcasted_iota(jnp.int32, (self.rows, self.padded[1]), 0)
        tile_row = jnp.where(wrapped_row >= self.rows - 2, wrapped_row - self.rows, wrapped_row)
        tile_row = tile_row - region_above
        top = place == 0
        bottom = place == count - 1
        mirror = jnp.where(
            top & (tile_row == -1), 1,
            jnp.where(top & (tile_row == -2), 2,
            jnp.where(bottom & (tile_row == tile_rows), 3,
            jnp.where(bottom & (tile_row == tile_rows + 1), 4, 0))),
        ).astype(jnp.int32)
        return inside.astype(jnp.float32), mirror


def local(surface, momentum_x, momentum_y, water_depth, wet_mask, slide_cells, slide_rate):
    wet_float = wet_mask.astype(jnp.float32)
    place = lax.axis_index("lat")
    count = lax.axis_size("lat")
    tile_rows, tile_cols = surface.shape
    wide_x = WINDOW_LON + 2
    wide_y = WINDOW_LAT + 2
    lift = (
        jnp.zeros((tile_rows * tile_cols,), jnp.float32)
        .at[slide_cells.reshape(-1)]
        .add(slide_rate.reshape(-1))
        .reshape(tile_rows, tile_cols)
    )
    ring = Geometry(tile_rows + 2 * wide_y, tile_cols + 2 * wide_x, wide_y, wide_x)
    plain = Geometry(tile_rows, tile_cols, wide_y, wide_x)
    ring_keep, ring_mirror = ring.masks(wide_y, place, count, tile_rows)
    plain_keep, plain_mirror = plain.masks(0, place, count, tile_rows)
    initial = (surface, momentum_x, momentum_y)

    big = halo_box(
        [surface, momentum_x, momentum_y, water_depth, wet_float, lift],
        2 * wide_x, 2 * wide_y, place, count, ring.padded,
    )
    ring_state = ring_step(
        tuple(big[k] for k in range(6)), ring_keep, ring_mirror, plain.padded,
        ring.first_row, ring.box_cols, ring.offset,
    )
    box = wall_mirrored(jnp.stack(ring_state[:3]), wide_y, place, count, plain.box_rows)
    depth_box, wet_box = ring_state[3], ring_state[4]
    for first, second in ((0.75, 0.25), (1.0 / 3.0, 2.0 / 3.0)):
        if box is None:
            box = halo_box(list(current), wide_x, wide_y, place, count, plain.padded)
        next_surface, next_east, next_north, velocity_u, velocity_v = section_step(
            (box[0], box[1], box[2], depth_box, wet_box), plain_keep, plain_mirror, lift, initial,
            plain.first_row, plain.box_cols, plain.offset, (first, second),
        )
        current = (next_surface, next_east, next_north)
        box = None
    return (current[0], current[1], current[2], velocity_u, velocity_v)


def solution(mesh):
    in_specs = (P("lat", "lon"),) * 7
    out_specs = (P("lat", "lon"),) * 5
    return jax.shard_map(local, mesh=mesh, in_specs=in_specs, out_specs=out_specs, check_vma=False)
```

```python
import jax
import jax.numpy as jnp
from jax import lax
from jax.sharding import PartitionSpec as P
from jax.experimental import pallas as pl
from jax.experimental.pallas import tpu as pltpu

GRAVITY = 1.0
LON_SPACING = 0.5
LAT_SPACING = 0.6
TIME_STEP = 0.1
WINDOW_LON = 40
WINDOW_LAT = 32
PCR_STEPS = 6


def shifted(block, axis, distance):
    devices = range(lax.axis_size(axis))
    route = [((i - distance) % len(devices), i) for i in devices]
    return lax.ppermute(block, axis, route)


def passed_along(x, axis, by):
    peers = lax.axis_size(axis)
    pairs = [(i, i + by) for i in range(peers) if 0 <= i + by < peers]
    return lax.ppermute(x, axis, pairs)


def extended(cells, sides, width, closed):
    for axis, dim in sides:
        count = lax.axis_size(axis)
        ends = count if closed else count - 1
        head = lax.slice_in_dim(cells, 0, width, axis=dim)
        tail = lax.slice_in_dim(cells, cells.shape[dim] - width, cells.shape[dim], axis=dim)
        cells = jnp.concatenate(
            [
                lax.ppermute(tail, axis, [(i, (i + 1) % count) for i in range(ends)]),
                cells,
                lax.ppermute(head, axis, [((i + 1) % count, i) for i in range(ends)]),
            ],
            axis=dim,
        )
    return cells


def slab_of(values, start, stop, along_axis):
    return lax.slice_in_dim(values, start, stop, axis=along_axis)


def limited(former, latter):
    return jnp.maximum(jnp.minimum(former, latter), 0.0) + jnp.minimum(
        jnp.maximum(former, latter), 0.0
    )


def face_states(values, along_axis):
    length = values.shape[along_axis]
    jumps = slab_of(values, 1, length, along_axis) - slab_of(values, 0, length - 1, along_axis)
    slopes = limited(
        slab_of(jumps, 0, length - 2, along_axis), slab_of(jumps, 1, length - 1, along_axis)
    )
    left_state = slab_of(values, 1, length - 2, along_axis) + 0.5 * slab_of(
        slopes, 0, length - 3, along_axis
    )
    right_state = slab_of(values, 2, length - 1, along_axis) - 0.5 * slab_of(
        slopes, 1, length - 2, along_axis
    )
    return (left_state, right_state)


def wave_flux(
    surface_left,
    surface_right,
    normal_left,
    normal_right,
    tangent_left,
    tangent_right,
    face_depth,
    opened,
):
    height_left = surface_left + face_depth
    height_right = surface_right + face_depth
    celerity_left = jnp.sqrt(GRAVITY * height_left)
    celerity_right = jnp.sqrt(GRAVITY * height_right)
    slowest = jnp.minimum(
        jnp.minimum(normal_left - celerity_left, normal_right - celerity_right), 0.0
    )
    fastest = jnp.maximum(
        jnp.maximum(normal_left + celerity_left, normal_right + celerity_right), 0.0
    )
    spread = fastest - slowest
    product = slowest * fastest
    mass_left = height_left * normal_left
    mass_right = height_right * normal_right
    push_left = mass_left * normal_left + GRAVITY * (
        0.5 * surface_left * surface_left + face_depth * surface_left
    )
    push_right = mass_right * normal_right + GRAVITY * (
        0.5 * surface_right * surface_right + face_depth * surface_right
    )
    carry_left = mass_left * tangent_left
    carry_right = mass_right * tangent_right
    mass_flux = (
        opened
        * (fastest * mass_left - slowest * mass_right + product * (surface_right - surface_left))
        / spread
    )
    push_flux = (
        opened
        * (fastest * push_left - slowest * push_right + product * (mass_right - mass_left))
        / spread
    )
    carry_flux = (
        opened
        * (
            fastest * carry_left
            - slowest * carry_right
            + product * (height_right * tangent_right - height_left * tangent_left)
        )
        / spread
    )
    return (mass_flux, push_flux, carry_flux)


def tendencies(across, along):
    width = across[0].shape[1] - 4
    row_count = along[0].shape[0] - 4
    surface_pair = face_states(across[0], 1)
    east_pair = face_states(across[1], 1)
    north_pair = face_states(across[2], 1)
    depth_lon = 0.5 * (across[3][:, 1 : width + 2] + across[3][:, 2 : width + 3])
    open_lon = across[4][:, 1 : width + 2] * across[4][:, 2 : width + 3]
    mass_lon, push_lon, carry_lon = wave_flux(
        surface_pair[0],
        surface_pair[1],
        east_pair[0],
        east_pair[1],
        north_pair[0],
        north_pair[1],
        depth_lon,
        open_lon,
    )
    surface_pair = face_states(along[0], 0)
    east_pair = face_states(along[1], 0)
    north_pair = face_states(along[2], 0)
    depth_lat = 0.5 * (along[3][1 : row_count + 2] + along[3][2 : row_count + 3])
    open_lat = along[4][1 : row_count + 2] * along[4][2 : row_count + 3]
    mass_lat, push_lat, carry_lat = wave_flux(
        surface_pair[0],
        surface_pair[1],
        north_pair[0],
        north_pair[1],
        east_pair[0],
        east_pair[1],
        depth_lat,
        open_lat,
    )
    surface_mid = across[0][:, 2 : width + 2]
    wet_mid = across[4][:, 2 : width + 2]
    rate_surface = (
        -(mass_lon[:, 1:] - mass_lon[:, :-1]) / LON_SPACING
        - (mass_lat[1:] - mass_lat[:-1]) / LAT_SPACING
    )
    source_east = GRAVITY * surface_mid * (depth_lon[:, 1:] - depth_lon[:, :-1]) / LON_SPACING
    source_north = GRAVITY * surface_mid * (depth_lat[1:] - depth_lat[:-1]) / LAT_SPACING
    rate_east = wet_mid * (
        source_east
        - (push_lon[:, 1:] - push_lon[:, :-1]) / LON_SPACING
        - (carry_lat[1:] - carry_lat[:-1]) / LAT_SPACING
    )
    rate_north = wet_mid * (
        source_north
        - (carry_lon[:, 1:] - carry_lon[:, :-1]) / LON_SPACING
        - (push_lat[1:] - push_lat[:-1]) / LAT_SPACING
    )
    return (rate_surface, rate_east, rate_north)


def from_below(values, stride, along_axis, filler):
    length = values.shape[along_axis]
    padding = jnp.full_like(slab_of(values, 0, stride, along_axis), filler)
    return jnp.concatenate([padding, slab_of(values, 0, length - stride, along_axis)], along_axis)


def from_above(values, stride, along_axis, filler):
    length = values.shape[along_axis]
    padding = jnp.full_like(slab_of(values, 0, stride, along_axis), filler)
    return jnp.concatenate([slab_of(values, stride, length, along_axis), padding], along_axis)


def reduce_lines(lower_band, main_band, upper_band, rights, along_axis):
    length = rights.shape[along_axis]
    position = lax.broadcasted_iota(jnp.int32, rights.shape, along_axis)
    stride = 1
    for _ in range(PCR_STEPS):
        def from_lower(values, fill):
            return jnp.where(position >= stride, pltpu.roll(values, stride, along_axis), fill)

        def from_upper(values, fill):
            return jnp.where(
                position < length - stride, pltpu.roll(values, length - stride, along_axis), fill
            )

        below = [from_lower(band, fill) for band, fill in
                 ((lower_band, 0.0), (main_band, 1.0), (upper_band, 0.0), (rights, 0.0))]
        above = [from_upper(band, fill) for band, fill in
                 ((lower_band, 0.0), (main_band, 1.0), (upper_band, 0.0), (rights, 0.0))]
        weight_below = lower_band / below[1]
        weight_above = upper_band / above[1]
        new_lower = -weight_below * below[0]
        new_main = main_band - weight_below * below[2] - weight_above * above[0]
        new_upper = -weight_above * above[2]
        rights = rights - weight_below * below[3] - weight_above * above[3]
        lower_band, main_band, upper_band = new_lower, new_main, new_upper
        stride = stride * 2
    return rights / main_band


def tendency_body(surface_ref, east_ref, north_ref, depth_ref, wet_ref, keep_ref, mirror_ref,
                  first_row, used_cols, tile_offset):
    rows, cols = mirror_ref.shape
    depth = depth_ref[pl.ds(first_row, rows), :]
    surface = surface_ref[pl.ds(first_row, rows), :]
    coef = depth * depth / (3.0 * LON_SPACING * LON_SPACING)
    keep = lax.broadcasted_iota(jnp.int32, depth.shape, 1) < used_cols
    rights = east_ref[pl.ds(first_row, rows), :] / (depth + surface)
    east_raw = reduce_lines(
        jnp.where(keep, -coef, 0.0),
        jnp.where(keep, 1.0 + 2.0 * coef, 1.0),
        jnp.where(keep, -coef, 0.0),
        jnp.where(keep, rights, 0.0),
        1,
    )
    full_depth = depth_ref[...]
    coef = full_depth * full_depth / (3.0 * LAT_SPACING * LAT_SPACING)
    keep = keep_ref[...] > 0.0
    rights = north_ref[...] / (full_depth + surface_ref[...])
    north_raw = reduce_lines(
        jnp.where(keep, -coef, 0.0),
        jnp.where(keep, 1.0 + 2.0 * coef, 1.0),
        jnp.where(keep, -coef, 0.0),
        jnp.where(keep, rights, 0.0),
        0,
    )[first_row : first_row + rows]

    def wrapped(values):
        values = pltpu.roll(values, rows - (tile_offset[0] - first_row), 0)
        return pltpu.roll(values, cols - tile_offset[1], 1)

    wet = wrapped(wet_ref[pl.ds(first_row, rows), :])
    surface = wrapped(surface)
    depth = wrapped(depth)
    velocity_u = wet * wrapped(east_raw)
    velocity_v = wet * wrapped(north_raw)
    mirror = mirror_ref[...]
    for code, shift in ((1, rows - 1), (2, rows - 3), (3, 1), (4, 3)):
        velocity_v = jnp.where(mirror == code, -pltpu.roll(velocity_v, shift, 0), velocity_v)

    def east_of(values):
        return pltpu.roll(values, cols - 1, 1)

    def west_of(values):
        return pltpu.roll(values, 1, 1)

    def north_of(values):
        return pltpu.roll(values, rows - 1, 0)

    def south_of(values):
        return pltpu.roll(values, 1, 0)

    def face_pair(values, later, earlier):
        jump = later(values) - values
        slope = limited(earlier(jump), jump)
        return values + 0.5 * slope, later(values - 0.5 * slope)

    surface_pair = face_pair(surface, east_of, west_of)
    east_pair = face_pair(velocity_u, east_of, west_of)
    north_pair = face_pair(velocity_v, east_of, west_of)
    depth_lon = 0.5 * (depth + east_of(depth))
    open_lon = wet * east_of(wet)
    mass_lon, push_lon, carry_lon = wave_flux(
        surface_pair[0], surface_pair[1], east_pair[0], east_pair[1],
        north_pair[0], north_pair[1], depth_lon, open_lon,
    )
    surface_pair = face_pair(surface, north_of, south_of)
    east_pair = face_pair(velocity_u, north_of, south_of)
    north_pair = face_pair(velocity_v, north_of, south_of)
    depth_lat = 0.5 * (depth + north_of(depth))
    open_lat = wet * north_of(wet)
    mass_lat, push_lat, carry_lat = wave_flux(
        surface_pair[0], surface_pair[1], north_pair[0], north_pair[1],
        east_pair[0], east_pair[1], depth_lat, open_lat,
    )
    rate_surface = (
        -(mass_lon - west_of(mass_lon)) / LON_SPACING - (mass_lat - south_of(mass_lat)) / LAT_SPACING
    )
    source_east = GRAVITY * surface * (depth_lon - west_of(depth_lon)) / LON_SPACING
    source_north = GRAVITY * surface * (depth_lat - south_of(depth_lat)) / LAT_SPACING
    rate_east = wet * (
        source_east
        - (push_lon - west_of(push_lon)) / LON_SPACING
        - (carry_lat - south_of(carry_lat)) / LAT_SPACING
    )
    rate_north = wet * (
        source_north
        - (carry_lon - west_of(carry_lon)) / LON_SPACING
        - (push_lat - south_of(push_lat)) / LAT_SPACING
    )
    return (rate_surface, rate_east, rate_north), (surface, velocity_u, velocity_v), wrapped


def section_kernel(surface_ref, east_ref, north_ref, depth_ref, wet_ref, keep_ref, mirror_ref,
                   lift_ref, start_surface, start_east, start_north,
                   next_surface, next_east, next_north, east_out, north_out, *,
                   first_row, used_cols, tile_offset, weights):
    tile_rows, tile_cols = lift_ref.shape
    rates, (surface, velocity_u, velocity_v), wrapped = tendency_body(
        surface_ref, east_ref, north_ref, depth_ref, wet_ref, keep_ref, mirror_ref,
        first_row, used_cols, tile_offset,
    )
    rows = mirror_ref.shape[0]
    nows = (
        surface,
        wrapped(east_ref[pl.ds(first_row, rows), :]),
        wrapped(north_ref[pl.ds(first_row, rows), :]),
    )
    first, second = weights
    rates = (
        rates[0][:tile_rows, :tile_cols] + lift_ref[...],
        rates[1][:tile_rows, :tile_cols],
        rates[2][:tile_rows, :tile_cols],
    )
    for out, start, now, rate in zip(
        (next_surface, next_east, next_north),
        (start_surface, start_east, start_north),
        nows,
        rates,
    ):
        out[...] = first * start[...] + second * (now[:tile_rows, :tile_cols] + TIME_STEP * rate)
    east_out[...] = velocity_u[:tile_rows, :tile_cols]
    north_out[...] = velocity_v[:tile_rows, :tile_cols]


def ring_kernel(surface_ref, east_ref, north_ref, depth_ref, wet_ref, keep_ref, mirror_ref,
                lift_ref, next_surface, next_east, next_north, depth_out, wet_out, *,
                first_row, used_cols, tile_offset):
    rows = mirror_ref.shape[0]
    out_rows, out_cols = next_surface.shape
    rates, (surface, _, _), wrapped = tendency_body(
        surface_ref, east_ref, north_ref, depth_ref, wet_ref, keep_ref, mirror_ref,
        first_row, used_cols, tile_offset,
    )
    lift = wrapped(lift_ref[pl.ds(first_row, rows), :])
    nows = (
        surface,
        wrapped(east_ref[pl.ds(first_row, rows), :]),
        wrapped(north_ref[pl.ds(first_row, rows), :]),
    )
    rates = (rates[0] + lift, rates[1], rates[2])
    for out, now, rate in zip((next_surface, next_east, next_north), nows, rates):
        out[...] = (0.0 * now + 1.0 * (now + TIME_STEP * rate))[:out_rows, :out_cols]
    depth_out[...] = wrapped(depth_ref[pl.ds(first_row, rows), :])[:out_rows, :out_cols]
    wet_out[...] = wrapped(wet_ref[pl.ds(first_row, rows), :])[:out_rows, :out_cols]


def ring_step(fields, keep, mirror, out_shape, first_row, used_cols, tile_offset):
    spec = pl.BlockSpec(memory_space=pltpu.VMEM)
    shape = jax.ShapeDtypeStruct(out_shape, jnp.float32)
    return pl.pallas_call(
        lambda *refs: ring_kernel(
            *refs, first_row=first_row, used_cols=used_cols, tile_offset=tile_offset
        ),
        out_shape=(shape,) * 5,
        in_specs=[spec] * 8,
        out_specs=(spec,) * 5,
        name="ring_step",
    )(*fields[:5], keep, mirror, fields[5])


def section_step(fields, keep, mirror, lift, initial, first_row, used_cols, tile_offset,
                 weights):
    spec = pl.BlockSpec(memory_space=pltpu.VMEM)
    shape = jax.ShapeDtypeStruct(lift.shape, jnp.float32)
    return pl.pallas_call(
        lambda *refs: section_kernel(
            *refs, first_row=first_row, used_cols=used_cols, tile_offset=tile_offset,
            weights=weights,
        ),
        out_shape=(shape,) * 5,
        in_specs=[spec] * 11,
        out_specs=(spec,) * 5,
        name="section_step",
    )(*fields, keep, mirror, lift, *initial)


def halo_box(fields, wide_x, wide_y, place, count, padded_shape):
    lon_count = lax.axis_size("lon")
    west = lax.ppermute(
        fields[:, :, -wide_x:], "lon", [(i, (i + 1) % lon_count) for i in range(lon_count)]
    )
    east = lax.ppermute(
        fields[:, :, :wide_x], "lon", [((i + 1) % lon_count, i) for i in range(lon_count)]
    )
    wide = jnp.concatenate([west, fields, east], axis=2)
    above = passed_along(wide[:, -wide_y:], "lat", 1)
    below = passed_along(wide[:, :wide_y], "lat", -1)
    above = jnp.where(
        place == 0, jnp.concatenate([above[:, :-2], wide[:, 1:2], wide[:, 0:1]], axis=1), above
    )
    below = jnp.where(
        place == count - 1,
        jnp.concatenate([wide[:, -1:], wide[:, -2:-1], below[:, 2:]], axis=1),
        below,
    )
    box = jnp.concatenate([above, wide, below], axis=1)
    return pad_to(box, padded_shape)


def pad_to(values, shape):
    widths = [(0, 0)] * (values.ndim - 2) + [
        (0, want - have) for want, have in zip(shape, values.shape[-2:])
    ]
    return jnp.pad(values, widths)


def wall_mirrored(values, halo, place, count, rows):
    top = jnp.concatenate(
        [
            values[..., : halo - 2, :],
            values[..., halo + 1 : halo + 2, :],
            values[..., halo : halo + 1, :],
            values[..., halo:, :],
        ],
        axis=-2,
    )
    values = jnp.where(place == 0, top, values)
    bottom = jnp.concatenate(
        [
            values[..., : rows - halo, :],
            values[..., rows - halo - 1 : rows - halo, :],
            values[..., rows - halo - 2 : rows - halo - 1, :],
            values[..., rows - halo + 2 :, :],
        ],
        axis=-2,
    )
    return jnp.where(place == count - 1, bottom, values)


class Geometry:
    def __init__(self, out_rows, out_cols, halo_y, halo_x):
        self.box_rows = out_rows + 2 * halo_y
        self.box_cols = out_cols + 2 * halo_x
        self.first_row = (halo_y - 2) // 8 * 8
        self.rows = -(-(halo_y + out_rows + 2 - self.first_row) // 8) * 8
        self.padded = (
            max(-(-self.box_rows // 8) * 8, self.first_row + self.rows),
            -(-self.box_cols // 128) * 128,
        )
        self.offset = (halo_y, halo_x)

    def masks(self, region_above, place, count, tile_rows):
        box_row = lax.broadcasted_iota(jnp.int32, self.padded, 0)
        global_row = place * tile_rows - region_above - self.offset[0] + box_row
        inside = (global_row >= 0) & (global_row < count * tile_rows) & (box_row < self.box_rows)
        wrapped_row = lax.broadcasted_iota(jnp.int32, (self.rows, self.padded[1]), 0)
        tile_row = jnp.where(wrapped_row >= self.rows - 2, wrapped_row - self.rows, wrapped_row)
        tile_row = tile_row - region_above
        top = place == 0
        bottom = place == count - 1
        mirror = jnp.where(
            top & (tile_row == -1), 1,
            jnp.where(top & (tile_row == -2), 2,
            jnp.where(bottom & (tile_row == tile_rows), 3,
            jnp.where(bottom & (tile_row == tile_rows + 1), 4, 0))),
        ).astype(jnp.int32)
        return inside.astype(jnp.float32), mirror


def local(surface, momentum_x, momentum_y, water_depth, wet_mask, slide_cells, slide_rate):
    wet_float = wet_mask.astype(jnp.float32)
    place = lax.axis_index("lat")
    count = lax.axis_size("lat")
    tile_rows, tile_cols = surface.shape
    wide_x = WINDOW_LON + 2
    wide_y = WINDOW_LAT + 2
    lift = (
        jnp.zeros((tile_rows * tile_cols,), jnp.float32)
        .at[slide_cells.reshape(-1)]
        .add(slide_rate.reshape(-1))
        .reshape(tile_rows, tile_cols)
    )
    ring = Geometry(tile_rows + 2 * wide_y, tile_cols + 2 * wide_x, wide_y, wide_x)
    plain = Geometry(tile_rows, tile_cols, wide_y, wide_x)
    ring_keep, ring_mirror = ring.masks(wide_y, place, count, tile_rows)
    plain_keep, plain_mirror = plain.masks(0, place, count, tile_rows)
    initial = (surface, momentum_x, momentum_y)

    big = halo_box(
        jnp.stack([surface, momentum_x, momentum_y, water_depth, wet_float, lift]),
        2 * wide_x, 2 * wide_y, place, count, ring.padded,
    )
    ring_state = ring_step(
        tuple(big[k] for k in range(6)), ring_keep, ring_mirror, plain.padded,
        ring.first_row, ring.box_cols, ring.offset,
    )
    box = wall_mirrored(jnp.stack(ring_state[:3]), wide_y, place, count, plain.box_rows)
    depth_box, wet_box = ring_state[3], ring_state[4]
    for first, second in ((0.75, 0.25), (1.0 / 3.0, 2.0 / 3.0)):
        if box is None:
            box = halo_box(jnp.stack(list(current)), wide_x, wide_y, place, count, plain.padded)
        next_surface, next_east, next_north, velocity_u, velocity_v = section_step(
            (box[0], box[1], box[2], depth_box, wet_box), plain_keep, plain_mirror, lift, initial,
            plain.first_row, plain.box_cols, plain.offset, (first, second),
        )
        current = (next_surface, next_east, next_north)
        box = None
    return (current[0], current[1], current[2], velocity_u, velocity_v)


def solution(mesh):
    in_specs = (P("lat", "lon"),) * 7
    out_specs = (P("lat", "lon"),) * 5
    return jax.shard_map(local, mesh=mesh, in_specs=in_specs, out_specs=out_specs, check_vma=False)
```

```python
import jax
import jax.numpy as jnp
from jax import lax
from jax.sharding import PartitionSpec as P
from jax.experimental import pallas as pl
from jax.experimental.pallas import tpu as pltpu

GRAVITY = 1.0
LON_SPACING = 0.5
LAT_SPACING = 0.6
TIME_STEP = 0.1
WINDOW_LON = 40
WINDOW_LAT = 32
PCR_STEPS = 6


def shifted(block, axis, distance):
    devices = range(lax.axis_size(axis))
    route = [((i - distance) % len(devices), i) for i in devices]
    return lax.ppermute(block, axis, route)


def passed_along(x, axis, by):
    peers = lax.axis_size(axis)
    pairs = [(i, i + by) for i in range(peers) if 0 <= i + by < peers]
    return lax.ppermute(x, axis, pairs)


def extended(cells, sides, width, closed):
    for axis, dim in sides:
        count = lax.axis_size(axis)
        ends = count if closed else count - 1
        head = lax.slice_in_dim(cells, 0, width, axis=dim)
        tail = lax.slice_in_dim(cells, cells.shape[dim] - width, cells.shape[dim], axis=dim)
        cells = jnp.concatenate(
            [
                lax.ppermute(tail, axis, [(i, (i + 1) % count) for i in range(ends)]),
                cells,
                lax.ppermute(head, axis, [((i + 1) % count, i) for i in range(ends)]),
            ],
            axis=dim,
        )
    return cells


def slab_of(values, start, stop, along_axis):
    return lax.slice_in_dim(values, start, stop, axis=along_axis)


def limited(former, latter):
    return jnp.maximum(jnp.minimum(former, latter), 0.0) + jnp.minimum(
        jnp.maximum(former, latter), 0.0
    )


def face_states(values, along_axis):
    length = values.shape[along_axis]
    jumps = slab_of(values, 1, length, along_axis) - slab_of(values, 0, length - 1, along_axis)
    slopes = limited(
        slab_of(jumps, 0, length - 2, along_axis), slab_of(jumps, 1, length - 1, along_axis)
    )
    left_state = slab_of(values, 1, length - 2, along_axis) + 0.5 * slab_of(
        slopes, 0, length - 3, along_axis
    )
    right_state = slab_of(values, 2, length - 1, along_axis) - 0.5 * slab_of(
        slopes, 1, length - 2, along_axis
    )
    return (left_state, right_state)


def wave_flux(
    surface_left,
    surface_right,
    normal_left,
    normal_right,
    tangent_left,
    tangent_right,
    face_depth,
    opened,
):
    height_left = surface_left + face_depth
    height_right = surface_right + face_depth
    celerity_left = jnp.sqrt(GRAVITY * height_left)
    celerity_right = jnp.sqrt(GRAVITY * height_right)
    slowest = jnp.minimum(
        jnp.minimum(normal_left - celerity_left, normal_right - celerity_right), 0.0
    )
    fastest = jnp.maximum(
        jnp.maximum(normal_left + celerity_left, normal_right + celerity_right), 0.0
    )
    spread = fastest - slowest
    product = slowest * fastest
    mass_left = height_left * normal_left
    mass_right = height_right * normal_right
    push_left = mass_left * normal_left + GRAVITY * (
        0.5 * surface_left * surface_left + face_depth * surface_left
    )
    push_right = mass_right * normal_right + GRAVITY * (
        0.5 * surface_right * surface_right + face_depth * surface_right
    )
    carry_left = mass_left * tangent_left
    carry_right = mass_right * tangent_right
    mass_flux = (
        opened
        * (fastest * mass_left - slowest * mass_right + product * (surface_right - surface_left))
        / spread
    )
    push_flux = (
        opened
        * (fastest * push_left - slowest * push_right + product * (mass_right - mass_left))
        / spread
    )
    carry_flux = (
        opened
        * (
            fastest * carry_left
            - slowest * carry_right
            + product * (height_right * tangent_right - height_left * tangent_left)
        )
        / spread
    )
    return (mass_flux, push_flux, carry_flux)


def tendencies(across, along):
    width = across[0].shape[1] - 4
    row_count = along[0].shape[0] - 4
    surface_pair = face_states(across[0], 1)
    east_pair = face_states(across[1], 1)
    north_pair = face_states(across[2], 1)
    depth_lon = 0.5 * (across[3][:, 1 : width + 2] + across[3][:, 2 : width + 3])
    open_lon = across[4][:, 1 : width + 2] * across[4][:, 2 : width + 3]
    mass_lon, push_lon, carry_lon = wave_flux(
        surface_pair[0],
        surface_pair[1],
        east_pair[0],
        east_pair[1],
        north_pair[0],
        north_pair[1],
        depth_lon,
        open_lon,
    )
    surface_pair = face_states(along[0], 0)
    east_pair = face_states(along[1], 0)
    north_pair = face_states(along[2], 0)
    depth_lat = 0.5 * (along[3][1 : row_count + 2] + along[3][2 : row_count + 3])
    open_lat = along[4][1 : row_count + 2] * along[4][2 : row_count + 3]
    mass_lat, push_lat, carry_lat = wave_flux(
        surface_pair[0],
        surface_pair[1],
        north_pair[0],
        north_pair[1],
        east_pair[0],
        east_pair[1],
        depth_lat,
        open_lat,
    )
    surface_mid = across[0][:, 2 : width + 2]
    wet_mid = across[4][:, 2 : width + 2]
    rate_surface = (
        -(mass_lon[:, 1:] - mass_lon[:, :-1]) / LON_SPACING
        - (mass_lat[1:] - mass_lat[:-1]) / LAT_SPACING
    )
    source_east = GRAVITY * surface_mid * (depth_lon[:, 1:] - depth_lon[:, :-1]) / LON_SPACING
    source_north = GRAVITY * surface_mid * (depth_lat[1:] - depth_lat[:-1]) / LAT_SPACING
    rate_east = wet_mid * (
        source_east
        - (push_lon[:, 1:] - push_lon[:, :-1]) / LON_SPACING
        - (carry_lat[1:] - carry_lat[:-1]) / LAT_SPACING
    )
    rate_north = wet_mid * (
        source_north
        - (carry_lon[:, 1:] - carry_lon[:, :-1]) / LON_SPACING
        - (push_lat[1:] - push_lat[:-1]) / LAT_SPACING
    )
    return (rate_surface, rate_east, rate_north)


def from_below(values, stride, along_axis, filler):
    length = values.shape[along_axis]
    padding = jnp.full_like(slab_of(values, 0, stride, along_axis), filler)
    return jnp.concatenate([padding, slab_of(values, 0, length - stride, along_axis)], along_axis)


def from_above(values, stride, along_axis, filler):
    length = values.shape[along_axis]
    padding = jnp.full_like(slab_of(values, 0, stride, along_axis), filler)
    return jnp.concatenate([slab_of(values, stride, length, along_axis), padding], along_axis)


def reduce_lines(lower_band, main_band, upper_band, rights, along_axis):
    length = rights.shape[along_axis]
    position = lax.broadcasted_iota(jnp.int32, rights.shape, along_axis)
    stride = 1
    for _ in range(PCR_STEPS):
        def from_lower(values, fill):
            return jnp.where(position >= stride, pltpu.roll(values, stride, along_axis), fill)

        def from_upper(values, fill):
            return jnp.where(
                position < length - stride, pltpu.roll(values, length - stride, along_axis), fill
            )

        below = [from_lower(band, fill) for band, fill in
                 ((lower_band, 0.0), (main_band, 1.0), (upper_band, 0.0), (rights, 0.0))]
        above = [from_upper(band, fill) for band, fill in
                 ((lower_band, 0.0), (main_band, 1.0), (upper_band, 0.0), (rights, 0.0))]
        weight_below = lower_band / below[1]
        weight_above = upper_band / above[1]
        new_lower = -weight_below * below[0]
        new_main = main_band - weight_below * below[2] - weight_above * above[0]
        new_upper = -weight_above * above[2]
        rights = rights - weight_below * below[3] - weight_above * above[3]
        lower_band, main_band, upper_band = new_lower, new_main, new_upper
        stride = stride * 2
    return rights / main_band


def tendency_body(surface_ref, east_ref, north_ref, depth_ref, wet_ref, place_ref, layout,
                  first_row, used_cols, tile_offset):
    rows, cols, box_rows, region_above, tile_rows, count = layout
    place = place_ref[0]
    depth = depth_ref[pl.ds(first_row, rows), :]
    surface = surface_ref[pl.ds(first_row, rows), :]
    coef = depth * depth / (3.0 * LON_SPACING * LON_SPACING)
    keep = lax.broadcasted_iota(jnp.int32, depth.shape, 1) < used_cols
    rights = east_ref[pl.ds(first_row, rows), :] / (depth + surface)
    east_raw = reduce_lines(
        jnp.where(keep, -coef, 0.0),
        jnp.where(keep, 1.0 + 2.0 * coef, 1.0),
        jnp.where(keep, -coef, 0.0),
        jnp.where(keep, rights, 0.0),
        1,
    )
    full_depth = depth_ref[...]
    coef = full_depth * full_depth / (3.0 * LAT_SPACING * LAT_SPACING)
    box_row = lax.broadcasted_iota(jnp.int32, depth_ref.shape, 0)
    global_row = place * tile_rows - region_above - tile_offset[0] + box_row
    keep = (global_row >= 0) & (global_row < count * tile_rows) & (box_row < box_rows)
    rights = north_ref[...] / (full_depth + surface_ref[...])
    north_raw = reduce_lines(
        jnp.where(keep, -coef, 0.0),
        jnp.where(keep, 1.0 + 2.0 * coef, 1.0),
        jnp.where(keep, -coef, 0.0),
        jnp.where(keep, rights, 0.0),
        0,
    )[first_row : first_row + rows]

    def wrapped(values):
        values = pltpu.roll(values, rows - (tile_offset[0] - first_row), 0)
        return pltpu.roll(values, cols - tile_offset[1], 1)

    wet = wrapped(wet_ref[pl.ds(first_row, rows), :])
    surface = wrapped(surface)
    depth = wrapped(depth)
    velocity_u = wet * wrapped(east_raw)
    velocity_v = wet * wrapped(north_raw)
    wrapped_row = lax.broadcasted_iota(jnp.int32, (rows, cols), 0)
    tile_row = jnp.where(wrapped_row >= rows - 2, wrapped_row - rows, wrapped_row) - region_above
    top = place == 0
    bottom = place == count - 1
    for wall, row, shift in (
        (top, -1, rows - 1), (top, -2, rows - 3), (bottom, tile_rows, 1), (bottom, tile_rows + 1, 3)
    ):
        velocity_v = jnp.where(
            wall & (tile_row == row), -pltpu.roll(velocity_v, shift, 0), velocity_v
        )

    def east_of(values):
        return pltpu.roll(values, cols - 1, 1)

    def west_of(values):
        return pltpu.roll(values, 1, 1)

    def north_of(values):
        return pltpu.roll(values, rows - 1, 0)

    def south_of(values):
        return pltpu.roll(values, 1, 0)

    def face_pair(values, later, earlier):
        jump = later(values) - values
        slope = limited(earlier(jump), jump)
        return values + 0.5 * slope, later(values - 0.5 * slope)

    surface_pair = face_pair(surface, east_of, west_of)
    east_pair = face_pair(velocity_u, east_of, west_of)
    north_pair = face_pair(velocity_v, east_of, west_of)
    depth_lon = 0.5 * (depth + east_of(depth))
    open_lon = wet * east_of(wet)
    mass_lon, push_lon, carry_lon = wave_flux(
        surface_pair[0], surface_pair[1], east_pair[0], east_pair[1],
        north_pair[0], north_pair[1], depth_lon, open_lon,
    )
    surface_pair = face_pair(surface, north_of, south_of)
    east_pair = face_pair(velocity_u, north_of, south_of)
    north_pair = face_pair(velocity_v, north_of, south_of)
    depth_lat = 0.5 * (depth + north_of(depth))
    open_lat = wet * north_of(wet)
    mass_lat, push_lat, carry_lat = wave_flux(
        surface_pair[0], surface_pair[1], north_pair[0], north_pair[1],
        east_pair[0], east_pair[1], depth_lat, open_lat,
    )
    rate_surface = (
        -(mass_lon - west_of(mass_lon)) / LON_SPACING - (mass_lat - south_of(mass_lat)) / LAT_SPACING
    )
    source_east = GRAVITY * surface * (depth_lon - west_of(depth_lon)) / LON_SPACING
    source_north = GRAVITY * surface * (depth_lat - south_of(depth_lat)) / LAT_SPACING
    rate_east = wet * (
        source_east
        - (push_lon - west_of(push_lon)) / LON_SPACING
        - (carry_lat - south_of(carry_lat)) / LAT_SPACING
    )
    rate_north = wet * (
        source_north
        - (carry_lon - west_of(carry_lon)) / LON_SPACING
        - (push_lat - south_of(push_lat)) / LAT_SPACING
    )
    return (rate_surface, rate_east, rate_north), (surface, velocity_u, velocity_v), wrapped


def section_kernel(surface_ref, east_ref, north_ref, depth_ref, wet_ref, place_ref,
                   lift_ref, start_surface, start_east, start_north,
                   next_surface, next_east, next_north, east_out, north_out, *,
                   first_row, used_cols, tile_offset, weights, layout):
    tile_rows, tile_cols = lift_ref.shape
    rates, (surface, velocity_u, velocity_v), wrapped = tendency_body(
        surface_ref, east_ref, north_ref, depth_ref, wet_ref, place_ref, layout,
        first_row, used_cols, tile_offset,
    )
    rows = layout[0]
    nows = (
        surface,
        wrapped(east_ref[pl.ds(first_row, rows), :]),
        wrapped(north_ref[pl.ds(first_row, rows), :]),
    )
    first, second = weights
    rates = (
        rates[0][:tile_rows, :tile_cols] + lift_ref[...],
        rates[1][:tile_rows, :tile_cols],
        rates[2][:tile_rows, :tile_cols],
    )
    for out, start, now, rate in zip(
        (next_surface, next_east, next_north),
        (start_surface, start_east, start_north),
        nows,
        rates,
    ):
        out[...] = first * start[...] + second * (now[:tile_rows, :tile_cols] + TIME_STEP * rate)
    east_out[...] = velocity_u[:tile_rows, :tile_cols]
    north_out[...] = velocity_v[:tile_rows, :tile_cols]


def ring_kernel(surface_ref, east_ref, north_ref, depth_ref, wet_ref, place_ref,
                lift_ref, next_surface, next_east, next_north, depth_out, wet_out, *,
                first_row, used_cols, tile_offset, layout):
    rows = layout[0]
    out_rows, out_cols = next_surface.shape
    rates, (surface, _, _), wrapped = tendency_body(
        surface_ref, east_ref, north_ref, depth_ref, wet_ref, place_ref, layout,
        first_row, used_cols, tile_offset,
    )
    lift = wrapped(lift_ref[pl.ds(first_row, rows), :])
    nows = (
        surface,
        wrapped(east_ref[pl.ds(first_row, rows), :]),
        wrapped(north_ref[pl.ds(first_row, rows), :]),
    )
    rates = (rates[0] + lift, rates[1], rates[2])
    for out, now, rate in zip((next_surface, next_east, next_north), nows, rates):
        out[...] = (0.0 * now + 1.0 * (now + TIME_STEP * rate))[:out_rows, :out_cols]
    depth_out[...] = wrapped(depth_ref[pl.ds(first_row, rows), :])[:out_rows, :out_cols]
    wet_out[...] = wrapped(wet_ref[pl.ds(first_row, rows), :])[:out_rows, :out_cols]


def ring_step(fields, place, layout, out_shape, first_row, used_cols, tile_offset):
    spec = pl.BlockSpec(memory_space=pltpu.VMEM)
    scalar = pl.BlockSpec(memory_space=pltpu.SMEM)
    shape = jax.ShapeDtypeStruct(out_shape, jnp.float32)
    return pl.pallas_call(
        lambda *refs: ring_kernel(
            *refs, first_row=first_row, used_cols=used_cols, tile_offset=tile_offset,
            layout=layout,
        ),
        out_shape=(shape,) * 5,
        in_specs=[spec] * 5 + [scalar, spec],
        out_specs=(spec,) * 5,
        name="ring_step",
    )(*fields[:5], place, fields[5])


def section_step(fields, place, layout, lift, initial, first_row, used_cols, tile_offset,
                 weights):
    spec = pl.BlockSpec(memory_space=pltpu.VMEM)
    scalar = pl.BlockSpec(memory_space=pltpu.SMEM)
    shape = jax.ShapeDtypeStruct(lift.shape, jnp.float32)
    return pl.pallas_call(
        lambda *refs: section_kernel(
            *refs, first_row=first_row, used_cols=used_cols, tile_offset=tile_offset,
            weights=weights, layout=layout,
        ),
        out_shape=(shape,) * 5,
        in_specs=[spec] * 5 + [scalar] + [spec] * 4,
        out_specs=(spec,) * 5,
        name="section_step",
    )(*fields, place, lift, *initial)


def halo_box(fields, wide_x, wide_y, place, count, padded_shape):
    lon_count = lax.axis_size("lon")
    west = lax.ppermute(
        fields[:, :, -wide_x:], "lon", [(i, (i + 1) % lon_count) for i in range(lon_count)]
    )
    east = lax.ppermute(
        fields[:, :, :wide_x], "lon", [((i + 1) % lon_count, i) for i in range(lon_count)]
    )
    wide = jnp.concatenate([west, fields, east], axis=2)
    above = passed_along(wide[:, -wide_y:], "lat", 1)
    below = passed_along(wide[:, :wide_y], "lat", -1)
    above = jnp.where(place == 0, wide[:, wide_y - 1 :: -1], above)
    below = jnp.where(place == count - 1, wide[:, : -wide_y - 1 : -1], below)
    box = jnp.concatenate([above, wide, below], axis=1)
    return pad_to(box, padded_shape)


def pad_to(values, shape):
    widths = [(0, 0)] * (values.ndim - 2) + [
        (0, want - have) for want, have in zip(shape, values.shape[-2:])
    ]
    return jnp.pad(values, widths)


def wall_mirrored(values, halo, place, count, rows):
    top = jnp.concatenate([values[..., 2 * halo - 1 : halo - 1 : -1, :], values[..., halo:, :]], axis=-2)
    values = jnp.where(place == 0, top, values)
    bottom = jnp.concatenate(
        [
            values[..., : rows - halo, :],
            values[..., rows - halo - 1 : rows - 2 * halo - 1 : -1, :],
            values[..., rows:, :],
        ],
        axis=-2,
    )
    return jnp.where(place == count - 1, bottom, values)


class Geometry:
    def __init__(self, out_rows, out_cols, halo_y, halo_x):
        self.box_rows = out_rows + 2 * halo_y
        self.box_cols = out_cols + 2 * halo_x
        self.first_row = (halo_y - 2) // 8 * 8
        self.rows = -(-(halo_y + out_rows + 2 - self.first_row) // 8) * 8
        self.padded = (
            max(-(-self.box_rows // 8) * 8, self.first_row + self.rows),
            -(-self.box_cols // 128) * 128,
        )
        self.offset = (halo_y, halo_x)

    def masks(self, region_above, place, count, tile_rows):
        box_row = lax.broadcasted_iota(jnp.int32, self.padded, 0)
        global_row = place * tile_rows - region_above - self.offset[0] + box_row
        inside = (global_row >= 0) & (global_row < count * tile_rows) & (box_row < self.box_rows)
        wrapped_row = lax.broadcasted_iota(jnp.int32, (self.rows, self.padded[1]), 0)
        tile_row = jnp.where(wrapped_row >= self.rows - 2, wrapped_row - self.rows, wrapped_row)
        tile_row = tile_row - region_above
        top = place == 0
        bottom = place == count - 1
        mirror = jnp.where(
            top & (tile_row == -1), 1,
            jnp.where(top & (tile_row == -2), 2,
            jnp.where(bottom & (tile_row == tile_rows), 3,
            jnp.where(bottom & (tile_row == tile_rows + 1), 4, 0))),
        ).astype(jnp.int32)
        return inside.astype(jnp.float32), mirror


def local(surface, momentum_x, momentum_y, water_depth, wet_mask, slide_cells, slide_rate):
    wet_float = wet_mask.astype(jnp.float32)
    place = lax.axis_index("lat")
    count = lax.axis_size("lat")
    tile_rows, tile_cols = surface.shape
    wide_x = WINDOW_LON + 2
    wide_y = WINDOW_LAT + 2
    lift = (
        jnp.zeros((tile_rows * tile_cols,), jnp.float32)
        .at[slide_cells.reshape(-1)]
        .add(slide_rate.reshape(-1))
        .reshape(tile_rows, tile_cols)
    )
    ring = Geometry(tile_rows + 2 * wide_y, tile_cols + 2 * wide_x, wide_y, wide_x)
    plain = Geometry(tile_rows, tile_cols, wide_y, wide_x)
    place_array = jnp.reshape(place, (1,)).astype(jnp.int32)
    ring_layout = (ring.rows, ring.padded[1], ring.box_rows, wide_y, tile_rows, count)
    plain_layout = (plain.rows, plain.padded[1], plain.box_rows, 0, tile_rows, count)
    initial = (surface, momentum_x, momentum_y)

    big = halo_box(
        jnp.stack([surface, momentum_x, momentum_y, water_depth, wet_float, lift]),
        2 * wide_x, 2 * wide_y, place, count, ring.padded,
    )
    ring_state = ring_step(
        tuple(big[k] for k in range(6)), place_array, ring_layout, plain.padded,
        ring.first_row, ring.box_cols, ring.offset,
    )
    box = wall_mirrored(jnp.stack(ring_state[:3]), wide_y, place, count, plain.box_rows)
    depth_box, wet_box = ring_state[3], ring_state[4]
    for first, second in ((0.75, 0.25), (1.0 / 3.0, 2.0 / 3.0)):
        if box is None:
            box = halo_box(jnp.stack(list(current)), wide_x, wide_y, place, count, plain.padded)
        next_surface, next_east, next_north, velocity_u, velocity_v = section_step(
            (box[0], box[1], box[2], depth_box, wet_box), place_array, plain_layout, lift, initial,
            plain.first_row, plain.box_cols, plain.offset, (first, second),
        )
        current = (next_surface, next_east, next_north)
        box = None
    return (current[0], current[1], current[2], velocity_u, velocity_v)


def solution(mesh):
    in_specs = (P("lat", "lon"),) * 7
    out_specs = (P("lat", "lon"),) * 5
    return jax.shard_map(local, mesh=mesh, in_specs=in_specs, out_specs=out_specs, check_vma=False)
```

```python
import jax
import jax.numpy as jnp
from jax import lax
from jax.sharding import PartitionSpec as P
from jax.experimental import pallas as pl
from jax.experimental.pallas import tpu as pltpu

GRAVITY = 1.0
LON_SPACING = 0.5
LAT_SPACING = 0.6
TIME_STEP = 0.1
WINDOW_LON = 40
WINDOW_LAT = 32
PCR_STEPS = 6


def shifted(block, axis, distance):
    devices = range(lax.axis_size(axis))
    route = [((i - distance) % len(devices), i) for i in devices]
    return lax.ppermute(block, axis, route)


def passed_along(x, axis, by):
    peers = lax.axis_size(axis)
    pairs = [(i, i + by) for i in range(peers) if 0 <= i + by < peers]
    return lax.ppermute(x, axis, pairs)


def extended(cells, sides, width, closed):
    for axis, dim in sides:
        count = lax.axis_size(axis)
        ends = count if closed else count - 1
        head = lax.slice_in_dim(cells, 0, width, axis=dim)
        tail = lax.slice_in_dim(cells, cells.shape[dim] - width, cells.shape[dim], axis=dim)
        cells = jnp.concatenate(
            [
                lax.ppermute(tail, axis, [(i, (i + 1) % count) for i in range(ends)]),
                cells,
                lax.ppermute(head, axis, [((i + 1) % count, i) for i in range(ends)]),
            ],
            axis=dim,
        )
    return cells


def slab_of(values, start, stop, along_axis):
    return lax.slice_in_dim(values, start, stop, axis=along_axis)


def limited(former, latter):
    return jnp.maximum(jnp.minimum(former, latter), 0.0) + jnp.minimum(
        jnp.maximum(former, latter), 0.0
    )


def face_states(values, along_axis):
    length = values.shape[along_axis]
    jumps = slab_of(values, 1, length, along_axis) - slab_of(values, 0, length - 1, along_axis)
    slopes = limited(
        slab_of(jumps, 0, length - 2, along_axis), slab_of(jumps, 1, length - 1, along_axis)
    )
    left_state = slab_of(values, 1, length - 2, along_axis) + 0.5 * slab_of(
        slopes, 0, length - 3, along_axis
    )
    right_state = slab_of(values, 2, length - 1, along_axis) - 0.5 * slab_of(
        slopes, 1, length - 2, along_axis
    )
    return (left_state, right_state)


def wave_flux(
    surface_left,
    surface_right,
    normal_left,
    normal_right,
    tangent_left,
    tangent_right,
    face_depth,
    opened,
):
    height_left = surface_left + face_depth
    height_right = surface_right + face_depth
    celerity_left = jnp.sqrt(GRAVITY * height_left)
    celerity_right = jnp.sqrt(GRAVITY * height_right)
    slowest = jnp.minimum(
        jnp.minimum(normal_left - celerity_left, normal_right - celerity_right), 0.0
    )
    fastest = jnp.maximum(
        jnp.maximum(normal_left + celerity_left, normal_right + celerity_right), 0.0
    )
    spread = fastest - slowest
    product = slowest * fastest
    mass_left = height_left * normal_left
    mass_right = height_right * normal_right
    push_left = mass_left * normal_left + GRAVITY * (
        0.5 * surface_left * surface_left + face_depth * surface_left
    )
    push_right = mass_right * normal_right + GRAVITY * (
        0.5 * surface_right * surface_right + face_depth * surface_right
    )
    carry_left = mass_left * tangent_left
    carry_right = mass_right * tangent_right
    mass_flux = (
        opened
        * (fastest * mass_left - slowest * mass_right + product * (surface_right - surface_left))
        / spread
    )
    push_flux = (
        opened
        * (fastest * push_left - slowest * push_right + product * (mass_right - mass_left))
        / spread
    )
    carry_flux = (
        opened
        * (
            fastest * carry_left
            - slowest * carry_right
            + product * (height_right * tangent_right - height_left * tangent_left)
        )
        / spread
    )
    return (mass_flux, push_flux, carry_flux)


def tendencies(across, along):
    width = across[0].shape[1] - 4
    row_count = along[0].shape[0] - 4
    surface_pair = face_states(across[0], 1)
    east_pair = face_states(across[1], 1)
    north_pair = face_states(across[2], 1)
    depth_lon = 0.5 * (across[3][:, 1 : width + 2] + across[3][:, 2 : width + 3])
    open_lon = across[4][:, 1 : width + 2] * across[4][:, 2 : width + 3]
    mass_lon, push_lon, carry_lon = wave_flux(
        surface_pair[0],
        surface_pair[1],
        east_pair[0],
        east_pair[1],
        north_pair[0],
        north_pair[1],
        depth_lon,
        open_lon,
    )
    surface_pair = face_states(along[0], 0)
    east_pair = face_states(along[1], 0)
    north_pair = face_states(along[2], 0)
    depth_lat = 0.5 * (along[3][1 : row_count + 2] + along[3][2 : row_count + 3])
    open_lat = along[4][1 : row_count + 2] * along[4][2 : row_count + 3]
    mass_lat, push_lat, carry_lat = wave_flux(
        surface_pair[0],
        surface_pair[1],
        north_pair[0],
        north_pair[1],
        east_pair[0],
        east_pair[1],
        depth_lat,
        open_lat,
    )
    surface_mid = across[0][:, 2 : width + 2]
    wet_mid = across[4][:, 2 : width + 2]
    rate_surface = (
        -(mass_lon[:, 1:] - mass_lon[:, :-1]) / LON_SPACING
        - (mass_lat[1:] - mass_lat[:-1]) / LAT_SPACING
    )
    source_east = GRAVITY * surface_mid * (depth_lon[:, 1:] - depth_lon[:, :-1]) / LON_SPACING
    source_north = GRAVITY * surface_mid * (depth_lat[1:] - depth_lat[:-1]) / LAT_SPACING
    rate_east = wet_mid * (
        source_east
        - (push_lon[:, 1:] - push_lon[:, :-1]) / LON_SPACING
        - (carry_lat[1:] - carry_lat[:-1]) / LAT_SPACING
    )
    rate_north = wet_mid * (
        source_north
        - (carry_lon[:, 1:] - carry_lon[:, :-1]) / LON_SPACING
        - (push_lat[1:] - push_lat[:-1]) / LAT_SPACING
    )
    return (rate_surface, rate_east, rate_north)


def from_below(values, stride, along_axis, filler):
    length = values.shape[along_axis]
    padding = jnp.full_like(slab_of(values, 0, stride, along_axis), filler)
    return jnp.concatenate([padding, slab_of(values, 0, length - stride, along_axis)], along_axis)


def from_above(values, stride, along_axis, filler):
    length = values.shape[along_axis]
    padding = jnp.full_like(slab_of(values, 0, stride, along_axis), filler)
    return jnp.concatenate([slab_of(values, stride, length, along_axis), padding], along_axis)


def reduce_lines(lower_band, main_band, upper_band, rights, along_axis):
    length = rights.shape[along_axis]
    position = lax.broadcasted_iota(jnp.int32, rights.shape, along_axis)
    stride = 1
    for _ in range(PCR_STEPS):
        def from_lower(values, fill):
            return jnp.where(position >= stride, pltpu.roll(values, stride, along_axis), fill)

        def from_upper(values, fill):
            return jnp.where(
                position < length - stride, pltpu.roll(values, length - stride, along_axis), fill
            )

        below = [from_lower(band, fill) for band, fill in
                 ((lower_band, 0.0), (main_band, 1.0), (upper_band, 0.0), (rights, 0.0))]
        above = [from_upper(band, fill) for band, fill in
                 ((lower_band, 0.0), (main_band, 1.0), (upper_band, 0.0), (rights, 0.0))]
        weight_below = lower_band / below[1]
        weight_above = upper_band / above[1]
        new_lower = -weight_below * below[0]
        new_main = main_band - weight_below * below[2] - weight_above * above[0]
        new_upper = -weight_above * above[2]
        rights = rights - weight_below * below[3] - weight_above * above[3]
        lower_band, main_band, upper_band = new_lower, new_main, new_upper
        stride = stride * 2
    return rights / main_band


def tendency_body(surface_ref, east_ref, north_ref, depth_ref, wet_ref, place_ref, layout,
                  first_row, used_cols, tile_offset):
    rows, cols, box_rows, region_above, tile_rows, count = layout
    place = place_ref[0]
    depth = depth_ref[pl.ds(first_row, rows), :]
    surface = surface_ref[pl.ds(first_row, rows), :]
    coef = depth * depth / (3.0 * LON_SPACING * LON_SPACING)
    keep = lax.broadcasted_iota(jnp.int32, depth.shape, 1) < used_cols
    rights = east_ref[pl.ds(first_row, rows), :] / (depth + surface)
    east_raw = reduce_lines(
        jnp.where(keep, -coef, 0.0),
        jnp.where(keep, 1.0 + 2.0 * coef, 1.0),
        jnp.where(keep, -coef, 0.0),
        jnp.where(keep, rights, 0.0),
        1,
    )
    full_depth = depth_ref[...]
    coef = full_depth * full_depth / (3.0 * LAT_SPACING * LAT_SPACING)
    box_row = lax.broadcasted_iota(jnp.int32, depth_ref.shape, 0)
    global_row = place * tile_rows - region_above - tile_offset[0] + box_row
    keep = (global_row >= 0) & (global_row < count * tile_rows) & (box_row < box_rows)
    rights = north_ref[...] / (full_depth + surface_ref[...])
    north_raw = reduce_lines(
        jnp.where(keep, -coef, 0.0),
        jnp.where(keep, 1.0 + 2.0 * coef, 1.0),
        jnp.where(keep, -coef, 0.0),
        jnp.where(keep, rights, 0.0),
        0,
    )[first_row : first_row + rows]

    def wrapped(values):
        values = pltpu.roll(values, rows - (tile_offset[0] - first_row), 0)
        return pltpu.roll(values, cols - tile_offset[1], 1)

    wet = wrapped(wet_ref[pl.ds(first_row, rows), :])
    surface = wrapped(surface)
    depth = wrapped(depth)
    velocity_u = wet * wrapped(east_raw)
    velocity_v = wet * wrapped(north_raw)
    wrapped_row = lax.broadcasted_iota(jnp.int32, (rows, cols), 0)
    tile_row = jnp.where(wrapped_row >= rows - 2, wrapped_row - rows, wrapped_row) - region_above
    top = place == 0
    bottom = place == count - 1
    for wall, row, shift in (
        (top, -1, rows - 1), (top, -2, rows - 3), (bottom, tile_rows, 1), (bottom, tile_rows + 1, 3)
    ):
        velocity_v = jnp.where(
            wall & (tile_row == row), -pltpu.roll(velocity_v, shift, 0), velocity_v
        )

    def east_of(values):
        return pltpu.roll(values, cols - 1, 1)

    def west_of(values):
        return pltpu.roll(values, 1, 1)

    def north_of(values):
        return pltpu.roll(values, rows - 1, 0)

    def south_of(values):
        return pltpu.roll(values, 1, 0)

    def face_pair(values, later, earlier):
        jump = later(values) - values
        slope = limited(earlier(jump), jump)
        return values + 0.5 * slope, later(values - 0.5 * slope)

    surface_pair = face_pair(surface, east_of, west_of)
    east_pair = face_pair(velocity_u, east_of, west_of)
    north_pair = face_pair(velocity_v, east_of, west_of)
    depth_lon = 0.5 * (depth + east_of(depth))
    open_lon = wet * east_of(wet)
    mass_lon, push_lon, carry_lon = wave_flux(
        surface_pair[0], surface_pair[1], east_pair[0], east_pair[1],
        north_pair[0], north_pair[1], depth_lon, open_lon,
    )
    surface_pair = face_pair(surface, north_of, south_of)
    east_pair = face_pair(velocity_u, north_of, south_of)
    north_pair = face_pair(velocity_v, north_of, south_of)
    depth_lat = 0.5 * (depth + north_of(depth))
    open_lat = wet * north_of(wet)
    mass_lat, push_lat, carry_lat = wave_flux(
        surface_pair[0], surface_pair[1], north_pair[0], north_pair[1],
        east_pair[0], east_pair[1], depth_lat, open_lat,
    )
    rate_surface = (
        -(mass_lon - west_of(mass_lon)) / LON_SPACING - (mass_lat - south_of(mass_lat)) / LAT_SPACING
    )
    source_east = GRAVITY * surface * (depth_lon - west_of(depth_lon)) / LON_SPACING
    source_north = GRAVITY * surface * (depth_lat - south_of(depth_lat)) / LAT_SPACING
    rate_east = wet * (
        source_east
        - (push_lon - west_of(push_lon)) / LON_SPACING
        - (carry_lat - south_of(carry_lat)) / LAT_SPACING
    )
    rate_north = wet * (
        source_north
        - (carry_lon - west_of(carry_lon)) / LON_SPACING
        - (push_lat - south_of(push_lat)) / LAT_SPACING
    )
    return (rate_surface, rate_east, rate_north), (surface, velocity_u, velocity_v), wrapped


def section_kernel(surface_ref, east_ref, north_ref, depth_ref, wet_ref, place_ref,
                   lift_ref, start_surface, start_east, start_north,
                   next_surface, next_east, next_north, east_out, north_out, *,
                   first_row, used_cols, tile_offset, weights, layout):
    tile_rows, tile_cols = lift_ref.shape
    rates, (surface, velocity_u, velocity_v), wrapped = tendency_body(
        surface_ref, east_ref, north_ref, depth_ref, wet_ref, place_ref, layout,
        first_row, used_cols, tile_offset,
    )
    rows = layout[0]
    nows = (
        surface,
        wrapped(east_ref[pl.ds(first_row, rows), :]),
        wrapped(north_ref[pl.ds(first_row, rows), :]),
    )
    first, second = weights
    rates = (
        rates[0][:tile_rows, :tile_cols] + lift_ref[...],
        rates[1][:tile_rows, :tile_cols],
        rates[2][:tile_rows, :tile_cols],
    )
    for out, start, now, rate in zip(
        (next_surface, next_east, next_north),
        (start_surface, start_east, start_north),
        nows,
        rates,
    ):
        out[...] = first * start[...] + second * (now[:tile_rows, :tile_cols] + TIME_STEP * rate)
    east_out[...] = velocity_u[:tile_rows, :tile_cols]
    north_out[...] = velocity_v[:tile_rows, :tile_cols]


def ring_kernel(surface_ref, east_ref, north_ref, depth_ref, wet_ref, place_ref,
                lift_ref, next_surface, next_east, next_north, depth_out, wet_out, *,
                first_row, used_cols, tile_offset, layout):
    rows = layout[0]
    out_rows, out_cols = next_surface.shape
    rates, (surface, _, _), wrapped = tendency_body(
        surface_ref, east_ref, north_ref, depth_ref, wet_ref, place_ref, layout,
        first_row, used_cols, tile_offset,
    )
    lift = wrapped(lift_ref[pl.ds(first_row, rows), :])
    nows = (
        surface,
        wrapped(east_ref[pl.ds(first_row, rows), :]),
        wrapped(north_ref[pl.ds(first_row, rows), :]),
    )
    rates = (rates[0] + lift, rates[1], rates[2])
    for out, now, rate in zip((next_surface, next_east, next_north), nows, rates):
        out[...] = (0.0 * now + 1.0 * (now + TIME_STEP * rate))[:out_rows, :out_cols]
    depth_out[...] = wrapped(depth_ref[pl.ds(first_row, rows), :])[:out_rows, :out_cols]
    wet_out[...] = wrapped(wet_ref[pl.ds(first_row, rows), :])[:out_rows, :out_cols]


def ring_step(fields, place, layout, out_shape, first_row, used_cols, tile_offset):
    spec = pl.BlockSpec(memory_space=pltpu.VMEM)
    scalar = pl.BlockSpec(memory_space=pltpu.SMEM)
    shape = jax.ShapeDtypeStruct(out_shape, jnp.float32)
    return pl.pallas_call(
        lambda *refs: ring_kernel(
            *refs, first_row=first_row, used_cols=used_cols, tile_offset=tile_offset,
            layout=layout,
        ),
        out_shape=(shape,) * 5,
        in_specs=[spec] * 5 + [scalar, spec],
        out_specs=(spec,) * 5,
        name="ring_step",
    )(*fields[:5], place, fields[5])


def section_step(fields, place, layout, lift, initial, first_row, used_cols, tile_offset,
                 weights):
    spec = pl.BlockSpec(memory_space=pltpu.VMEM)
    scalar = pl.BlockSpec(memory_space=pltpu.SMEM)
    shape = jax.ShapeDtypeStruct(lift.shape, jnp.float32)
    return pl.pallas_call(
        lambda *refs: section_kernel(
            *refs, first_row=first_row, used_cols=used_cols, tile_offset=tile_offset,
            weights=weights, layout=layout,
        ),
        out_shape=(shape,) * 5,
        in_specs=[spec] * 5 + [scalar] + [spec] * 4,
        out_specs=(spec,) * 5,
        name="section_step",
    )(*fields, place, lift, *initial)


def halo_box(fields, wide_x, wide_y, place, count, padded_shape):
    lon_count = lax.axis_size("lon")
    west = lax.ppermute(
        fields[:, :, -wide_x:], "lon", [(i, (i + 1) % lon_count) for i in range(lon_count)]
    )
    east = lax.ppermute(
        fields[:, :, :wide_x], "lon", [((i + 1) % lon_count, i) for i in range(lon_count)]
    )
    wide = jnp.concatenate([west, fields, east], axis=2)
    above = passed_along(wide[:, -wide_y:], "lat", 1)
    below = passed_along(wide[:, :wide_y], "lat", -1)
    above = jnp.where(
        place == 0, jnp.concatenate([above[:, :-2], wide[:, 1:2], wide[:, 0:1]], axis=1), above
    )
    below = jnp.where(
        place == count - 1,
        jnp.concatenate([wide[:, -1:], wide[:, -2:-1], below[:, 2:]], axis=1),
        below,
    )
    box = jnp.concatenate([above, wide, below], axis=1)
    return pad_to(box, padded_shape)


def pad_to(values, shape):
    widths = [(0, 0)] * (values.ndim - 2) + [
        (0, want - have) for want, have in zip(shape, values.shape[-2:])
    ]
    return jnp.pad(values, widths)


def wall_mirrored(values, halo, place, count, rows):
    top = jnp.concatenate(
        [
            values[..., : halo - 2, :],
            values[..., halo + 1 : halo + 2, :],
            values[..., halo : halo + 1, :],
            values[..., halo:, :],
        ],
        axis=-2,
    )
    values = jnp.where(place == 0, top, values)
    bottom = jnp.concatenate(
        [
            values[..., : rows - halo, :],
            values[..., rows - halo - 1 : rows - halo, :],
            values[..., rows - halo - 2 : rows - halo - 1, :],
            values[..., rows - halo + 2 :, :],
        ],
        axis=-2,
    )
    return jnp.where(place == count - 1, bottom, values)


class Geometry:
    def __init__(self, out_rows, out_cols, halo_y, halo_x):
        self.box_rows = out_rows + 2 * halo_y
        self.box_cols = out_cols + 2 * halo_x
        self.first_row = (halo_y - 2) // 8 * 8
        self.rows = -(-(halo_y + out_rows + 2 - self.first_row) // 8) * 8
        self.padded = (
            max(-(-self.box_rows // 8) * 8, self.first_row + self.rows),
            -(-self.box_cols // 128) * 128,
        )
        self.offset = (halo_y, halo_x)

    def masks(self, region_above, place, count, tile_rows):
        box_row = lax.broadcasted_iota(jnp.int32, self.padded, 0)
        global_row = place * tile_rows - region_above - self.offset[0] + box_row
        inside = (global_row >= 0) & (global_row < count * tile_rows) & (box_row < self.box_rows)
        wrapped_row = lax.broadcasted_iota(jnp.int32, (self.rows, self.padded[1]), 0)
        tile_row = jnp.where(wrapped_row >= self.rows - 2, wrapped_row - self.rows, wrapped_row)
        tile_row = tile_row - region_above
        top = place == 0
        bottom = place == count - 1
        mirror = jnp.where(
            top & (tile_row == -1), 1,
            jnp.where(top & (tile_row == -2), 2,
            jnp.where(bottom & (tile_row == tile_rows), 3,
            jnp.where(bottom & (tile_row == tile_rows + 1), 4, 0))),
        ).astype(jnp.int32)
        return inside.astype(jnp.float32), mirror


def local(surface, momentum_x, momentum_y, water_depth, wet_mask, slide_cells, slide_rate):
    wet_float = wet_mask.astype(jnp.float32)
    place = lax.axis_index("lat")
    count = lax.axis_size("lat")
    tile_rows, tile_cols = surface.shape
    wide_x = WINDOW_LON + 2
    wide_y = WINDOW_LAT + 2
    lift = (
        jnp.zeros((tile_rows * tile_cols,), jnp.float32)
        .at[slide_cells.reshape(-1)]
        .add(slide_rate.reshape(-1))
        .reshape(tile_rows, tile_cols)
    )
    ring = Geometry(tile_rows + 2 * wide_y, tile_cols + 2 * wide_x, wide_y, wide_x)
    plain = Geometry(tile_rows, tile_cols, wide_y, wide_x)
    place_array = jnp.reshape(place, (1,)).astype(jnp.int32)
    ring_layout = (ring.rows, ring.padded[1], ring.box_rows, wide_y, tile_rows, count)
    plain_layout = (plain.rows, plain.padded[1], plain.box_rows, 0, tile_rows, count)
    initial = (surface, momentum_x, momentum_y)

    big = halo_box(
        jnp.stack([surface, momentum_x, momentum_y, water_depth, wet_float, lift]),
        2 * wide_x, 2 * wide_y, place, count, ring.padded,
    )
    ring_state = ring_step(
        tuple(big[k] for k in range(6)), place_array, ring_layout, plain.padded,
        ring.first_row, ring.box_cols, ring.offset,
    )
    box = wall_mirrored(jnp.stack(ring_state[:3]), wide_y, place, count, plain.box_rows)
    depth_box, wet_box = ring_state[3], ring_state[4]
    for first, second in ((0.75, 0.25), (1.0 / 3.0, 2.0 / 3.0)):
        if box is None:
            box = halo_box(jnp.stack(list(current)), wide_x, wide_y, place, count, plain.padded)
        next_surface, next_east, next_north, velocity_u, velocity_v = section_step(
            (box[0], box[1], box[2], depth_box, wet_box), place_array, plain_layout, lift, initial,
            plain.first_row, plain.box_cols, plain.offset, (first, second),
        )
        current = (next_surface, next_east, next_north)
        box = None
    return (current[0], current[1], current[2], velocity_u, velocity_v)


def solution(mesh):
    in_specs = (P("lat", "lon"),) * 7
    out_specs = (P("lat", "lon"),) * 5
    return jax.shard_map(local, mesh=mesh, in_specs=in_specs, out_specs=out_specs, check_vma=False)
```

```python
import jax
import jax.numpy as jnp
from jax import lax
from jax.sharding import PartitionSpec as P
from jax.experimental import pallas as pl
from jax.experimental.pallas import tpu as pltpu

GRAVITY = 1.0
LON_SPACING = 0.5
LAT_SPACING = 0.6
TIME_STEP = 0.1
WINDOW_LON = 40
WINDOW_LAT = 32
PCR_STEPS = 6


def shifted(block, axis, distance):
    devices = range(lax.axis_size(axis))
    route = [((i - distance) % len(devices), i) for i in devices]
    return lax.ppermute(block, axis, route)


def passed_along(x, axis, by):
    peers = lax.axis_size(axis)
    pairs = [(i, i + by) for i in range(peers) if 0 <= i + by < peers]
    return lax.ppermute(x, axis, pairs)


def extended(cells, sides, width, closed):
    for axis, dim in sides:
        count = lax.axis_size(axis)
        ends = count if closed else count - 1
        head = lax.slice_in_dim(cells, 0, width, axis=dim)
        tail = lax.slice_in_dim(cells, cells.shape[dim] - width, cells.shape[dim], axis=dim)
        cells = jnp.concatenate(
            [
                lax.ppermute(tail, axis, [(i, (i + 1) % count) for i in range(ends)]),
                cells,
                lax.ppermute(head, axis, [((i + 1) % count, i) for i in range(ends)]),
            ],
            axis=dim,
        )
    return cells


def slab_of(values, start, stop, along_axis):
    return lax.slice_in_dim(values, start, stop, axis=along_axis)


def limited(former, latter):
    return jnp.maximum(jnp.minimum(former, latter), 0.0) + jnp.minimum(
        jnp.maximum(former, latter), 0.0
    )


def face_states(values, along_axis):
    length = values.shape[along_axis]
    jumps = slab_of(values, 1, length, along_axis) - slab_of(values, 0, length - 1, along_axis)
    slopes = limited(
        slab_of(jumps, 0, length - 2, along_axis), slab_of(jumps, 1, length - 1, along_axis)
    )
    left_state = slab_of(values, 1, length - 2, along_axis) + 0.5 * slab_of(
        slopes, 0, length - 3, along_axis
    )
    right_state = slab_of(values, 2, length - 1, along_axis) - 0.5 * slab_of(
        slopes, 1, length - 2, along_axis
    )
    return (left_state, right_state)


def wave_flux(
    surface_left,
    surface_right,
    normal_left,
    normal_right,
    tangent_left,
    tangent_right,
    face_depth,
    opened,
):
    height_left = surface_left + face_depth
    height_right = surface_right + face_depth
    celerity_left = jnp.sqrt(GRAVITY * height_left)
    celerity_right = jnp.sqrt(GRAVITY * height_right)
    slowest = jnp.minimum(
        jnp.minimum(normal_left - celerity_left, normal_right - celerity_right), 0.0
    )
    fastest = jnp.maximum(
        jnp.maximum(normal_left + celerity_left, normal_right + celerity_right), 0.0
    )
    spread = fastest - slowest
    product = slowest * fastest
    mass_left = height_left * normal_left
    mass_right = height_right * normal_right
    push_left = mass_left * normal_left + GRAVITY * (
        0.5 * surface_left * surface_left + face_depth * surface_left
    )
    push_right = mass_right * normal_right + GRAVITY * (
        0.5 * surface_right * surface_right + face_depth * surface_right
    )
    carry_left = mass_left * tangent_left
    carry_right = mass_right * tangent_right
    mass_flux = (
        opened
        * (fastest * mass_left - slowest * mass_right + product * (surface_right - surface_left))
        / spread
    )
    push_flux = (
        opened
        * (fastest * push_left - slowest * push_right + product * (mass_right - mass_left))
        / spread
    )
    carry_flux = (
        opened
        * (
            fastest * carry_left
            - slowest * carry_right
            + product * (height_right * tangent_right - height_left * tangent_left)
        )
        / spread
    )
    return (mass_flux, push_flux, carry_flux)


def tendencies(across, along):
    width = across[0].shape[1] - 4
    row_count = along[0].shape[0] - 4
    surface_pair = face_states(across[0], 1)
    east_pair = face_states(across[1], 1)
    north_pair = face_states(across[2], 1)
    depth_lon = 0.5 * (across[3][:, 1 : width + 2] + across[3][:, 2 : width + 3])
    open_lon = across[4][:, 1 : width + 2] * across[4][:, 2 : width + 3]
    mass_lon, push_lon, carry_lon = wave_flux(
        surface_pair[0],
        surface_pair[1],
        east_pair[0],
        east_pair[1],
        north_pair[0],
        north_pair[1],
        depth_lon,
        open_lon,
    )
    surface_pair = face_states(along[0], 0)
    east_pair = face_states(along[1], 0)
    north_pair = face_states(along[2], 0)
    depth_lat = 0.5 * (along[3][1 : row_count + 2] + along[3][2 : row_count + 3])
    open_lat = along[4][1 : row_count + 2] * along[4][2 : row_count + 3]
    mass_lat, push_lat, carry_lat = wave_flux(
        surface_pair[0],
        surface_pair[1],
        north_pair[0],
        north_pair[1],
        east_pair[0],
        east_pair[1],
        depth_lat,
        open_lat,
    )
    surface_mid = across[0][:, 2 : width + 2]
    wet_mid = across[4][:, 2 : width + 2]
    rate_surface = (
        -(mass_lon[:, 1:] - mass_lon[:, :-1]) / LON_SPACING
        - (mass_lat[1:] - mass_lat[:-1]) / LAT_SPACING
    )
    source_east = GRAVITY * surface_mid * (depth_lon[:, 1:] - depth_lon[:, :-1]) / LON_SPACING
    source_north = GRAVITY * surface_mid * (depth_lat[1:] - depth_lat[:-1]) / LAT_SPACING
    rate_east = wet_mid * (
        source_east
        - (push_lon[:, 1:] - push_lon[:, :-1]) / LON_SPACING
        - (carry_lat[1:] - carry_lat[:-1]) / LAT_SPACING
    )
    rate_north = wet_mid * (
        source_north
        - (carry_lon[:, 1:] - carry_lon[:, :-1]) / LON_SPACING
        - (push_lat[1:] - push_lat[:-1]) / LAT_SPACING
    )
    return (rate_surface, rate_east, rate_north)


def from_below(values, stride, along_axis, filler):
    length = values.shape[along_axis]
    padding = jnp.full_like(slab_of(values, 0, stride, along_axis), filler)
    return jnp.concatenate([padding, slab_of(values, 0, length - stride, along_axis)], along_axis)


def from_above(values, stride, along_axis, filler):
    length = values.shape[along_axis]
    padding = jnp.full_like(slab_of(values, 0, stride, along_axis), filler)
    return jnp.concatenate([slab_of(values, stride, length, along_axis), padding], along_axis)


def reduce_lines(lower_band, main_band, upper_band, rights, along_axis):
    length = rights.shape[along_axis]
    position = lax.broadcasted_iota(jnp.int32, rights.shape, along_axis)
    stride = 1
    for _ in range(PCR_STEPS):
        def from_lower(values, fill):
            return jnp.where(position >= stride, pltpu.roll(values, stride, along_axis), fill)

        def from_upper(values, fill):
            return jnp.where(
                position < length - stride, pltpu.roll(values, length - stride, along_axis), fill
            )

        below = [from_lower(band, fill) for band, fill in
                 ((lower_band, 0.0), (main_band, 1.0), (upper_band, 0.0), (rights, 0.0))]
        above = [from_upper(band, fill) for band, fill in
                 ((lower_band, 0.0), (main_band, 1.0), (upper_band, 0.0), (rights, 0.0))]
        weight_below = lower_band / below[1]
        weight_above = upper_band / above[1]
        new_lower = -weight_below * below[0]
        new_main = main_band - weight_below * below[2] - weight_above * above[0]
        new_upper = -weight_above * above[2]
        rights = rights - weight_below * below[3] - weight_above * above[3]
        lower_band, main_band, upper_band = new_lower, new_main, new_upper
        stride = stride * 2
    return rights / main_band


def tendency_body(surface_ref, east_ref, north_ref, depth_ref, wet_ref, place_ref, layout,
                  first_row, used_cols, tile_offset):
    rows, cols, box_rows, region_above, tile_rows, count = layout
    place = place_ref[0]
    depth = depth_ref[pl.ds(first_row, rows), :]
    surface = surface_ref[pl.ds(first_row, rows), :]
    coef = depth * depth / (3.0 * LON_SPACING * LON_SPACING)
    keep = lax.broadcasted_iota(jnp.int32, depth.shape, 1) < used_cols
    rights = east_ref[pl.ds(first_row, rows), :] / (depth + surface)
    east_raw = reduce_lines(
        jnp.where(keep, -coef, 0.0),
        jnp.where(keep, 1.0 + 2.0 * coef, 1.0),
        jnp.where(keep, -coef, 0.0),
        jnp.where(keep, rights, 0.0),
        1,
    )
    full_depth = depth_ref[...]
    coef = full_depth * full_depth / (3.0 * LAT_SPACING * LAT_SPACING)
    box_row = lax.broadcasted_iota(jnp.int32, depth_ref.shape, 0)
    global_row = place * tile_rows - region_above - tile_offset[0] + box_row
    keep = (global_row >= 0) & (global_row < count * tile_rows) & (box_row < box_rows)
    rights = north_ref[...] / (full_depth + surface_ref[...])
    north_raw = reduce_lines(
        jnp.where(keep, -coef, 0.0),
        jnp.where(keep, 1.0 + 2.0 * coef, 1.0),
        jnp.where(keep, -coef, 0.0),
        jnp.where(keep, rights, 0.0),
        0,
    )[first_row : first_row + rows]

    def wrapped(values):
        values = pltpu.roll(values, rows - (tile_offset[0] - first_row), 0)
        return pltpu.roll(values, cols - tile_offset[1], 1)

    wet = wrapped(wet_ref[pl.ds(first_row, rows), :])
    surface = wrapped(surface)
    depth = wrapped(depth)
    velocity_u = wet * wrapped(east_raw)
    velocity_v = wet * wrapped(north_raw)
    wrapped_row = lax.broadcasted_iota(jnp.int32, (rows, cols), 0)
    tile_row = jnp.where(wrapped_row >= rows - 2, wrapped_row - rows, wrapped_row) - region_above
    top = place == 0
    bottom = place == count - 1
    for wall, row, shift in (
        (top, -1, rows - 1), (top, -2, rows - 3), (bottom, tile_rows, 1), (bottom, tile_rows + 1, 3)
    ):
        velocity_v = jnp.where(
            wall & (tile_row == row), -pltpu.roll(velocity_v, shift, 0), velocity_v
        )

    def east_of(values):
        return pltpu.roll(values, cols - 1, 1)

    def west_of(values):
        return pltpu.roll(values, 1, 1)

    def north_of(values):
        return pltpu.roll(values, rows - 1, 0)

    def south_of(values):
        return pltpu.roll(values, 1, 0)

    def face_pair(values, later, earlier):
        jump = later(values) - values
        slope = limited(earlier(jump), jump)
        return values + 0.5 * slope, later(values - 0.5 * slope)

    surface_pair = face_pair(surface, east_of, west_of)
    east_pair = face_pair(velocity_u, east_of, west_of)
    north_pair = face_pair(velocity_v, east_of, west_of)
    depth_lon = 0.5 * (depth + east_of(depth))
    open_lon = wet * east_of(wet)
    mass_lon, push_lon, carry_lon = wave_flux(
        surface_pair[0], surface_pair[1], east_pair[0], east_pair[1],
        north_pair[0], north_pair[1], depth_lon, open_lon,
    )
    surface_pair = face_pair(surface, north_of, south_of)
    east_pair = face_pair(velocity_u, north_of, south_of)
    north_pair = face_pair(velocity_v, north_of, south_of)
    depth_lat = 0.5 * (depth + north_of(depth))
    open_lat = wet * north_of(wet)
    mass_lat, push_lat, carry_lat = wave_flux(
        surface_pair[0], surface_pair[1], north_pair[0], north_pair[1],
        east_pair[0], east_pair[1], depth_lat, open_lat,
    )
    rate_surface = (
        -(mass_lon - west_of(mass_lon)) / LON_SPACING - (mass_lat - south_of(mass_lat)) / LAT_SPACING
    )
    source_east = GRAVITY * surface * (depth_lon - west_of(depth_lon)) / LON_SPACING
    source_north = GRAVITY * surface * (depth_lat - south_of(depth_lat)) / LAT_SPACING
    rate_east = wet * (
        source_east
        - (push_lon - west_of(push_lon)) / LON_SPACING
        - (carry_lat - south_of(carry_lat)) / LAT_SPACING
    )
    rate_north = wet * (
        source_north
        - (carry_lon - west_of(carry_lon)) / LON_SPACING
        - (push_lat - south_of(push_lat)) / LAT_SPACING
    )
    return (rate_surface, rate_east, rate_north), (surface, velocity_u, velocity_v), wrapped


def section_kernel(surface_ref, east_ref, north_ref, depth_ref, wet_ref, place_ref,
                   lift_ref, start_surface, start_east, start_north,
                   *outs, first_row, used_cols, tile_offset, weights, layout):
    tile_rows, tile_cols = lift_ref.shape
    rates, (surface, velocity_u, velocity_v), wrapped = tendency_body(
        surface_ref, east_ref, north_ref, depth_ref, wet_ref, place_ref, layout,
        first_row, used_cols, tile_offset,
    )
    rows = layout[0]
    nows = (
        surface,
        wrapped(east_ref[pl.ds(first_row, rows), :]),
        wrapped(north_ref[pl.ds(first_row, rows), :]),
    )
    first, second = weights
    rates = (
        rates[0][:tile_rows, :tile_cols] + lift_ref[...],
        rates[1][:tile_rows, :tile_cols],
        rates[2][:tile_rows, :tile_cols],
    )
    if len(outs) == 3:
        next_state, east_out, north_out = outs
        nexts = (next_state.at[0], next_state.at[1], next_state.at[2])
    else:
        next_surface, next_east, next_north, east_out, north_out = outs
        nexts = (next_surface, next_east, next_north)
    for out, start, now, rate in zip(
        nexts, (start_surface, start_east, start_north), nows, rates
    ):
        out[...] = first * start[...] + second * (now[:tile_rows, :tile_cols] + TIME_STEP * rate)
    east_out[...] = velocity_u[:tile_rows, :tile_cols]
    north_out[...] = velocity_v[:tile_rows, :tile_cols]


def ring_kernel(surface_ref, east_ref, north_ref, depth_ref, wet_ref, place_ref,
                lift_ref, next_state, depth_out, wet_out, *,
                first_row, used_cols, tile_offset, layout):
    rows = layout[0]
    out_rows, out_cols = depth_out.shape
    rates, (surface, _, _), wrapped = tendency_body(
        surface_ref, east_ref, north_ref, depth_ref, wet_ref, place_ref, layout,
        first_row, used_cols, tile_offset,
    )
    lift = wrapped(lift_ref[pl.ds(first_row, rows), :])
    nows = (
        surface,
        wrapped(east_ref[pl.ds(first_row, rows), :]),
        wrapped(north_ref[pl.ds(first_row, rows), :]),
    )
    rates = (rates[0] + lift, rates[1], rates[2])
    for k, (now, rate) in enumerate(zip(nows, rates)):
        next_state[k] = (0.0 * now + 1.0 * (now + TIME_STEP * rate))[:out_rows, :out_cols]
    depth_out[...] = wrapped(depth_ref[pl.ds(first_row, rows), :])[:out_rows, :out_cols]
    wet_out[...] = wrapped(wet_ref[pl.ds(first_row, rows), :])[:out_rows, :out_cols]


def ring_step(fields, place, layout, out_shape, first_row, used_cols, tile_offset):
    spec = pl.BlockSpec(memory_space=pltpu.VMEM)
    scalar = pl.BlockSpec(memory_space=pltpu.SMEM)
    shape = jax.ShapeDtypeStruct(out_shape, jnp.float32)
    return pl.pallas_call(
        lambda *refs: ring_kernel(
            *refs, first_row=first_row, used_cols=used_cols, tile_offset=tile_offset,
            layout=layout,
        ),
        out_shape=(jax.ShapeDtypeStruct((3,) + out_shape, jnp.float32), shape, shape),
        in_specs=[spec] * 5 + [scalar, spec],
        out_specs=(spec,) * 3,
        name="ring_step",
    )(*fields[:5], place, fields[5])


def section_step(fields, place, layout, lift, initial, first_row, used_cols, tile_offset,
                 weights, stacked_out):
    spec = pl.BlockSpec(memory_space=pltpu.VMEM)
    scalar = pl.BlockSpec(memory_space=pltpu.SMEM)
    shape = jax.ShapeDtypeStruct(lift.shape, jnp.float32)
    return pl.pallas_call(
        lambda *refs: section_kernel(
            *refs, first_row=first_row, used_cols=used_cols, tile_offset=tile_offset,
            weights=weights, layout=layout,
        ),
        out_shape=(
            (jax.ShapeDtypeStruct((3,) + lift.shape, jnp.float32), shape, shape)
            if stacked_out else (shape,) * 5
        ),
        in_specs=[spec] * 5 + [scalar] + [spec] * 4,
        out_specs=(spec,) * (3 if stacked_out else 5),
        name="section_step",
    )(*fields, place, lift, *initial)


def stack_kernel(*refs):
    for k, field in enumerate(refs[:-1]):
        refs[-1][k] = field[...]


def stacked(fields):
    spec = pl.BlockSpec(memory_space=pltpu.VMEM)
    return pl.pallas_call(
        stack_kernel,
        out_shape=jax.ShapeDtypeStruct((len(fields),) + fields[0].shape, jnp.float32),
        in_specs=[spec] * len(fields),
        out_specs=spec,
        name="stacked",
    )(*fields)


def halo_box(fields, wide_x, wide_y, place, count, padded_shape):
    lon_count = lax.axis_size("lon")
    west = lax.ppermute(
        fields[:, :, -wide_x:], "lon", [(i, (i + 1) % lon_count) for i in range(lon_count)]
    )
    east = lax.ppermute(
        fields[:, :, :wide_x], "lon", [((i + 1) % lon_count, i) for i in range(lon_count)]
    )
    wide = jnp.concatenate([west, fields, east], axis=2)
    above = passed_along(wide[:, -wide_y:], "lat", 1)
    below = passed_along(wide[:, :wide_y], "lat", -1)
    above = jnp.where(place == 0, wide[:, wide_y - 1 :: -1], above)
    below = jnp.where(place == count - 1, wide[:, : -wide_y - 1 : -1], below)
    box = jnp.concatenate([above, wide, below], axis=1)
    return pad_to(box, padded_shape)


def pad_to(values, shape):
    widths = [(0, 0)] * (values.ndim - 2) + [
        (0, want - have) for want, have in zip(shape, values.shape[-2:])
    ]
    return jnp.pad(values, widths)


def wall_mirrored(values, halo, place, count, rows):
    top = jnp.concatenate([values[..., 2 * halo - 1 : halo - 1 : -1, :], values[..., halo:, :]], axis=-2)
    values = jnp.where(place == 0, top, values)
    bottom = jnp.concatenate(
        [
            values[..., : rows - halo, :],
            values[..., rows - halo - 1 : rows - 2 * halo - 1 : -1, :],
            values[..., rows:, :],
        ],
        axis=-2,
    )
    return jnp.where(place == count - 1, bottom, values)


class Geometry:
    def __init__(self, out_rows, out_cols, halo_y, halo_x):
        self.box_rows = out_rows + 2 * halo_y
        self.box_cols = out_cols + 2 * halo_x
        self.first_row = (halo_y - 2) // 8 * 8
        self.rows = -(-(halo_y + out_rows + 2 - self.first_row) // 8) * 8
        self.padded = (
            max(-(-self.box_rows // 8) * 8, self.first_row + self.rows),
            -(-self.box_cols // 128) * 128,
        )
        self.offset = (halo_y, halo_x)

    def masks(self, region_above, place, count, tile_rows):
        box_row = lax.broadcasted_iota(jnp.int32, self.padded, 0)
        global_row = place * tile_rows - region_above - self.offset[0] + box_row
        inside = (global_row >= 0) & (global_row < count * tile_rows) & (box_row < self.box_rows)
        wrapped_row = lax.broadcasted_iota(jnp.int32, (self.rows, self.padded[1]), 0)
        tile_row = jnp.where(wrapped_row >= self.rows - 2, wrapped_row - self.rows, wrapped_row)
        tile_row = tile_row - region_above
        top = place == 0
        bottom = place == count - 1
        mirror = jnp.where(
            top & (tile_row == -1), 1,
            jnp.where(top & (tile_row == -2), 2,
            jnp.where(bottom & (tile_row == tile_rows), 3,
            jnp.where(bottom & (tile_row == tile_rows + 1), 4, 0))),
        ).astype(jnp.int32)
        return inside.astype(jnp.float32), mirror


def local(surface, momentum_x, momentum_y, water_depth, wet_mask, slide_cells, slide_rate):
    wet_float = wet_mask.astype(jnp.float32)
    place = lax.axis_index("lat")
    count = lax.axis_size("lat")
    tile_rows, tile_cols = surface.shape
    wide_x = WINDOW_LON + 2
    wide_y = WINDOW_LAT + 2
    lift = (
        jnp.zeros((tile_rows * tile_cols,), jnp.float32)
        .at[slide_cells.reshape(-1)]
        .add(slide_rate.reshape(-1))
        .reshape(tile_rows, tile_cols)
    )
    ring = Geometry(tile_rows + 2 * wide_y, tile_cols + 2 * wide_x, wide_y, wide_x)
    plain = Geometry(tile_rows, tile_cols, wide_y, wide_x)
    place_array = jnp.reshape(place, (1,)).astype(jnp.int32)
    ring_layout = (ring.rows, ring.padded[1], ring.box_rows, wide_y, tile_rows, count)
    plain_layout = (plain.rows, plain.padded[1], plain.box_rows, 0, tile_rows, count)
    initial = (surface, momentum_x, momentum_y)

    big = halo_box(
        stacked([surface, momentum_x, momentum_y, water_depth, wet_float, lift]),
        2 * wide_x, 2 * wide_y, place, count, ring.padded,
    )
    ring_state = ring_step(
        tuple(big[k] for k in range(6)), place_array, ring_layout, plain.padded,
        ring.first_row, ring.box_cols, ring.offset,
    )
    box = wall_mirrored(ring_state[0], wide_y, place, count, plain.box_rows)
    depth_box, wet_box = ring_state[1], ring_state[2]
    second_state = section_step(
        (box[0], box[1], box[2], depth_box, wet_box), place_array, plain_layout, lift, initial,
        plain.first_row, plain.box_cols, plain.offset, (0.75, 0.25), True,
    )[0]
    box = halo_box(second_state, wide_x, wide_y, place, count, plain.padded)
    return section_step(
        (box[0], box[1], box[2], depth_box, wet_box), place_array, plain_layout, lift, initial,
        plain.first_row, plain.box_cols, plain.offset, (1.0 / 3.0, 2.0 / 3.0), False,
    )


def solution(mesh):
    in_specs = (P("lat", "lon"),) * 7
    out_specs = (P("lat", "lon"),) * 5
    return jax.shard_map(local, mesh=mesh, in_specs=in_specs, out_specs=out_specs, check_vma=False)
```

```python
import jax
import jax.numpy as jnp
from jax import lax
from jax.sharding import PartitionSpec as P
from jax.experimental import pallas as pl
from jax.experimental.pallas import tpu as pltpu

GRAVITY = 1.0
LON_SPACING = 0.5
LAT_SPACING = 0.6
TIME_STEP = 0.1
WINDOW_LON = 40
WINDOW_LAT = 32
PCR_STEPS = 6


def shifted(block, axis, distance):
    devices = range(lax.axis_size(axis))
    route = [((i - distance) % len(devices), i) for i in devices]
    return lax.ppermute(block, axis, route)


def passed_along(x, axis, by):
    peers = lax.axis_size(axis)
    pairs = [(i, i + by) for i in range(peers) if 0 <= i + by < peers]
    return lax.ppermute(x, axis, pairs)


def extended(cells, sides, width, closed):
    for axis, dim in sides:
        count = lax.axis_size(axis)
        ends = count if closed else count - 1
        head = lax.slice_in_dim(cells, 0, width, axis=dim)
        tail = lax.slice_in_dim(cells, cells.shape[dim] - width, cells.shape[dim], axis=dim)
        cells = jnp.concatenate(
            [
                lax.ppermute(tail, axis, [(i, (i + 1) % count) for i in range(ends)]),
                cells,
                lax.ppermute(head, axis, [((i + 1) % count, i) for i in range(ends)]),
            ],
            axis=dim,
        )
    return cells


def slab_of(values, start, stop, along_axis):
    return lax.slice_in_dim(values, start, stop, axis=along_axis)


def limited(former, latter):
    return jnp.maximum(jnp.minimum(former, latter), 0.0) + jnp.minimum(
        jnp.maximum(former, latter), 0.0
    )


def face_states(values, along_axis):
    length = values.shape[along_axis]
    jumps = slab_of(values, 1, length, along_axis) - slab_of(values, 0, length - 1, along_axis)
    slopes = limited(
        slab_of(jumps, 0, length - 2, along_axis), slab_of(jumps, 1, length - 1, along_axis)
    )
    left_state = slab_of(values, 1, length - 2, along_axis) + 0.5 * slab_of(
        slopes, 0, length - 3, along_axis
    )
    right_state = slab_of(values, 2, length - 1, along_axis) - 0.5 * slab_of(
        slopes, 1, length - 2, along_axis
    )
    return (left_state, right_state)


def wave_flux(
    surface_left,
    surface_right,
    normal_left,
    normal_right,
    tangent_left,
    tangent_right,
    face_depth,
    opened,
):
    height_left = surface_left + face_depth
    height_right = surface_right + face_depth
    celerity_left = jnp.sqrt(GRAVITY * height_left)
    celerity_right = jnp.sqrt(GRAVITY * height_right)
    slowest = jnp.minimum(
        jnp.minimum(normal_left - celerity_left, normal_right - celerity_right), 0.0
    )
    fastest = jnp.maximum(
        jnp.maximum(normal_left + celerity_left, normal_right + celerity_right), 0.0
    )
    spread = fastest - slowest
    product = slowest * fastest
    mass_left = height_left * normal_left
    mass_right = height_right * normal_right
    push_left = mass_left * normal_left + GRAVITY * (
        0.5 * surface_left * surface_left + face_depth * surface_left
    )
    push_right = mass_right * normal_right + GRAVITY * (
        0.5 * surface_right * surface_right + face_depth * surface_right
    )
    carry_left = mass_left * tangent_left
    carry_right = mass_right * tangent_right
    mass_flux = (
        opened
        * (fastest * mass_left - slowest * mass_right + product * (surface_right - surface_left))
        / spread
    )
    push_flux = (
        opened
        * (fastest * push_left - slowest * push_right + product * (mass_right - mass_left))
        / spread
    )
    carry_flux = (
        opened
        * (
            fastest * carry_left
            - slowest * carry_right
            + product * (height_right * tangent_right - height_left * tangent_left)
        )
        / spread
    )
    return (mass_flux, push_flux, carry_flux)


def tendencies(across, along):
    width = across[0].shape[1] - 4
    row_count = along[0].shape[0] - 4
    surface_pair = face_states(across[0], 1)
    east_pair = face_states(across[1], 1)
    north_pair = face_states(across[2], 1)
    depth_lon = 0.5 * (across[3][:, 1 : width + 2] + across[3][:, 2 : width + 3])
    open_lon = across[4][:, 1 : width + 2] * across[4][:, 2 : width + 3]
    mass_lon, push_lon, carry_lon = wave_flux(
        surface_pair[0],
        surface_pair[1],
        east_pair[0],
        east_pair[1],
        north_pair[0],
        north_pair[1],
        depth_lon,
        open_lon,
    )
    surface_pair = face_states(along[0], 0)
    east_pair = face_states(along[1], 0)
    north_pair = face_states(along[2], 0)
    depth_lat = 0.5 * (along[3][1 : row_count + 2] + along[3][2 : row_count + 3])
    open_lat = along[4][1 : row_count + 2] * along[4][2 : row_count + 3]
    mass_lat, push_lat, carry_lat = wave_flux(
        surface_pair[0],
        surface_pair[1],
        north_pair[0],
        north_pair[1],
        east_pair[0],
        east_pair[1],
        depth_lat,
        open_lat,
    )
    surface_mid = across[0][:, 2 : width + 2]
    wet_mid = across[4][:, 2 : width + 2]
    rate_surface = (
        -(mass_lon[:, 1:] - mass_lon[:, :-1]) / LON_SPACING
        - (mass_lat[1:] - mass_lat[:-1]) / LAT_SPACING
    )
    source_east = GRAVITY * surface_mid * (depth_lon[:, 1:] - depth_lon[:, :-1]) / LON_SPACING
    source_north = GRAVITY * surface_mid * (depth_lat[1:] - depth_lat[:-1]) / LAT_SPACING
    rate_east = wet_mid * (
        source_east
        - (push_lon[:, 1:] - push_lon[:, :-1]) / LON_SPACING
        - (carry_lat[1:] - carry_lat[:-1]) / LAT_SPACING
    )
    rate_north = wet_mid * (
        source_north
        - (carry_lon[:, 1:] - carry_lon[:, :-1]) / LON_SPACING
        - (push_lat[1:] - push_lat[:-1]) / LAT_SPACING
    )
    return (rate_surface, rate_east, rate_north)


def from_below(values, stride, along_axis, filler):
    length = values.shape[along_axis]
    padding = jnp.full_like(slab_of(values, 0, stride, along_axis), filler)
    return jnp.concatenate([padding, slab_of(values, 0, length - stride, along_axis)], along_axis)


def from_above(values, stride, along_axis, filler):
    length = values.shape[along_axis]
    padding = jnp.full_like(slab_of(values, 0, stride, along_axis), filler)
    return jnp.concatenate([slab_of(values, stride, length, along_axis), padding], along_axis)


def reduce_lines(lower_band, main_band, upper_band, rights, along_axis):
    length = rights.shape[along_axis]
    position = lax.broadcasted_iota(jnp.int32, rights.shape, along_axis)
    stride = 1
    for _ in range(PCR_STEPS):
        def from_lower(values, fill):
            return jnp.where(position >= stride, pltpu.roll(values, stride, along_axis), fill)

        def from_upper(values, fill):
            return jnp.where(
                position < length - stride, pltpu.roll(values, length - stride, along_axis), fill
            )

        below = [from_lower(band, fill) for band, fill in
                 ((lower_band, 0.0), (main_band, 1.0), (upper_band, 0.0), (rights, 0.0))]
        above = [from_upper(band, fill) for band, fill in
                 ((lower_band, 0.0), (main_band, 1.0), (upper_band, 0.0), (rights, 0.0))]
        weight_below = lower_band / below[1]
        weight_above = upper_band / above[1]
        new_lower = -weight_below * below[0]
        new_main = main_band - weight_below * below[2] - weight_above * above[0]
        new_upper = -weight_above * above[2]
        rights = rights - weight_below * below[3] - weight_above * above[3]
        lower_band, main_band, upper_band = new_lower, new_main, new_upper
        stride = stride * 2
    return rights / main_band


def tendency_body(surface_ref, east_ref, north_ref, depth_ref, wet_ref, place_ref, layout,
                  first_row, used_cols, tile_offset):
    rows, cols, box_rows, region_above, tile_rows, count = layout
    place = place_ref[0]
    depth = depth_ref[pl.ds(first_row, rows), :]
    surface = surface_ref[pl.ds(first_row, rows), :]
    coef = depth * depth / (3.0 * LON_SPACING * LON_SPACING)
    keep = lax.broadcasted_iota(jnp.int32, depth.shape, 1) < used_cols
    rights = east_ref[pl.ds(first_row, rows), :] / (depth + surface)
    east_raw = reduce_lines(
        jnp.where(keep, -coef, 0.0),
        jnp.where(keep, 1.0 + 2.0 * coef, 1.0),
        jnp.where(keep, -coef, 0.0),
        jnp.where(keep, rights, 0.0),
        1,
    )
    full_depth = depth_ref[...]
    coef = full_depth * full_depth / (3.0 * LAT_SPACING * LAT_SPACING)
    box_row = lax.broadcasted_iota(jnp.int32, depth_ref.shape, 0)
    global_row = place * tile_rows - region_above - tile_offset[0] + box_row
    keep = (global_row >= 0) & (global_row < count * tile_rows) & (box_row < box_rows)
    rights = north_ref[...] / (full_depth + surface_ref[...])
    north_raw = reduce_lines(
        jnp.where(keep, -coef, 0.0),
        jnp.where(keep, 1.0 + 2.0 * coef, 1.0),
        jnp.where(keep, -coef, 0.0),
        jnp.where(keep, rights, 0.0),
        0,
    )[first_row : first_row + rows]

    def wrapped(values):
        values = pltpu.roll(values, rows - (tile_offset[0] - first_row), 0)
        return pltpu.roll(values, cols - tile_offset[1], 1)

    wet = wrapped(wet_ref[pl.ds(first_row, rows), :])
    surface = wrapped(surface)
    depth = wrapped(depth)
    velocity_u = wet * wrapped(east_raw)
    velocity_v = wet * wrapped(north_raw)
    wrapped_row = lax.broadcasted_iota(jnp.int32, (rows, cols), 0)
    tile_row = jnp.where(wrapped_row >= rows - 2, wrapped_row - rows, wrapped_row) - region_above
    top = place == 0
    bottom = place == count - 1
    for wall, row, shift in (
        (top, -1, rows - 1), (top, -2, rows - 3), (bottom, tile_rows, 1), (bottom, tile_rows + 1, 3)
    ):
        velocity_v = jnp.where(
            wall & (tile_row == row), -pltpu.roll(velocity_v, shift, 0), velocity_v
        )

    def east_of(values):
        return pltpu.roll(values, cols - 1, 1)

    def west_of(values):
        return pltpu.roll(values, 1, 1)

    def north_of(values):
        return pltpu.roll(values, rows - 1, 0)

    def south_of(values):
        return pltpu.roll(values, 1, 0)

    def face_pair(values, later, earlier):
        jump = later(values) - values
        slope = limited(earlier(jump), jump)
        return values + 0.5 * slope, later(values - 0.5 * slope)

    surface_pair = face_pair(surface, east_of, west_of)
    east_pair = face_pair(velocity_u, east_of, west_of)
    north_pair = face_pair(velocity_v, east_of, west_of)
    depth_lon = 0.5 * (depth + east_of(depth))
    open_lon = wet * east_of(wet)
    mass_lon, push_lon, carry_lon = wave_flux(
        surface_pair[0], surface_pair[1], east_pair[0], east_pair[1],
        north_pair[0], north_pair[1], depth_lon, open_lon,
    )
    surface_pair = face_pair(surface, north_of, south_of)
    east_pair = face_pair(velocity_u, north_of, south_of)
    north_pair = face_pair(velocity_v, north_of, south_of)
    depth_lat = 0.5 * (depth + north_of(depth))
    open_lat = wet * north_of(wet)
    mass_lat, push_lat, carry_lat = wave_flux(
        surface_pair[0], surface_pair[1], north_pair[0], north_pair[1],
        east_pair[0], east_pair[1], depth_lat, open_lat,
    )
    rate_surface = (
        -(mass_lon - west_of(mass_lon)) / LON_SPACING - (mass_lat - south_of(mass_lat)) / LAT_SPACING
    )
    source_east = GRAVITY * surface * (depth_lon - west_of(depth_lon)) / LON_SPACING
    source_north = GRAVITY * surface * (depth_lat - south_of(depth_lat)) / LAT_SPACING
    rate_east = wet * (
        source_east
        - (push_lon - west_of(push_lon)) / LON_SPACING
        - (carry_lat - south_of(carry_lat)) / LAT_SPACING
    )
    rate_north = wet * (
        source_north
        - (carry_lon - west_of(carry_lon)) / LON_SPACING
        - (push_lat - south_of(push_lat)) / LAT_SPACING
    )
    return (rate_surface, rate_east, rate_north), (surface, velocity_u, velocity_v), wrapped


def section_kernel(surface_ref, east_ref, north_ref, depth_ref, wet_ref, place_ref,
                   lift_ref, start_surface, start_east, start_north,
                   next_surface, next_east, next_north, east_out, north_out, *,
                   first_row, used_cols, tile_offset, weights, layout):
    tile_rows, tile_cols = lift_ref.shape
    rates, (surface, velocity_u, velocity_v), wrapped = tendency_body(
        surface_ref, east_ref, north_ref, depth_ref, wet_ref, place_ref, layout,
        first_row, used_cols, tile_offset,
    )
    rows = layout[0]
    nows = (
        surface,
        wrapped(east_ref[pl.ds(first_row, rows), :]),
        wrapped(north_ref[pl.ds(first_row, rows), :]),
    )
    first, second = weights
    rates = (
        rates[0][:tile_rows, :tile_cols] + lift_ref[...],
        rates[1][:tile_rows, :tile_cols],
        rates[2][:tile_rows, :tile_cols],
    )
    for out, start, now, rate in zip(
        (next_surface, next_east, next_north),
        (start_surface, start_east, start_north),
        nows,
        rates,
    ):
        out[...] = first * start[...] + second * (now[:tile_rows, :tile_cols] + TIME_STEP * rate)
    east_out[...] = velocity_u[:tile_rows, :tile_cols]
    north_out[...] = velocity_v[:tile_rows, :tile_cols]


def ring_kernel(surface_ref, east_ref, north_ref, depth_ref, wet_ref, place_ref,
                lift_ref, next_surface, next_east, next_north, depth_out, wet_out, *,
                first_row, used_cols, tile_offset, layout):
    rows = layout[0]
    out_rows, out_cols = next_surface.shape
    rates, (surface, _, _), wrapped = tendency_body(
        surface_ref, east_ref, north_ref, depth_ref, wet_ref, place_ref, layout,
        first_row, used_cols, tile_offset,
    )
    lift = wrapped(lift_ref[pl.ds(first_row, rows), :])
    nows = (
        surface,
        wrapped(east_ref[pl.ds(first_row, rows), :]),
        wrapped(north_ref[pl.ds(first_row, rows), :]),
    )
    rates = (rates[0] + lift, rates[1], rates[2])
    for out, now, rate in zip((next_surface, next_east, next_north), nows, rates):
        out[...] = (0.0 * now + 1.0 * (now + TIME_STEP * rate))[:out_rows, :out_cols]
    depth_out[...] = wrapped(depth_ref[pl.ds(first_row, rows), :])[:out_rows, :out_cols]
    wet_out[...] = wrapped(wet_ref[pl.ds(first_row, rows), :])[:out_rows, :out_cols]


def ring_step(fields, place, layout, out_shape, first_row, used_cols, tile_offset):
    spec = pl.BlockSpec(memory_space=pltpu.VMEM)
    scalar = pl.BlockSpec(memory_space=pltpu.SMEM)
    shape = jax.ShapeDtypeStruct(out_shape, jnp.float32)
    return pl.pallas_call(
        lambda *refs: ring_kernel(
            *refs, first_row=first_row, used_cols=used_cols, tile_offset=tile_offset,
            layout=layout,
        ),
        out_shape=(shape,) * 5,
        in_specs=[spec] * 5 + [scalar, spec],
        out_specs=(spec,) * 5,
        name="ring_step",
    )(*fields[:5], place, fields[5])


def section_step(fields, place, layout, lift, initial, first_row, used_cols, tile_offset,
                 weights):
    spec = pl.BlockSpec(memory_space=pltpu.VMEM)
    scalar = pl.BlockSpec(memory_space=pltpu.SMEM)
    shape = jax.ShapeDtypeStruct(lift.shape, jnp.float32)
    return pl.pallas_call(
        lambda *refs: section_kernel(
            *refs, first_row=first_row, used_cols=used_cols, tile_offset=tile_offset,
            weights=weights, layout=layout,
        ),
        out_shape=(shape,) * 5,
        in_specs=[spec] * 5 + [scalar] + [spec] * 4,
        out_specs=(spec,) * 5,
        name="section_step",
    )(*fields, place, lift, *initial)


def halo_box(fields, wide_x, wide_y, place, count, padded_shape):
    lon_count = lax.axis_size("lon")
    above = passed_along(fields[:, -wide_y:], "lat", 1)
    below = passed_along(fields[:, :wide_y], "lat", -1)
    above = jnp.where(place == 0, fields[:, wide_y - 1 :: -1], above)
    below = jnp.where(place == count - 1, fields[:, : -wide_y - 1 : -1], below)
    tall = jnp.concatenate([above, fields, below], axis=1)
    west = lax.ppermute(
        tall[:, :, -wide_x:], "lon", [(i, (i + 1) % lon_count) for i in range(lon_count)]
    )
    east = lax.ppermute(
        tall[:, :, :wide_x], "lon", [((i + 1) % lon_count, i) for i in range(lon_count)]
    )
    box = jnp.concatenate([west, tall, east], axis=2)
    return pad_to(box, padded_shape)


def pad_to(values, shape):
    widths = [(0, 0)] * (values.ndim - 2) + [
        (0, want - have) for want, have in zip(shape, values.shape[-2:])
    ]
    return jnp.pad(values, widths)


def wall_mirrored(values, halo, place, count, rows):
    top = jnp.concatenate([values[..., 2 * halo - 1 : halo - 1 : -1, :], values[..., halo:, :]], axis=-2)
    values = jnp.where(place == 0, top, values)
    bottom = jnp.concatenate(
        [
            values[..., : rows - halo, :],
            values[..., rows - halo - 1 : rows - 2 * halo - 1 : -1, :],
            values[..., rows:, :],
        ],
        axis=-2,
    )
    return jnp.where(place == count - 1, bottom, values)


class Geometry:
    def __init__(self, out_rows, out_cols, halo_y, halo_x):
        self.box_rows = out_rows + 2 * halo_y
        self.box_cols = out_cols + 2 * halo_x
        self.first_row = (halo_y - 2) // 8 * 8
        self.rows = -(-(halo_y + out_rows + 2 - self.first_row) // 8) * 8
        self.padded = (
            max(-(-self.box_rows // 8) * 8, self.first_row + self.rows),
            -(-self.box_cols // 128) * 128,
        )
        self.offset = (halo_y, halo_x)

    def masks(self, region_above, place, count, tile_rows):
        box_row = lax.broadcasted_iota(jnp.int32, self.padded, 0)
        global_row = place * tile_rows - region_above - self.offset[0] + box_row
        inside = (global_row >= 0) & (global_row < count * tile_rows) & (box_row < self.box_rows)
        wrapped_row = lax.broadcasted_iota(jnp.int32, (self.rows, self.padded[1]), 0)
        tile_row = jnp.where(wrapped_row >= self.rows - 2, wrapped_row - self.rows, wrapped_row)
        tile_row = tile_row - region_above
        top = place == 0
        bottom = place == count - 1
        mirror = jnp.where(
            top & (tile_row == -1), 1,
            jnp.where(top & (tile_row == -2), 2,
            jnp.where(bottom & (tile_row == tile_rows), 3,
            jnp.where(bottom & (tile_row == tile_rows + 1), 4, 0))),
        ).astype(jnp.int32)
        return inside.astype(jnp.float32), mirror


def local(surface, momentum_x, momentum_y, water_depth, wet_mask, slide_cells, slide_rate):
    wet_float = wet_mask.astype(jnp.float32)
    place = lax.axis_index("lat")
    count = lax.axis_size("lat")
    tile_rows, tile_cols = surface.shape
    wide_x = WINDOW_LON + 2
    wide_y = WINDOW_LAT + 2
    lift = (
        jnp.zeros((tile_rows * tile_cols,), jnp.float32)
        .at[slide_cells.reshape(-1)]
        .add(slide_rate.reshape(-1))
        .reshape(tile_rows, tile_cols)
    )
    ring = Geometry(tile_rows + 2 * wide_y, tile_cols + 2 * wide_x, wide_y, wide_x)
    plain = Geometry(tile_rows, tile_cols, wide_y, wide_x)
    place_array = jnp.reshape(place, (1,)).astype(jnp.int32)
    ring_layout = (ring.rows, ring.padded[1], ring.box_rows, wide_y, tile_rows, count)
    plain_layout = (plain.rows, plain.padded[1], plain.box_rows, 0, tile_rows, count)
    initial = (surface, momentum_x, momentum_y)

    big = halo_box(
        jnp.stack([surface, momentum_x, momentum_y, water_depth, wet_float, lift]),
        2 * wide_x, 2 * wide_y, place, count, ring.padded,
    )
    ring_state = ring_step(
        tuple(big[k] for k in range(6)), place_array, ring_layout, plain.padded,
        ring.first_row, ring.box_cols, ring.offset,
    )
    box = wall_mirrored(jnp.stack(ring_state[:3]), wide_y, place, count, plain.box_rows)
    depth_box, wet_box = ring_state[3], ring_state[4]
    for first, second in ((0.75, 0.25), (1.0 / 3.0, 2.0 / 3.0)):
        if box is None:
            box = halo_box(jnp.stack(list(current)), wide_x, wide_y, place, count, plain.padded)
        next_surface, next_east, next_north, velocity_u, velocity_v = section_step(
            (box[0], box[1], box[2], depth_box, wet_box), place_array, plain_layout, lift, initial,
            plain.first_row, plain.box_cols, plain.offset, (first, second),
        )
        current = (next_surface, next_east, next_north)
        box = None
    return (current[0], current[1], current[2], velocity_u, velocity_v)


def solution(mesh):
    in_specs = (P("lat", "lon"),) * 7
    out_specs = (P("lat", "lon"),) * 5
    return jax.shard_map(local, mesh=mesh, in_specs=in_specs, out_specs=out_specs, check_vma=False)
```

```python
import jax
import jax.numpy as jnp
from jax import lax
from jax.sharding import PartitionSpec as P
from jax.experimental import pallas as pl
from jax.experimental.pallas import tpu as pltpu

GRAVITY = 1.0
LON_SPACING = 0.5
LAT_SPACING = 0.6
TIME_STEP = 0.1
WINDOW_LON = 40
WINDOW_LAT = 32
PCR_STEPS = (5, 6)


def shifted(block, axis, distance):
    devices = range(lax.axis_size(axis))
    route = [((i - distance) % len(devices), i) for i in devices]
    return lax.ppermute(block, axis, route)


def passed_along(x, axis, by):
    peers = lax.axis_size(axis)
    pairs = [(i, i + by) for i in range(peers) if 0 <= i + by < peers]
    return lax.ppermute(x, axis, pairs)


def extended(cells, sides, width, closed):
    for axis, dim in sides:
        count = lax.axis_size(axis)
        ends = count if closed else count - 1
        head = lax.slice_in_dim(cells, 0, width, axis=dim)
        tail = lax.slice_in_dim(cells, cells.shape[dim] - width, cells.shape[dim], axis=dim)
        cells = jnp.concatenate(
            [
                lax.ppermute(tail, axis, [(i, (i + 1) % count) for i in range(ends)]),
                cells,
                lax.ppermute(head, axis, [((i + 1) % count, i) for i in range(ends)]),
            ],
            axis=dim,
        )
    return cells


def slab_of(values, start, stop, along_axis):
    return lax.slice_in_dim(values, start, stop, axis=along_axis)


def limited(former, latter):
    return jnp.maximum(jnp.minimum(former, latter), 0.0) + jnp.minimum(
        jnp.maximum(former, latter), 0.0
    )


def face_states(values, along_axis):
    length = values.shape[along_axis]
    jumps = slab_of(values, 1, length, along_axis) - slab_of(values, 0, length - 1, along_axis)
    slopes = limited(
        slab_of(jumps, 0, length - 2, along_axis), slab_of(jumps, 1, length - 1, along_axis)
    )
    left_state = slab_of(values, 1, length - 2, along_axis) + 0.5 * slab_of(
        slopes, 0, length - 3, along_axis
    )
    right_state = slab_of(values, 2, length - 1, along_axis) - 0.5 * slab_of(
        slopes, 1, length - 2, along_axis
    )
    return (left_state, right_state)


def wave_flux(
    surface_left,
    surface_right,
    normal_left,
    normal_right,
    tangent_left,
    tangent_right,
    face_depth,
    opened,
):
    height_left = surface_left + face_depth
    height_right = surface_right + face_depth
    celerity_left = jnp.sqrt(GRAVITY * height_left)
    celerity_right = jnp.sqrt(GRAVITY * height_right)
    slowest = jnp.minimum(
        jnp.minimum(normal_left - celerity_left, normal_right - celerity_right), 0.0
    )
    fastest = jnp.maximum(
        jnp.maximum(normal_left + celerity_left, normal_right + celerity_right), 0.0
    )
    spread = fastest - slowest
    product = slowest * fastest
    mass_left = height_left * normal_left
    mass_right = height_right * normal_right
    push_left = mass_left * normal_left + GRAVITY * (
        0.5 * surface_left * surface_left + face_depth * surface_left
    )
    push_right = mass_right * normal_right + GRAVITY * (
        0.5 * surface_right * surface_right + face_depth * surface_right
    )
    carry_left = mass_left * tangent_left
    carry_right = mass_right * tangent_right
    mass_flux = (
        opened
        * (fastest * mass_left - slowest * mass_right + product * (surface_right - surface_left))
        / spread
    )
    push_flux = (
        opened
        * (fastest * push_left - slowest * push_right + product * (mass_right - mass_left))
        / spread
    )
    carry_flux = (
        opened
        * (
            fastest * carry_left
            - slowest * carry_right
            + product * (height_right * tangent_right - height_left * tangent_left)
        )
        / spread
    )
    return (mass_flux, push_flux, carry_flux)


def tendencies(across, along):
    width = across[0].shape[1] - 4
    row_count = along[0].shape[0] - 4
    surface_pair = face_states(across[0], 1)
    east_pair = face_states(across[1], 1)
    north_pair = face_states(across[2], 1)
    depth_lon = 0.5 * (across[3][:, 1 : width + 2] + across[3][:, 2 : width + 3])
    open_lon = across[4][:, 1 : width + 2] * across[4][:, 2 : width + 3]
    mass_lon, push_lon, carry_lon = wave_flux(
        surface_pair[0],
        surface_pair[1],
        east_pair[0],
        east_pair[1],
        north_pair[0],
        north_pair[1],
        depth_lon,
        open_lon,
    )
    surface_pair = face_states(along[0], 0)
    east_pair = face_states(along[1], 0)
    north_pair = face_states(along[2], 0)
    depth_lat = 0.5 * (along[3][1 : row_count + 2] + along[3][2 : row_count + 3])
    open_lat = along[4][1 : row_count + 2] * along[4][2 : row_count + 3]
    mass_lat, push_lat, carry_lat = wave_flux(
        surface_pair[0],
        surface_pair[1],
        north_pair[0],
        north_pair[1],
        east_pair[0],
        east_pair[1],
        depth_lat,
        open_lat,
    )
    surface_mid = across[0][:, 2 : width + 2]
    wet_mid = across[4][:, 2 : width + 2]
    rate_surface = (
        -(mass_lon[:, 1:] - mass_lon[:, :-1]) / LON_SPACING
        - (mass_lat[1:] - mass_lat[:-1]) / LAT_SPACING
    )
    source_east = GRAVITY * surface_mid * (depth_lon[:, 1:] - depth_lon[:, :-1]) / LON_SPACING
    source_north = GRAVITY * surface_mid * (depth_lat[1:] - depth_lat[:-1]) / LAT_SPACING
    rate_east = wet_mid * (
        source_east
        - (push_lon[:, 1:] - push_lon[:, :-1]) / LON_SPACING
        - (carry_lat[1:] - carry_lat[:-1]) / LAT_SPACING
    )
    rate_north = wet_mid * (
        source_north
        - (carry_lon[:, 1:] - carry_lon[:, :-1]) / LON_SPACING
        - (push_lat[1:] - push_lat[:-1]) / LAT_SPACING
    )
    return (rate_surface, rate_east, rate_north)


def from_below(values, stride, along_axis, filler):
    length = values.shape[along_axis]
    padding = jnp.full_like(slab_of(values, 0, stride, along_axis), filler)
    return jnp.concatenate([padding, slab_of(values, 0, length - stride, along_axis)], along_axis)


def from_above(values, stride, along_axis, filler):
    length = values.shape[along_axis]
    padding = jnp.full_like(slab_of(values, 0, stride, along_axis), filler)
    return jnp.concatenate([slab_of(values, stride, length, along_axis), padding], along_axis)


def reduce_lines(lower_band, main_band, upper_band, rights, along_axis):
    length = rights.shape[along_axis]
    position = lax.broadcasted_iota(jnp.int32, rights.shape, along_axis)
    stride = 1
    for _ in range(PCR_STEPS[along_axis]):
        def from_lower(values, fill):
            return jnp.where(position >= stride, pltpu.roll(values, stride, along_axis), fill)

        def from_upper(values, fill):
            return jnp.where(
                position < length - stride, pltpu.roll(values, length - stride, along_axis), fill
            )

        below = [from_lower(band, fill) for band, fill in
                 ((lower_band, 0.0), (main_band, 1.0), (upper_band, 0.0), (rights, 0.0))]
        above = [from_upper(band, fill) for band, fill in
                 ((lower_band, 0.0), (main_band, 1.0), (upper_band, 0.0), (rights, 0.0))]
        weight_below = lower_band / below[1]
        weight_above = upper_band / above[1]
        new_lower = -weight_below * below[0]
        new_main = main_band - weight_below * below[2] - weight_above * above[0]
        new_upper = -weight_above * above[2]
        rights = rights - weight_below * below[3] - weight_above * above[3]
        lower_band, main_band, upper_band = new_lower, new_main, new_upper
        stride = stride * 2
    return rights / main_band


def tendency_body(surface_ref, east_ref, north_ref, depth_ref, wet_ref, place_ref, layout,
                  first_row, used_cols, tile_offset):
    rows, cols, box_rows, region_above, tile_rows, count = layout
    place = place_ref[0]
    depth = depth_ref[pl.ds(first_row, rows), :]
    surface = surface_ref[pl.ds(first_row, rows), :]
    coef = depth * depth / (3.0 * LON_SPACING * LON_SPACING)
    keep = lax.broadcasted_iota(jnp.int32, depth.shape, 1) < used_cols
    rights = east_ref[pl.ds(first_row, rows), :] / (depth + surface)
    east_raw = reduce_lines(
        jnp.where(keep, -coef, 0.0),
        jnp.where(keep, 1.0 + 2.0 * coef, 1.0),
        jnp.where(keep, -coef, 0.0),
        jnp.where(keep, rights, 0.0),
        1,
    )
    full_depth = depth_ref[...]
    coef = full_depth * full_depth / (3.0 * LAT_SPACING * LAT_SPACING)
    box_row = lax.broadcasted_iota(jnp.int32, depth_ref.shape, 0)
    global_row = place * tile_rows - region_above - tile_offset[0] + box_row
    keep = (global_row >= 0) & (global_row < count * tile_rows) & (box_row < box_rows)
    rights = north_ref[...] / (full_depth + surface_ref[...])
    north_raw = reduce_lines(
        jnp.where(keep, -coef, 0.0),
        jnp.where(keep, 1.0 + 2.0 * coef, 1.0),
        jnp.where(keep, -coef, 0.0),
        jnp.where(keep, rights, 0.0),
        0,
    )[first_row : first_row + rows]

    def wrapped(values):
        values = pltpu.roll(values, rows - (tile_offset[0] - first_row), 0)
        return pltpu.roll(values, cols - tile_offset[1], 1)

    wet = wrapped(wet_ref[pl.ds(first_row, rows), :])
    surface = wrapped(surface)
    depth = wrapped(depth)
    velocity_u = wet * wrapped(east_raw)
    velocity_v = wet * wrapped(north_raw)
    wrapped_row = lax.broadcasted_iota(jnp.int32, (rows, cols), 0)
    tile_row = jnp.where(wrapped_row >= rows - 2, wrapped_row - rows, wrapped_row) - region_above
    top = place == 0
    bottom = place == count - 1
    for wall, row, shift in (
        (top, -1, rows - 1), (top, -2, rows - 3), (bottom, tile_rows, 1), (bottom, tile_rows + 1, 3)
    ):
        velocity_v = jnp.where(
            wall & (tile_row == row), -pltpu.roll(velocity_v, shift, 0), velocity_v
        )

    def east_of(values):
        return pltpu.roll(values, cols - 1, 1)

    def west_of(values):
        return pltpu.roll(values, 1, 1)

    def north_of(values):
        return pltpu.roll(values, rows - 1, 0)

    def south_of(values):
        return pltpu.roll(values, 1, 0)

    def face_pair(values, later, earlier):
        jump = later(values) - values
        slope = limited(earlier(jump), jump)
        return values + 0.5 * slope, later(values - 0.5 * slope)

    surface_pair = face_pair(surface, east_of, west_of)
    east_pair = face_pair(velocity_u, east_of, west_of)
    north_pair = face_pair(velocity_v, east_of, west_of)
    depth_lon = 0.5 * (depth + east_of(depth))
    open_lon = wet * east_of(wet)
    mass_lon, push_lon, carry_lon = wave_flux(
        surface_pair[0], surface_pair[1], east_pair[0], east_pair[1],
        north_pair[0], north_pair[1], depth_lon, open_lon,
    )
    surface_pair = face_pair(surface, north_of, south_of)
    east_pair = face_pair(velocity_u, north_of, south_of)
    north_pair = face_pair(velocity_v, north_of, south_of)
    depth_lat = 0.5 * (depth + north_of(depth))
    open_lat = wet * north_of(wet)
    mass_lat, push_lat, carry_lat = wave_flux(
        surface_pair[0], surface_pair[1], north_pair[0], north_pair[1],
        east_pair[0], east_pair[1], depth_lat, open_lat,
    )
    rate_surface = (
        -(mass_lon - west_of(mass_lon)) / LON_SPACING - (mass_lat - south_of(mass_lat)) / LAT_SPACING
    )
    source_east = GRAVITY * surface * (depth_lon - west_of(depth_lon)) / LON_SPACING
    source_north = GRAVITY * surface * (depth_lat - south_of(depth_lat)) / LAT_SPACING
    rate_east = wet * (
        source_east
        - (push_lon - west_of(push_lon)) / LON_SPACING
        - (carry_lat - south_of(carry_lat)) / LAT_SPACING
    )
    rate_north = wet * (
        source_north
        - (carry_lon - west_of(carry_lon)) / LON_SPACING
        - (push_lat - south_of(push_lat)) / LAT_SPACING
    )
    return (rate_surface, rate_east, rate_north), (surface, velocity_u, velocity_v), wrapped


def section_kernel(surface_ref, east_ref, north_ref, depth_ref, wet_ref, place_ref,
                   lift_ref, start_surface, start_east, start_north,
                   next_surface, next_east, next_north, east_out, north_out, *,
                   first_row, used_cols, tile_offset, weights, layout):
    tile_rows, tile_cols = lift_ref.shape
    rates, (surface, velocity_u, velocity_v), wrapped = tendency_body(
        surface_ref, east_ref, north_ref, depth_ref, wet_ref, place_ref, layout,
        first_row, used_cols, tile_offset,
    )
    rows = layout[0]
    nows = (
        surface,
        wrapped(east_ref[pl.ds(first_row, rows), :]),
        wrapped(north_ref[pl.ds(first_row, rows), :]),
    )
    first, second = weights
    rates = (
        rates[0][:tile_rows, :tile_cols] + lift_ref[...],
        rates[1][:tile_rows, :tile_cols],
        rates[2][:tile_rows, :tile_cols],
    )
    for out, start, now, rate in zip(
        (next_surface, next_east, next_north),
        (start_surface, start_east, start_north),
        nows,
        rates,
    ):
        out[...] = first * start[...] + second * (now[:tile_rows, :tile_cols] + TIME_STEP * rate)
    east_out[...] = velocity_u[:tile_rows, :tile_cols]
    north_out[...] = velocity_v[:tile_rows, :tile_cols]


def ring_kernel(surface_ref, east_ref, north_ref, depth_ref, wet_ref, place_ref,
                lift_ref, next_surface, next_east, next_north, depth_out, wet_out, *,
                first_row, used_cols, tile_offset, layout):
    rows = layout[0]
    out_rows, out_cols = next_surface.shape
    rates, (surface, _, _), wrapped = tendency_body(
        surface_ref, east_ref, north_ref, depth_ref, wet_ref, place_ref, layout,
        first_row, used_cols, tile_offset,
    )
    lift = wrapped(lift_ref[pl.ds(first_row, rows), :])
    nows = (
        surface,
        wrapped(east_ref[pl.ds(first_row, rows), :]),
        wrapped(north_ref[pl.ds(first_row, rows), :]),
    )
    rates = (rates[0] + lift, rates[1], rates[2])
    for out, now, rate in zip((next_surface, next_east, next_north), nows, rates):
        out[...] = (0.0 * now + 1.0 * (now + TIME_STEP * rate))[:out_rows, :out_cols]
    depth_out[...] = wrapped(depth_ref[pl.ds(first_row, rows), :])[:out_rows, :out_cols]
    wet_out[...] = wrapped(wet_ref[pl.ds(first_row, rows), :])[:out_rows, :out_cols]


def ring_step(fields, place, layout, out_shape, first_row, used_cols, tile_offset):
    spec = pl.BlockSpec(memory_space=pltpu.VMEM)
    scalar = pl.BlockSpec(memory_space=pltpu.SMEM)
    shape = jax.ShapeDtypeStruct(out_shape, jnp.float32)
    return pl.pallas_call(
        lambda *refs: ring_kernel(
            *refs, first_row=first_row, used_cols=used_cols, tile_offset=tile_offset,
            layout=layout,
        ),
        out_shape=(shape,) * 5,
        in_specs=[spec] * 5 + [scalar, spec],
        out_specs=(spec,) * 5,
        name="ring_step",
    )(*fields[:5], place, fields[5])


def section_step(fields, place, layout, lift, initial, first_row, used_cols, tile_offset,
                 weights):
    spec = pl.BlockSpec(memory_space=pltpu.VMEM)
    scalar = pl.BlockSpec(memory_space=pltpu.SMEM)
    shape = jax.ShapeDtypeStruct(lift.shape, jnp.float32)
    return pl.pallas_call(
        lambda *refs: section_kernel(
            *refs, first_row=first_row, used_cols=used_cols, tile_offset=tile_offset,
            weights=weights, layout=layout,
        ),
        out_shape=(shape,) * 5,
        in_specs=[spec] * 5 + [scalar] + [spec] * 4,
        out_specs=(spec,) * 5,
        name="section_step",
    )(*fields, place, lift, *initial)


def halo_box(fields, wide_x, wide_y, place, count, padded_shape):
    lon_count = lax.axis_size("lon")
    west = lax.ppermute(
        fields[:, :, -wide_x:], "lon", [(i, (i + 1) % lon_count) for i in range(lon_count)]
    )
    east = lax.ppermute(
        fields[:, :, :wide_x], "lon", [((i + 1) % lon_count, i) for i in range(lon_count)]
    )
    wide = jnp.concatenate([west, fields, east], axis=2)
    above = passed_along(wide[:, -wide_y:], "lat", 1)
    below = passed_along(wide[:, :wide_y], "lat", -1)
    above = jnp.where(place == 0, wide[:, wide_y - 1 :: -1], above)
    below = jnp.where(place == count - 1, wide[:, : -wide_y - 1 : -1], below)
    box = jnp.concatenate([above, wide, below], axis=1)
    return pad_to(box, padded_shape)


def pad_to(values, shape):
    widths = [(0, 0)] * (values.ndim - 2) + [
        (0, want - have) for want, have in zip(shape, values.shape[-2:])
    ]
    return jnp.pad(values, widths)


def wall_mirrored(values, halo, place, count, rows):
    top = jnp.concatenate([values[..., 2 * halo - 1 : halo - 1 : -1, :], values[..., halo:, :]], axis=-2)
    values = jnp.where(place == 0, top, values)
    bottom = jnp.concatenate(
        [
            values[..., : rows - halo, :],
            values[..., rows - halo - 1 : rows - 2 * halo - 1 : -1, :],
            values[..., rows:, :],
        ],
        axis=-2,
    )
    return jnp.where(place == count - 1, bottom, values)


class Geometry:
    def __init__(self, out_rows, out_cols, halo_y, halo_x):
        self.box_rows = out_rows + 2 * halo_y
        self.box_cols = out_cols + 2 * halo_x
        self.first_row = (halo_y - 2) // 8 * 8
        self.rows = -(-(halo_y + out_rows + 2 - self.first_row) // 8) * 8
        self.padded = (
            max(-(-self.box_rows // 8) * 8, self.first_row + self.rows),
            -(-self.box_cols // 128) * 128,
        )
        self.offset = (halo_y, halo_x)

    def masks(self, region_above, place, count, tile_rows):
        box_row = lax.broadcasted_iota(jnp.int32, self.padded, 0)
        global_row = place * tile_rows - region_above - self.offset[0] + box_row
        inside = (global_row >= 0) & (global_row < count * tile_rows) & (box_row < self.box_rows)
        wrapped_row = lax.broadcasted_iota(jnp.int32, (self.rows, self.padded[1]), 0)
        tile_row = jnp.where(wrapped_row >= self.rows - 2, wrapped_row - self.rows, wrapped_row)
        tile_row = tile_row - region_above
        top = place == 0
        bottom = place == count - 1
        mirror = jnp.where(
            top & (tile_row == -1), 1,
            jnp.where(top & (tile_row == -2), 2,
            jnp.where(bottom & (tile_row == tile_rows), 3,
            jnp.where(bottom & (tile_row == tile_rows + 1), 4, 0))),
        ).astype(jnp.int32)
        return inside.astype(jnp.float32), mirror


def local(surface, momentum_x, momentum_y, water_depth, wet_mask, slide_cells, slide_rate):
    wet_float = wet_mask.astype(jnp.float32)
    place = lax.axis_index("lat")
    count = lax.axis_size("lat")
    tile_rows, tile_cols = surface.shape
    wide_x = WINDOW_LON + 2
    wide_y = WINDOW_LAT + 2
    lift = (
        jnp.zeros((tile_rows * tile_cols,), jnp.float32)
        .at[slide_cells.reshape(-1)]
        .add(slide_rate.reshape(-1))
        .reshape(tile_rows, tile_cols)
    )
    ring = Geometry(tile_rows + 2 * wide_y, tile_cols + 2 * wide_x, wide_y, wide_x)
    plain = Geometry(tile_rows, tile_cols, wide_y, wide_x)
    place_array = jnp.reshape(place, (1,)).astype(jnp.int32)
    ring_layout = (ring.rows, ring.padded[1], ring.box_rows, wide_y, tile_rows, count)
    plain_layout = (plain.rows, plain.padded[1], plain.box_rows, 0, tile_rows, count)
    initial = (surface, momentum_x, momentum_y)

    big = halo_box(
        jnp.stack([surface, momentum_x, momentum_y, water_depth, wet_float, lift]),
        2 * wide_x, 2 * wide_y, place, count, ring.padded,
    )
    ring_state = ring_step(
        tuple(big[k] for k in range(6)), place_array, ring_layout, plain.padded,
        ring.first_row, ring.box_cols, ring.offset,
    )
    box = wall_mirrored(jnp.stack(ring_state[:3]), wide_y, place, count, plain.box_rows)
    depth_box, wet_box = ring_state[3], ring_state[4]
    for first, second in ((0.75, 0.25), (1.0 / 3.0, 2.0 / 3.0)):
        if box is None:
            box = halo_box(jnp.stack(list(current)), wide_x, wide_y, place, count, plain.padded)
        next_surface, next_east, next_north, velocity_u, velocity_v = section_step(
            (box[0], box[1], box[2], depth_box, wet_box), place_array, plain_layout, lift, initial,
            plain.first_row, plain.box_cols, plain.offset, (first, second),
        )
        current = (next_surface, next_east, next_north)
        box = None
    return (current[0], current[1], current[2], velocity_u, velocity_v)


def solution(mesh):
    in_specs = (P("lat", "lon"),) * 7
    out_specs = (P("lat", "lon"),) * 5
    return jax.shard_map(local, mesh=mesh, in_specs=in_specs, out_specs=out_specs, check_vma=False)
```

```python
import jax
import jax.numpy as jnp
from jax import lax
from jax.sharding import PartitionSpec as P
from jax.experimental import pallas as pl
from jax.experimental.pallas import tpu as pltpu

GRAVITY = 1.0
LON_SPACING = 0.5
LAT_SPACING = 0.6
TIME_STEP = 0.1
WINDOW_LON = 40
WINDOW_LAT = 32
PCR_STEPS = (5, 6)


def shifted(block, axis, distance):
    devices = range(lax.axis_size(axis))
    route = [((i - distance) % len(devices), i) for i in devices]
    return lax.ppermute(block, axis, route)


def passed_along(x, axis, by):
    peers = lax.axis_size(axis)
    pairs = [(i, i + by) for i in range(peers) if 0 <= i + by < peers]
    return lax.ppermute(x, axis, pairs)


def extended(cells, sides, width, closed):
    for axis, dim in sides:
        count = lax.axis_size(axis)
        ends = count if closed else count - 1
        head = lax.slice_in_dim(cells, 0, width, axis=dim)
        tail = lax.slice_in_dim(cells, cells.shape[dim] - width, cells.shape[dim], axis=dim)
        cells = jnp.concatenate(
            [
                lax.ppermute(tail, axis, [(i, (i + 1) % count) for i in range(ends)]),
                cells,
                lax.ppermute(head, axis, [((i + 1) % count, i) for i in range(ends)]),
            ],
            axis=dim,
        )
    return cells


def slab_of(values, start, stop, along_axis):
    return lax.slice_in_dim(values, start, stop, axis=along_axis)


def limited(former, latter):
    return jnp.maximum(jnp.minimum(former, latter), 0.0) + jnp.minimum(
        jnp.maximum(former, latter), 0.0
    )


def face_states(values, along_axis):
    length = values.shape[along_axis]
    jumps = slab_of(values, 1, length, along_axis) - slab_of(values, 0, length - 1, along_axis)
    slopes = limited(
        slab_of(jumps, 0, length - 2, along_axis), slab_of(jumps, 1, length - 1, along_axis)
    )
    left_state = slab_of(values, 1, length - 2, along_axis) + 0.5 * slab_of(
        slopes, 0, length - 3, along_axis
    )
    right_state = slab_of(values, 2, length - 1, along_axis) - 0.5 * slab_of(
        slopes, 1, length - 2, along_axis
    )
    return (left_state, right_state)


def wave_flux(
    surface_left,
    surface_right,
    normal_left,
    normal_right,
    tangent_left,
    tangent_right,
    face_depth,
    opened,
):
    height_left = surface_left + face_depth
    height_right = surface_right + face_depth
    celerity_left = jnp.sqrt(GRAVITY * height_left)
    celerity_right = jnp.sqrt(GRAVITY * height_right)
    slowest = jnp.minimum(
        jnp.minimum(normal_left - celerity_left, normal_right - celerity_right), 0.0
    )
    fastest = jnp.maximum(
        jnp.maximum(normal_left + celerity_left, normal_right + celerity_right), 0.0
    )
    spread = fastest - slowest
    product = slowest * fastest
    mass_left = height_left * normal_left
    mass_right = height_right * normal_right
    push_left = mass_left * normal_left + GRAVITY * (
        0.5 * surface_left * surface_left + face_depth * surface_left
    )
    push_right = mass_right * normal_right + GRAVITY * (
        0.5 * surface_right * surface_right + face_depth * surface_right
    )
    carry_left = mass_left * tangent_left
    carry_right = mass_right * tangent_right
    mass_flux = (
        opened
        * (fastest * mass_left - slowest * mass_right + product * (surface_right - surface_left))
        / spread
    )
    push_flux = (
        opened
        * (fastest * push_left - slowest * push_right + product * (mass_right - mass_left))
        / spread
    )
    carry_flux = (
        opened
        * (
            fastest * carry_left
            - slowest * carry_right
            + product * (height_right * tangent_right - height_left * tangent_left)
        )
        / spread
    )
    return (mass_flux, push_flux, carry_flux)


def tendencies(across, along):
    width = across[0].shape[1] - 4
    row_count = along[0].shape[0] - 4
    surface_pair = face_states(across[0], 1)
    east_pair = face_states(across[1], 1)
    north_pair = face_states(across[2], 1)
    depth_lon = 0.5 * (across[3][:, 1 : width + 2] + across[3][:, 2 : width + 3])
    open_lon = across[4][:, 1 : width + 2] * across[4][:, 2 : width + 3]
    mass_lon, push_lon, carry_lon = wave_flux(
        surface_pair[0],
        surface_pair[1],
        east_pair[0],
        east_pair[1],
        north_pair[0],
        north_pair[1],
        depth_lon,
        open_lon,
    )
    surface_pair = face_states(along[0], 0)
    east_pair = face_states(along[1], 0)
    north_pair = face_states(along[2], 0)
    depth_lat = 0.5 * (along[3][1 : row_count + 2] + along[3][2 : row_count + 3])
    open_lat = along[4][1 : row_count + 2] * along[4][2 : row_count + 3]
    mass_lat, push_lat, carry_lat = wave_flux(
        surface_pair[0],
        surface_pair[1],
        north_pair[0],
        north_pair[1],
        east_pair[0],
        east_pair[1],
        depth_lat,
        open_lat,
    )
    surface_mid = across[0][:, 2 : width + 2]
    wet_mid = across[4][:, 2 : width + 2]
    rate_surface = (
        -(mass_lon[:, 1:] - mass_lon[:, :-1]) / LON_SPACING
        - (mass_lat[1:] - mass_lat[:-1]) / LAT_SPACING
    )
    source_east = GRAVITY * surface_mid * (depth_lon[:, 1:] - depth_lon[:, :-1]) / LON_SPACING
    source_north = GRAVITY * surface_mid * (depth_lat[1:] - depth_lat[:-1]) / LAT_SPACING
    rate_east = wet_mid * (
        source_east
        - (push_lon[:, 1:] - push_lon[:, :-1]) / LON_SPACING
        - (carry_lat[1:] - carry_lat[:-1]) / LAT_SPACING
    )
    rate_north = wet_mid * (
        source_north
        - (carry_lon[:, 1:] - carry_lon[:, :-1]) / LON_SPACING
        - (push_lat[1:] - push_lat[:-1]) / LAT_SPACING
    )
    return (rate_surface, rate_east, rate_north)


def from_below(values, stride, along_axis, filler):
    length = values.shape[along_axis]
    padding = jnp.full_like(slab_of(values, 0, stride, along_axis), filler)
    return jnp.concatenate([padding, slab_of(values, 0, length - stride, along_axis)], along_axis)


def from_above(values, stride, along_axis, filler):
    length = values.shape[along_axis]
    padding = jnp.full_like(slab_of(values, 0, stride, along_axis), filler)
    return jnp.concatenate([slab_of(values, stride, length, along_axis), padding], along_axis)


def reduce_lines(lower_band, main_band, upper_band, rights, along_axis):
    length = rights.shape[along_axis]
    position = lax.broadcasted_iota(jnp.int32, rights.shape, along_axis)
    stride = 1
    for _ in range(PCR_STEPS[along_axis]):
        def from_lower(values, fill):
            return jnp.where(position >= stride, pltpu.roll(values, stride, along_axis), fill)

        def from_upper(values, fill):
            return jnp.where(
                position < length - stride, pltpu.roll(values, length - stride, along_axis), fill
            )

        below = [from_lower(band, fill) for band, fill in
                 ((lower_band, 0.0), (main_band, 1.0), (upper_band, 0.0), (rights, 0.0))]
        above = [from_upper(band, fill) for band, fill in
                 ((lower_band, 0.0), (main_band, 1.0), (upper_band, 0.0), (rights, 0.0))]
        weight_below = lower_band / below[1]
        weight_above = upper_band / above[1]
        new_lower = -weight_below * below[0]
        new_main = main_band - weight_below * below[2] - weight_above * above[0]
        new_upper = -weight_above * above[2]
        rights = rights - weight_below * below[3] - weight_above * above[3]
        lower_band, main_band, upper_band = new_lower, new_main, new_upper
        stride = stride * 2
    return rights / main_band


def tendency_body(surface_ref, east_ref, north_ref, depth_ref, wet_ref, place_ref, layout,
                  first_row, used_cols, tile_offset):
    rows, cols, box_rows, region_above, tile_rows, count = layout
    place = place_ref[0]
    depth = depth_ref[pl.ds(first_row, rows), :]
    surface = surface_ref[pl.ds(first_row, rows), :]
    coef = depth * depth / (3.0 * LON_SPACING * LON_SPACING)
    keep = lax.broadcasted_iota(jnp.int32, depth.shape, 1) < used_cols
    rights = east_ref[pl.ds(first_row, rows), :] / (depth + surface)
    east_raw = reduce_lines(
        jnp.where(keep, -coef, 0.0),
        jnp.where(keep, 1.0 + 2.0 * coef, 1.0),
        jnp.where(keep, -coef, 0.0),
        jnp.where(keep, rights, 0.0),
        1,
    )
    full_depth = depth_ref[...]
    coef = full_depth * full_depth / (3.0 * LAT_SPACING * LAT_SPACING)
    box_row = lax.broadcasted_iota(jnp.int32, depth_ref.shape, 0)
    global_row = place * tile_rows - region_above - tile_offset[0] + box_row
    keep = (global_row >= 0) & (global_row < count * tile_rows) & (box_row < box_rows)
    rights = north_ref[...] / (full_depth + surface_ref[...])
    north_raw = reduce_lines(
        jnp.where(keep, -coef, 0.0),
        jnp.where(keep, 1.0 + 2.0 * coef, 1.0),
        jnp.where(keep, -coef, 0.0),
        jnp.where(keep, rights, 0.0),
        0,
    )[first_row : first_row + rows]

    def wrapped(values):
        values = pltpu.roll(values, rows - (tile_offset[0] - first_row), 0)
        return pltpu.roll(values, cols - tile_offset[1], 1)

    wet = wrapped(wet_ref[pl.ds(first_row, rows), :])
    surface = wrapped(surface)
    depth = wrapped(depth)
    velocity_u = wet * wrapped(east_raw)
    velocity_v = wet * wrapped(north_raw)
    wrapped_row = lax.broadcasted_iota(jnp.int32, (rows, cols), 0)
    tile_row = jnp.where(wrapped_row >= rows - 2, wrapped_row - rows, wrapped_row) - region_above
    top = place == 0
    bottom = place == count - 1
    for wall, row, shift in (
        (top, -1, rows - 1), (top, -2, rows - 3), (bottom, tile_rows, 1), (bottom, tile_rows + 1, 3)
    ):
        velocity_v = jnp.where(
            wall & (tile_row == row), -pltpu.roll(velocity_v, shift, 0), velocity_v
        )

    def east_of(values):
        return pltpu.roll(values, cols - 1, 1)

    def west_of(values):
        return pltpu.roll(values, 1, 1)

    def north_of(values):
        return pltpu.roll(values, rows - 1, 0)

    def south_of(values):
        return pltpu.roll(values, 1, 0)

    def face_pair(values, later, earlier):
        jump = later(values) - values
        slope = limited(earlier(jump), jump)
        return values + 0.5 * slope, later(values - 0.5 * slope)

    surface_pair = face_pair(surface, east_of, west_of)
    east_pair = face_pair(velocity_u, east_of, west_of)
    north_pair = face_pair(velocity_v, east_of, west_of)
    depth_lon = 0.5 * (depth + east_of(depth))
    open_lon = wet * east_of(wet)
    mass_lon, push_lon, carry_lon = wave_flux(
        surface_pair[0], surface_pair[1], east_pair[0], east_pair[1],
        north_pair[0], north_pair[1], depth_lon, open_lon,
    )
    surface_pair = face_pair(surface, north_of, south_of)
    east_pair = face_pair(velocity_u, north_of, south_of)
    north_pair = face_pair(velocity_v, north_of, south_of)
    depth_lat = 0.5 * (depth + north_of(depth))
    open_lat = wet * north_of(wet)
    mass_lat, push_lat, carry_lat = wave_flux(
        surface_pair[0], surface_pair[1], north_pair[0], north_pair[1],
        east_pair[0], east_pair[1], depth_lat, open_lat,
    )
    rate_surface = (
        -(mass_lon - west_of(mass_lon)) / LON_SPACING - (mass_lat - south_of(mass_lat)) / LAT_SPACING
    )
    source_east = GRAVITY * surface * (depth_lon - west_of(depth_lon)) / LON_SPACING
    source_north = GRAVITY * surface * (depth_lat - south_of(depth_lat)) / LAT_SPACING
    rate_east = wet * (
        source_east
        - (push_lon - west_of(push_lon)) / LON_SPACING
        - (carry_lat - south_of(carry_lat)) / LAT_SPACING
    )
    rate_north = wet * (
        source_north
        - (carry_lon - west_of(carry_lon)) / LON_SPACING
        - (push_lat - south_of(push_lat)) / LAT_SPACING
    )
    return (rate_surface, rate_east, rate_north), (surface, velocity_u, velocity_v), wrapped


def section_kernel(surface_ref, east_ref, north_ref, depth_ref, wet_ref, place_ref,
                   lift_ref, start_surface, start_east, start_north,
                   next_surface, next_east, next_north, east_out, north_out, *,
                   first_row, used_cols, tile_offset, weights, layout):
    tile_rows, tile_cols = lift_ref.shape
    rates, (surface, velocity_u, velocity_v), wrapped = tendency_body(
        surface_ref, east_ref, north_ref, depth_ref, wet_ref, place_ref, layout,
        first_row, used_cols, tile_offset,
    )
    rows = layout[0]
    nows = (
        surface,
        wrapped(east_ref[pl.ds(first_row, rows), :]),
        wrapped(north_ref[pl.ds(first_row, rows), :]),
    )
    first, second = weights
    rates = (
        rates[0][:tile_rows, :tile_cols] + lift_ref[...],
        rates[1][:tile_rows, :tile_cols],
        rates[2][:tile_rows, :tile_cols],
    )
    for out, start, now, rate in zip(
        (next_surface, next_east, next_north),
        (start_surface, start_east, start_north),
        nows,
        rates,
    ):
        out[...] = first * start[...] + second * (now[:tile_rows, :tile_cols] + TIME_STEP * rate)
    east_out[...] = velocity_u[:tile_rows, :tile_cols]
    north_out[...] = velocity_v[:tile_rows, :tile_cols]


def ring_kernel(surface_ref, east_ref, north_ref, depth_ref, wet_ref, place_ref,
                lift_ref, next_surface, next_east, next_north, depth_out, wet_out, *,
                first_row, used_cols, tile_offset, layout):
    rows = layout[0]
    out_rows, out_cols = next_surface.shape
    rates, (surface, _, _), wrapped = tendency_body(
        surface_ref, east_ref, north_ref, depth_ref, wet_ref, place_ref, layout,
        first_row, used_cols, tile_offset,
    )
    lift = wrapped(lift_ref[pl.ds(first_row, rows), :])
    nows = (
        surface,
        wrapped(east_ref[pl.ds(first_row, rows), :]),
        wrapped(north_ref[pl.ds(first_row, rows), :]),
    )
    rates = (rates[0] + lift, rates[1], rates[2])
    for out, now, rate in zip((next_surface, next_east, next_north), nows, rates):
        out[...] = (0.0 * now + 1.0 * (now + TIME_STEP * rate))[:out_rows, :out_cols]
    depth_out[...] = wrapped(depth_ref[pl.ds(first_row, rows), :])[:out_rows, :out_cols]
    wet_out[...] = wrapped(wet_ref[pl.ds(first_row, rows), :])[:out_rows, :out_cols]


def ring_step(fields, place, layout, out_shape, first_row, used_cols, tile_offset):
    spec = pl.BlockSpec(memory_space=pltpu.VMEM)
    scalar = pl.BlockSpec(memory_space=pltpu.SMEM)
    shape = jax.ShapeDtypeStruct(out_shape, jnp.float32)
    return pl.pallas_call(
        lambda *refs: ring_kernel(
            *refs, first_row=first_row, used_cols=used_cols, tile_offset=tile_offset,
            layout=layout,
        ),
        out_shape=(shape,) * 5,
        in_specs=[spec] * 5 + [scalar, spec],
        out_specs=(spec,) * 5,
        name="ring_step",
    )(*fields[:5], place, fields[5])


def section_step(fields, place, layout, lift, initial, first_row, used_cols, tile_offset,
                 weights):
    spec = pl.BlockSpec(memory_space=pltpu.VMEM)
    scalar = pl.BlockSpec(memory_space=pltpu.SMEM)
    shape = jax.ShapeDtypeStruct(lift.shape, jnp.float32)
    return pl.pallas_call(
        lambda *refs: section_kernel(
            *refs, first_row=first_row, used_cols=used_cols, tile_offset=tile_offset,
            weights=weights, layout=layout,
        ),
        out_shape=(shape,) * 5,
        in_specs=[spec] * 5 + [scalar] + [spec] * 4,
        out_specs=(spec,) * 5,
        name="section_step",
    )(*fields, place, lift, *initial)


def stack_kernel(*refs):
    for k, field in enumerate(refs[:-1]):
        refs[-1][k] = field[...]


def stacked(fields):
    spec = pl.BlockSpec(memory_space=pltpu.VMEM)
    return pl.pallas_call(
        stack_kernel,
        out_shape=jax.ShapeDtypeStruct((len(fields),) + fields[0].shape, jnp.float32),
        in_specs=[spec] * len(fields),
        out_specs=spec,
        name="stacked",
    )(*fields)


def halo_box(fields, wide_x, wide_y, place, count, padded_shape):
    lon_count = lax.axis_size("lon")
    west = lax.ppermute(
        fields[:, :, -wide_x:], "lon", [(i, (i + 1) % lon_count) for i in range(lon_count)]
    )
    east = lax.ppermute(
        fields[:, :, :wide_x], "lon", [((i + 1) % lon_count, i) for i in range(lon_count)]
    )
    wide = jnp.concatenate([west, fields, east], axis=2)
    above = passed_along(wide[:, -wide_y:], "lat", 1)
    below = passed_along(wide[:, :wide_y], "lat", -1)
    above = jnp.where(place == 0, wide[:, wide_y - 1 :: -1], above)
    below = jnp.where(place == count - 1, wide[:, : -wide_y - 1 : -1], below)
    box = jnp.concatenate([above, wide, below], axis=1)
    return pad_to(box, padded_shape)


def pad_to(values, shape):
    widths = [(0, 0)] * (values.ndim - 2) + [
        (0, want - have) for want, have in zip(shape, values.shape[-2:])
    ]
    return jnp.pad(values, widths)


def wall_mirrored(values, halo, place, count, rows):
    top = jnp.concatenate([values[..., 2 * halo - 1 : halo - 1 : -1, :], values[..., halo:, :]], axis=-2)
    values = jnp.where(place == 0, top, values)
    bottom = jnp.concatenate(
        [
            values[..., : rows - halo, :],
            values[..., rows - halo - 1 : rows - 2 * halo - 1 : -1, :],
            values[..., rows:, :],
        ],
        axis=-2,
    )
    return jnp.where(place == count - 1, bottom, values)


class Geometry:
    def __init__(self, out_rows, out_cols, halo_y, halo_x):
        self.box_rows = out_rows + 2 * halo_y
        self.box_cols = out_cols + 2 * halo_x
        self.first_row = (halo_y - 2) // 8 * 8
        self.rows = -(-(halo_y + out_rows + 2 - self.first_row) // 8) * 8
        self.padded = (
            max(-(-self.box_rows // 8) * 8, self.first_row + self.rows),
            -(-self.box_cols // 128) * 128,
        )
        self.offset = (halo_y, halo_x)

    def masks(self, region_above, place, count, tile_rows):
        box_row = lax.broadcasted_iota(jnp.int32, self.padded, 0)
        global_row = place * tile_rows - region_above - self.offset[0] + box_row
        inside = (global_row >= 0) & (global_row < count * tile_rows) & (box_row < self.box_rows)
        wrapped_row = lax.broadcasted_iota(jnp.int32, (self.rows, self.padded[1]), 0)
        tile_row = jnp.where(wrapped_row >= self.rows - 2, wrapped_row - self.rows, wrapped_row)
        tile_row = tile_row - region_above
        top = place == 0
        bottom = place == count - 1
        mirror = jnp.where(
            top & (tile_row == -1), 1,
            jnp.where(top & (tile_row == -2), 2,
            jnp.where(bottom & (tile_row == tile_rows), 3,
            jnp.where(bottom & (tile_row == tile_rows + 1), 4, 0))),
        ).astype(jnp.int32)
        return inside.astype(jnp.float32), mirror


def local(surface, momentum_x, momentum_y, water_depth, wet_mask, slide_cells, slide_rate):
    wet_float = wet_mask.astype(jnp.float32)
    place = lax.axis_index("lat")
    count = lax.axis_size("lat")
    tile_rows, tile_cols = surface.shape
    wide_x = WINDOW_LON + 2
    wide_y = WINDOW_LAT + 2
    lift = (
        jnp.zeros((tile_rows * tile_cols,), jnp.float32)
        .at[slide_cells.reshape(-1)]
        .add(slide_rate.reshape(-1))
        .reshape(tile_rows, tile_cols)
    )
    ring = Geometry(tile_rows + 2 * wide_y, tile_cols + 2 * wide_x, wide_y, wide_x)
    plain = Geometry(tile_rows, tile_cols, wide_y, wide_x)
    place_array = jnp.reshape(place, (1,)).astype(jnp.int32)
    ring_layout = (ring.rows, ring.padded[1], ring.box_rows, wide_y, tile_rows, count)
    plain_layout = (plain.rows, plain.padded[1], plain.box_rows, 0, tile_rows, count)
    initial = (surface, momentum_x, momentum_y)

    big = halo_box(
        stacked([surface, momentum_x, momentum_y, water_depth, wet_float, lift]),
        2 * wide_x, 2 * wide_y, place, count, ring.padded,
    )
    ring_state = ring_step(
        tuple(big[k] for k in range(6)), place_array, ring_layout, plain.padded,
        ring.first_row, ring.box_cols, ring.offset,
    )
    box = wall_mirrored(jnp.stack(ring_state[:3]), wide_y, place, count, plain.box_rows)
    depth_box, wet_box = ring_state[3], ring_state[4]
    for first, second in ((0.75, 0.25), (1.0 / 3.0, 2.0 / 3.0)):
        if box is None:
            box = halo_box(jnp.stack(list(current)), wide_x, wide_y, place, count, plain.padded)
        next_surface, next_east, next_north, velocity_u, velocity_v = section_step(
            (box[0], box[1], box[2], depth_box, wet_box), place_array, plain_layout, lift, initial,
            plain.first_row, plain.box_cols, plain.offset, (first, second),
        )
        current = (next_surface, next_east, next_north)
        box = None
    return (current[0], current[1], current[2], velocity_u, velocity_v)


def solution(mesh):
    in_specs = (P("lat", "lon"),) * 7
    out_specs = (P("lat", "lon"),) * 5
    return jax.shard_map(local, mesh=mesh, in_specs=in_specs, out_specs=out_specs, check_vma=False)
```
